32 devices in a mesh: groups: 2 (over y), ctx: 4 (over z), eg: 4 (over x, core), rep: 1.
Axes of the slice: x: 2, y: 2, z: 4, core: 2. Of those that a mesh axis runs over, the one named last changes fastest.
Arguments:
- queries: bfloat16 [4096, 2048], P(('groups', 'ctx', 'eg'), 'rep'), parts along dimension 0, may hold values from -12 to 12
- keys: bfloat16 [8, 512, 256], P(('groups', 'ctx'), 'eg', 'rep'), parts along dimension 0, may hold values from -4 to 4
- values: bfloat16 [8, 512, 256], P(('groups', 'ctx'), 'eg', 'rep'), parts along dimension 0, may hold values from -12 to 12
- selected: int32 [8, 2], P('groups'), parts along dimension 0, may hold values from 0 to 3, as said below
- out_weight: bfloat16 [2048, 2048], P('rep', 'eg'), may hold values from -0.125 to 0.125
- residual: bfloat16 [4096, 2048], P(('groups', 'ctx', 'eg', 'rep')), parts along dimension 0, may hold values from -27 to 27
- norm_gain: float32 [2048], replicated, may hold values from 0.5 to 1.5
- expert_ids: int32 [4096, 8], P(('groups', 'ctx', 'eg', 'rep')), parts along dimension 0, may hold values from 0 to 15, all different within a row; in each aligned block of 128 rows (0 to 127, 128 to 255, ...) at most 64 rows name the same one
- gate_weights: float32 [4096, 8], P(('groups', 'ctx', 'eg', 'rep')), parts along dimension 0, may hold values from 0.05 to 0.5
- expert_home: int32 [16], replicated, may hold values from 0 to 15, each once
- w_gate: bfloat16 [16, 2048, 384], P(('ctx', 'eg'), None, 'rep'), may hold values from -0.125 to 0.125
- w_up: bfloat16 [16, 2048, 384], P(('ctx', 'eg'), None, 'rep'), may hold values from -0.125 to 0.125
- w_down: bfloat16 [16, 384, 2048], P(('ctx', 'eg'), 'rep'), may hold values from -0.3125 to 0.3125
Outputs:
- attn_out: bfloat16 [4096, 2048], P(('groups', 'ctx', 'eg', 'rep')), parts along dimension 0
- moe_out: bfloat16 [4096, 2048], P(('groups', 'ctx', 'eg', 'rep')), parts along dimension 0
The draws below stay inside these ranges and needn't reach their ends.
There are 2 independent parts, one for each index of `groups`. The reference program is written for one: setup_inputs(seed, part) draws one part's arguments, and reference() takes and returns one part's arrays. A program takes and returns all parts, laid end to end along the dimension named above; an argument that names none is the same for every part. Nothing has to cross between parts.
Inputs may be any that keep to these rules, and one draw needn't show every extreme that they name: `selected`: block c lies in context shard c; query block b lies in shard b. The 2 blocks listed by the query blocks of one shard lie in distinct shards, and no query block lists itself. `expert_ids`: each aligned block of 128 rows (the rows of one device) names every expert exactly 64 times. Expert e's weights are entry expert_home[e] of w_gate, w_up and w_down.
All inputs are finite; a program needn't handle non-finite values.
Results may differ from the reference program's by a relative error of at most 0.0085.
Values may be sent and summed in bfloat16 or wider, within the bound.
No kernel may reach another device: no remote copies, remote signals or barrier semaphores. Data moves between devices by JAX's collectives and lax.ppermute only.
A program may use at most 64 MiB of HBM per device.

```python
import math
import jax
import jax.numpy as jnp
import numpy as np
from jax import lax

D = 2048
HQ = 16
KVH = 2
HD = 128
H = 384
TOPK = 8
BLK = 512
SEL = 2
TOK_DEV = 128
TOKENS = 2048
BPS = 1
NB = 4
EXPERTS = 16
CAP = 64
N_REP = 1


def draw_keys(key, part):
    return jnp.clip(jax.random.normal(jax.random.fold_in(key, 12), (NB, BLK, KVH * HD), jnp.float32), -4.0, 4.0).astype(jnp.bfloat16)


def draw_queries(key, part):
    return jnp.clip(2.0 * jax.random.normal(jax.random.fold_in(key, 22), (TOKENS, HQ * HD), jnp.float32), -6.0, 6.0).astype(jnp.bfloat16)


def draw_residual(key, part):
    row_scale = jnp.exp(jax.random.uniform(jax.random.fold_in(key, 31), (TOKENS, 1), jnp.float32, math.log(0.3), math.log(3.0)))
    column_scale = jnp.exp(jax.random.uniform(jax.random.fold_in(key, 32), (1, D), jnp.float32, math.log(0.3), math.log(3.0)))
    rough = jnp.clip(jax.random.normal(jax.random.fold_in(key, 35), (TOKENS, D), jnp.float32), -3.0, 3.0)
    return (row_scale * column_scale * rough).astype(jnp.bfloat16)


def draw_selected(key, part):
    shard_count = NB // BPS
    listed_count = BPS * SEL
    shard_ids = jnp.arange(shard_count, dtype=jnp.int32)
    scores = jax.random.randint(jax.random.fold_in(key, 41), (shard_count, shard_count), 0, 1 << 20, dtype=jnp.int32) * shard_count + shard_ids[None, :]
    scores = jnp.where(shard_ids[None, :] == shard_ids[:, None], jnp.int32(1 << 30), scores)
    ranking = jnp.argsort(scores, axis=1, stable=True).astype(jnp.int32)
    picked = ranking[:, :listed_count]
    random_bits = jax.random.randint(jax.random.fold_in(key, 42), (shard_count, listed_count), 0, 1 << 20, dtype=jnp.int32)
    query_local = (jnp.arange(listed_count, dtype=jnp.int32) // SEL)[None, :]
    generic = random_bits % BPS
    avoiding = (query_local + 1 + random_bits % max(BPS - 1, 1)) % BPS
    local_block = jnp.where(picked == shard_ids[:, None], avoiding, generic)
    blocks = picked * BPS + local_block
    return blocks.reshape(NB, SEL).astype(jnp.int32)


def level_of(key, shape, pieces, low, top_value):
    def one(dim, parts):
        draws = jax.random.uniform(jax.random.fold_in(jax.random.fold_in(key, 6), dim), (parts,), jnp.float32, low / len(pieces), top_value / len(pieces))
        return jnp.repeat(jnp.exp(draws), shape[dim] // parts).reshape((-1,) + (1,) * (len(shape) - dim - 1))

    gain = one(*pieces[0])
    for cut in pieces[1:]:
        gain = gain * one(*cut)
    return gain


def assign_block(own_key, own, number, rows, number_of, top, most, lean):
    order = jax.random.permutation(own_key, number_of)
    crowded, usual = load_shares(number_of, rows * top, most, lean, True), load_shares(number_of, rows * top, most, lean, False)
    places = jnp.arange(number_of)

    def named(sizes, offset_by):
        used = int((sizes > 0).sum())
        fixed = max(1, used // 4)
        moved = fixed + (places - fixed + offset_by * (used - fixed)) % max(1, number_of - fixed)
        return jnp.zeros((number_of,), jnp.int32).at[order[jnp.where(places < fixed, places, moved)]].set(jnp.asarray(sizes, jnp.int32))

    sizes = jnp.where(number % 4 == 0, named(crowded, number // 4), named(usual, number - number // 4 - 1))
    mixed = jax.random.permutation(jax.random.fold_in(own, 3), number_of)
    giver, receiver = mixed[0:number_of // 2 * 2:2], mixed[1:number_of // 2 * 2:2]
    slack = jnp.minimum(sizes[giver] - 1, most - sizes[receiver]) // 2
    slack = jnp.where((giver == order[0]) | (receiver == order[0]) | (sizes[receiver] == 0), 0, jnp.maximum(slack, 0))
    moved = jax.random.randint(jax.random.fold_in(own, 4), (number_of // 2,), 0, 1 << 20) % (slack + 1)
    sizes = sizes.at[giver].add(-moved).at[receiver].add(moved)
    labels = jnp.searchsorted(jnp.cumsum(sizes), jnp.arange(rows * top), side="right").astype(jnp.int32)
    listing = labels.reshape(top, rows).T
    listing = listing[jax.random.permutation(jax.random.fold_in(own, 1), rows)]
    offset_by = jax.random.randint(jax.random.fold_in(own, 2), (rows, 1), 0, top)
    return jnp.take_along_axis(listing, (jnp.arange(top)[None, :] + offset_by) % top, axis=1)


def load_shares(amount, total, reach, skew, full):
    weights = [(1 << 20) // math.isqrt(rank ** skew) + 1 for rank in range(1, amount + 1)]
    largest = reach if full else min(reach, max(-(-total // amount), total * weights[0] // sum(weights)))
    least = 1 if total - largest >= amount - 1 else 0
    given, surplus = [largest] + [least] * (amount - 1), total - largest - least * (amount - 1)
    while surplus > 0:
        movable = [i for i in range(1, amount) if given[i] < largest] or [i for i in range(1, amount) if given[i] < reach]
        whole, left = sum([weights[i] for i in movable]), surplus
        for i in movable:
            more = min(reach - given[i], max(1, left * weights[i] // whole), surplus)
            given[i] = given[i] + more
            surplus = surplus - more
    return np.array(given)


def normal_values(key, shape, scale, most, pieces=(), held_as=jnp.bfloat16):
    values = scale * jax.random.normal(key, shape, jnp.float32)
    if pieces:
        values = values * level_of(key, shape, pieces, -0.22, 0.18)
    return jnp.clip(values, -most, most).astype(held_as)


def setup_inputs(seed: int = 0, part: int = 0) -> dict:
    streams_of = jax.random.split(jax.random.key(seed), 14)
    part_splits = jax.random.split(jax.random.fold_in(streams_of[13], part), 14)
    queries = draw_queries(jax.random.fold_in(jax.random.fold_in(streams_of[13], part), 71), part)
    keys = draw_keys(jax.random.fold_in(jax.random.fold_in(streams_of[13], part), 71), part)
    values = normal_values(part_splits[2], (NB, BLK, KVH * HD), 3.0, 12.0, ((0, 4), (1, 4)))
    selected = draw_selected(jax.random.fold_in(jax.random.fold_in(streams_of[13], part), 71), part)
    out_weight = normal_values(streams_of[4], (HQ * HD, D), (HQ * HD) ** -0.5, 0.125, ((1, 4),))
    residual = draw_residual(jax.random.fold_in(jax.random.fold_in(streams_of[13], part), 71), part)
    norm_gain = jnp.clip(1.0 + 0.1 * jax.random.normal(streams_of[6], (D,), jnp.float32), 0.5, 1.5)
    expert_ids_keys = jax.random.split(jax.random.fold_in(part_splits[7], 1), TOKENS // TOK_DEV)
    expert_ids_turns = jax.random.permutation(jax.random.fold_in(part_splits[7], 3), TOKENS // TOK_DEV)
    expert_ids = jax.vmap(lambda own, number: assign_block(jax.random.fold_in(part_splits[7], 2), own, number, TOK_DEV, EXPERTS, TOPK, CAP, 0))(expert_ids_keys, expert_ids_turns).reshape((TOKENS, TOPK))
    gate_weights = jnp.clip(jnp.exp(math.log(0.5) - 2.3025851 * jax.random.uniform(part_splits[8], (TOKENS, TOPK), jnp.float32) ** level_of(part_splits[8], (TOKENS, TOPK), ((0, 16),), -0.2, 0.2)), 0.05, 0.5)
    expert_home = jax.random.permutation(streams_of[9], EXPERTS).astype(jnp.int32)
    w_gate = normal_values(streams_of[10], (EXPERTS, D, H), D ** -0.5, 0.125, ((0, 16),))
    w_up = normal_values(streams_of[11], (EXPERTS, D, H), D ** -0.5, 0.125, ((0, 16),))
    w_down = normal_values(streams_of[12], (EXPERTS, H, D), H ** -0.5, 0.3125, ((0, 16),))
    return dict(queries=queries, keys=keys, values=values, selected=selected, out_weight=out_weight, residual=residual, norm_gain=norm_gain, expert_ids=expert_ids, gate_weights=gate_weights, expert_home=expert_home, w_gate=w_gate, w_up=w_up, w_down=w_down)


def attend_pair(query_pair, key_rows, value_rows, inverse_root):
    logits = jnp.einsum('rkgd,nkd->krgn', query_pair.astype(jnp.float32), key_rows.astype(jnp.float32)) * inverse_root
    largest = lax.optimization_barrier(jnp.max(logits, axis=-1, keepdims=True))
    raised = jnp.exp(logits - largest)
    denominator = lax.optimization_barrier(jnp.sum(raised, axis=-1, keepdims=True))
    weights_low = (raised / denominator).astype(jnp.bfloat16)
    blended = jnp.einsum('krgn,nkd->rkgd', weights_low.astype(jnp.float32), value_rows.astype(jnp.float32))
    return blended.astype(jnp.bfloat16)

def attend_rows(queries_flat, key_rows, value_rows):
    row_count = queries_flat.shape[0]
    kv_heads = key_rows.shape[1]
    per_group = queries_flat.shape[1] // (kv_heads * HD)
    arranged = queries_flat.reshape(row_count, kv_heads, per_group // 2, 2, HD)
    inverse_root = 1.0 / math.sqrt(HD)

    def one_pair(pair_index):
        query_pair = lax.dynamic_index_in_dim(arranged, pair_index, 2, keepdims=False)
        return attend_pair(query_pair, key_rows, value_rows, inverse_root)
    stacked = lax.map(one_pair, jnp.arange(per_group // 2, dtype=jnp.int32))
    return jnp.moveaxis(stacked, 0, 2).reshape(row_count, kv_heads * per_group * HD)

def reference(queries, keys, values, selected, out_weight, residual, norm_gain, expert_ids, gate_weights, expert_home, w_gate, w_up, w_down):
    span = (1 + SEL) * BLK

    def one_block(block_id):
        query_block = lax.dynamic_slice_in_dim(queries, block_id * BLK, BLK, 0)
        chosen = jnp.concatenate([block_id[None].astype(jnp.int32), selected[block_id].astype(jnp.int32)])
        key_rows = jnp.take(keys, chosen, axis=0).reshape(span, KVH, HD)
        value_rows = jnp.take(values, chosen, axis=0).reshape(span, KVH, HD)
        return attend_rows(query_block, key_rows, value_rows)
    attended = lax.map(one_block, jnp.arange(NB, dtype=jnp.int32)).reshape(TOKENS, HQ * HD)
    half_width = HQ * HD // N_REP
    summed = jnp.zeros((TOKENS, D), jnp.float32)
    for half_index in range(N_REP):
        lower = half_index * half_width
        partial_out = jnp.dot(attended[:, lower:lower + half_width], out_weight[lower:lower + half_width], preferred_element_type=jnp.float32)
        rounded = lax.optimization_barrier(partial_out.astype(jnp.bfloat16))
        summed = summed + rounded.astype(jnp.float32)
    attn_out = summed.astype(jnp.bfloat16)
    stream = residual.astype(jnp.float32) + attn_out.astype(jnp.float32)
    meansq = lax.optimization_barrier(jnp.mean(stream * stream, axis=1, keepdims=True))
    normed = (stream * lax.rsqrt(meansq + 1e-06) * norm_gain).astype(jnp.bfloat16)
    flat_ids = expert_ids.reshape(-1).astype(jnp.int32)
    sorting = jnp.argsort(flat_ids, stable=True).astype(jnp.int32)
    per_expert = TOKENS * TOPK // EXPERTS
    token_rows = (sorting // TOPK).reshape(EXPERTS, per_expert)
    gate_sorted = jnp.take(gate_weights.reshape(-1), sorting).reshape(EXPERTS, per_expert)

    def expert_step(accumulated, expert_index):
        slot_index = expert_home[expert_index]
        rows_in = jnp.take(normed, token_rows[expert_index], axis=0)
        gate_act = jnp.dot(rows_in, w_gate[slot_index], preferred_element_type=jnp.float32)
        up_act = jnp.dot(rows_in, w_up[slot_index], preferred_element_type=jnp.float32)
        activation = (jax.nn.silu(gate_act) * up_act).astype(jnp.bfloat16)
        expert_rows = jnp.dot(activation, w_down[slot_index], preferred_element_type=jnp.float32).astype(jnp.bfloat16)
        weighted = gate_sorted[expert_index][:, None] * expert_rows.astype(jnp.float32)
        return (accumulated.at[token_rows[expert_index]].add(weighted), None)
    accumulated, _ = lax.scan(expert_step, jnp.zeros((TOKENS, D), jnp.float32), jnp.arange(EXPERTS, dtype=jnp.int32))
    moe_out = accumulated.astype(jnp.bfloat16)
    return (attn_out, moe_out)
```

```python
import math

import jax
import jax.numpy as jnp
from jax import lax
from jax.sharding import PartitionSpec as P

HD = 128


def swapped(value, axis, bit):
    mask = 2**bit
    pairs = [(source, source ^ mask) for source in range(lax.axis_size(axis))]
    return lax.ppermute(value, axis, pairs)


def attend_pair(query_pair, key_rows, value_rows, inverse_root):
    logits = (
        jnp.einsum("rkgd,nkd->krgn", query_pair, key_rows, preferred_element_type=jnp.float32)
        * inverse_root
    )
    largest = jnp.max(logits, axis=-1, keepdims=True)
    raised = jnp.exp(logits - largest)
    denominator = jnp.sum(raised, axis=-1, keepdims=True)
    weights_low = (raised / denominator).astype(jnp.bfloat16)
    blended = jnp.einsum(
        "krgn,nkd->rkgd", weights_low, value_rows, preferred_element_type=jnp.float32
    )
    return blended.astype(jnp.bfloat16)


def attend_rows(queries_flat, key_rows, value_rows):
    row_count = queries_flat.shape[0]
    kv_heads = key_rows.shape[1]
    per_group = queries_flat.shape[1] // (kv_heads * HD)
    arranged = queries_flat.reshape(row_count, kv_heads, per_group // 2, 2, HD)
    inverse_root = 1.0 / math.sqrt(HD)

    def one_pair(pair_index):
        query_pair = lax.dynamic_index_in_dim(arranged, pair_index, 2, keepdims=False)
        return attend_pair(query_pair, key_rows, value_rows, inverse_root)

    stacked = lax.map(one_pair, jnp.arange(per_group // 2, dtype=jnp.int32))
    return jnp.moveaxis(stacked, 0, 2).reshape(row_count, kv_heads * per_group * HD)


def expert_apply(rows_in, gate_full, up_full, down_full):
    gate_act = jnp.dot(rows_in, gate_full, preferred_element_type=jnp.float32)
    up_act = jnp.dot(rows_in, up_full, preferred_element_type=jnp.float32)
    activation = (jax.nn.silu(gate_act) * up_act).astype(jnp.bfloat16)
    return jnp.dot(activation, down_full, preferred_element_type=jnp.float32).astype(jnp.bfloat16)


def local(
    queries,
    keys,
    values,
    selected,
    out_weight,
    residual,
    norm_gain,
    expert_ids,
    gate_weights,
    expert_home,
    w_gate,
    w_up,
    w_down,
):
    n_ctx = lax.axis_size("ctx")
    n_eg = lax.axis_size("eg")
    n_rep = lax.axis_size("rep")
    my_ctx = lax.axis_index("ctx")

    def fetch_panels():
        if n_rep == 1:
            return (w_gate[0], w_up[0], w_down[0])
        other_gate, other_up, other_down = swapped((w_gate, w_up, w_down), "rep", 0)
        first = lax.axis_index("rep") == 0
        gate_full = jnp.where(
            first,
            jnp.concatenate([w_gate[0], other_gate[0]], axis=1),
            jnp.concatenate([other_gate[0], w_gate[0]], axis=1),
        )
        up_full = jnp.where(
            first,
            jnp.concatenate([w_up[0], other_up[0]], axis=1),
            jnp.concatenate([other_up[0], w_up[0]], axis=1),
        )
        down_full = jnp.where(
            first,
            jnp.concatenate([w_down[0], other_down[0]], axis=0),
            jnp.concatenate([other_down[0], w_down[0]], axis=0),
        )
        return (gate_full, up_full, down_full)

    shard_blocks, slice_rows, kv_width = keys.shape
    pick_count = selected.shape[1]
    block_rows = slice_rows * n_eg
    listed = selected.reshape(n_ctx, shard_blocks * pick_count)
    owned_here = listed // shard_blocks == my_ctx
    block_match = (listed % shard_blocks)[:, :, None] == jnp.arange(shard_blocks, dtype=jnp.int32)[
        None, None, :
    ]
    request = jnp.max(
        jnp.logical_and(owned_here[:, :, None], block_match).astype(jnp.int32), axis=1
    ).astype(jnp.bfloat16)
    outgoing_keys = jnp.einsum(
        "cb,btw->ctw", request, keys, preferred_element_type=jnp.float32
    ).astype(jnp.bfloat16)
    outgoing_values = jnp.einsum(
        "cb,btw->ctw", request, values, preferred_element_type=jnp.float32
    ).astype(jnp.bfloat16)
    far_keys, far_values = (
        lax.all_to_all(outgoing_keys, "ctx", split_axis=0, concat_axis=0, tiled=True),
        lax.all_to_all(outgoing_values, "ctx", split_axis=0, concat_axis=0, tiled=True),
    )
    query_rows = queries.shape[0]
    peer_ids = jnp.arange(n_eg, dtype=jnp.int32)
    own_block = peer_ids * query_rows // block_rows
    peer_lists = jnp.take(selected, my_ctx * shard_blocks + own_block, axis=0) // shard_blocks

    def assemble(local_part, fetched):
        own_rows = jnp.take(local_part, own_block, axis=0)[:, None]
        far_rows = jnp.take(fetched, peer_lists.reshape(-1), axis=0).reshape(
            n_eg, pick_count, slice_rows, kv_width
        )
        return jnp.concatenate([own_rows, far_rows], axis=1)

    context_keys, context_values = (
        lax.all_to_all(assemble(keys, far_keys), "eg", split_axis=0, concat_axis=2, tiled=True),
        lax.all_to_all(assemble(values, far_values), "eg", split_axis=0, concat_axis=2, tiled=True),
    )
    span = (1 + pick_count) * block_rows
    kv_heads = kv_width // HD
    attended = attend_rows(
        queries,
        context_keys.reshape(span, kv_heads, HD),
        context_values.reshape(span, kv_heads, HD),
    )
    tok_dev = residual.shape[0]
    partial_out = jnp.dot(
        attended,
        lax.all_gather(out_weight, "eg", axis=1, tiled=True),
        preferred_element_type=jnp.float32,
    )
    attn_out = lax.psum_scatter(
        partial_out.astype(jnp.bfloat16), "rep", scatter_dimension=0, tiled=True
    )
    stream = residual.astype(jnp.float32) + attn_out.astype(jnp.float32)
    meansq = jnp.mean(stream * stream, axis=1, keepdims=True)
    normed = (stream * lax.rsqrt(meansq + 1e-06) * norm_gain).astype(jnp.bfloat16)
    top_count = expert_ids.shape[1]
    slot_count = n_ctx * n_eg
    pair_count = tok_dev * top_count
    per_slot = pair_count // slot_count
    home_slot = jnp.take(expert_home, expert_ids.reshape(-1), axis=0)
    indicator = (home_slot[:, None] == jnp.arange(slot_count, dtype=jnp.int32)[None, :]).astype(
        jnp.int32
    )
    rank_in_slot = jnp.sum((jnp.cumsum(indicator, axis=0) - 1) * indicator, axis=1)
    position = home_slot * per_slot + rank_in_slot
    source_pair = (
        jnp.zeros((pair_count,), jnp.int32)
        .at[position]
        .set(jnp.arange(pair_count, dtype=jnp.int32))
    )
    partner = fetch_panels()
    if slot_count <= 4 * top_count:
        my_slot = my_ctx * n_eg + lax.axis_index("eg")
        all_normed = lax.all_gather(normed, ("ctx", "eg"), axis=0, tiled=True)
        all_ids = lax.all_gather(expert_ids, ("ctx", "eg"), axis=0, tiled=True)
        hits = jnp.any(jnp.take(expert_home, all_ids, axis=0) == my_slot, axis=1)
        hits = hits.reshape(slot_count, tok_dev).astype(jnp.int32)
        rank = jnp.cumsum(hits, axis=1) - 1
        chosen = jnp.logical_and(
            hits[:, None, :] == 1,
            rank[:, None, :] == jnp.arange(per_slot, dtype=jnp.int32)[None, :, None],
        )
        local_row = jnp.sum(
            chosen.astype(jnp.int32) * jnp.arange(tok_dev, dtype=jnp.int32)[None, None, :], axis=2
        )
        src_rows = local_row + jnp.arange(slot_count, dtype=jnp.int32)[:, None] * tok_dev
        flat_rows = jnp.take(all_normed, src_rows.reshape(-1), axis=0)
    else:
        outbound = jnp.take(normed, source_pair // top_count, axis=0).reshape(
            slot_count, per_slot, -1
        )
        arrived = lax.all_to_all(outbound, ("ctx", "eg"), split_axis=0, concat_axis=0, tiled=True)
        flat_rows = arrived.reshape(-1, arrived.shape[2])
    produced = expert_apply(flat_rows, partner[0], partner[1], partner[2])
    returned = lax.all_to_all(
        produced.reshape(slot_count, per_slot, -1),
        ("ctx", "eg"),
        split_axis=0,
        concat_axis=0,
        tiled=True,
    )
    answers = jnp.take(returned.reshape(pair_count, -1), position, axis=0).reshape(
        tok_dev, top_count, -1
    )
    combined = gate_weights[:, 0:1] * answers[:, 0].astype(jnp.float32)
    for choice_slot in range(1, top_count):
        combined = combined + gate_weights[:, choice_slot : choice_slot + 1] * answers[
            :, choice_slot
        ].astype(jnp.float32)
    moe_out = combined.astype(jnp.bfloat16)
    return (attn_out, moe_out)


def solution(mesh):
    return jax.shard_map(
        local,
        mesh=mesh,
        in_specs=(
            P(("groups", "ctx", "eg"), "rep"),
            P(("groups", "ctx"), "eg", "rep"),
            P(("groups", "ctx"), "eg", "rep"),
            P("groups", None),
            P("rep", "eg"),
            P(("groups", "ctx", "eg", "rep"), None),
            P(),
            P(("groups", "ctx", "eg", "rep"), None),
            P(("groups", "ctx", "eg", "rep"), None),
            P(),
            P(("ctx", "eg"), None, "rep"),
            P(("ctx", "eg"), None, "rep"),
            P(("ctx", "eg"), "rep", None),
        ),
        out_specs=(
            P(("groups", "ctx", "eg", "rep"), None),
            P(("groups", "ctx", "eg", "rep"), None),
        ),
        check_vma=False,
    )
```

```python
import math

import jax
import jax.numpy as jnp
from jax import lax
from jax.sharding import PartitionSpec as P

HD = 128


def swapped(value, axis, bit):
    mask = 2**bit
    pairs = [(source, source ^ mask) for source in range(lax.axis_size(axis))]
    return lax.ppermute(value, axis, pairs)


def attend_pair(query_pair, key_rows, value_rows, inverse_root):
    logits = (
        jnp.einsum("rkgd,nkd->krgn", query_pair, key_rows, preferred_element_type=jnp.float32)
        * inverse_root
    )
    largest = jnp.max(logits, axis=-1, keepdims=True)
    raised = jnp.exp(logits - largest)
    denominator = jnp.sum(raised, axis=-1, keepdims=True)
    weights_low = (raised / denominator).astype(jnp.bfloat16)
    blended = jnp.einsum(
        "krgn,nkd->rkgd", weights_low, value_rows, preferred_element_type=jnp.float32
    )
    return blended.astype(jnp.bfloat16)


def attend_rows(queries_flat, key_rows, value_rows):
    row_count = queries_flat.shape[0]
    kv_heads = key_rows.shape[1]
    per_group = queries_flat.shape[1] // (kv_heads * HD)
    arranged = queries_flat.reshape(row_count, kv_heads, per_group // 2, 2, HD)
    inverse_root = 1.0 / math.sqrt(HD)

    def one_pair(pair_index):
        query_pair = lax.dynamic_index_in_dim(arranged, pair_index, 2, keepdims=False)
        return attend_pair(query_pair, key_rows, value_rows, inverse_root)

    stacked = lax.map(one_pair, jnp.arange(per_group // 2, dtype=jnp.int32))
    return jnp.moveaxis(stacked, 0, 2).reshape(row_count, kv_heads * per_group * HD)


def expert_apply(rows_in, gate_full, up_full, down_full):
    gate_act = jnp.dot(rows_in, gate_full, preferred_element_type=jnp.float32)
    up_act = jnp.dot(rows_in, up_full, preferred_element_type=jnp.float32)
    activation = (jax.nn.silu(gate_act) * up_act).astype(jnp.bfloat16)
    return jnp.dot(activation, down_full, preferred_element_type=jnp.float32).astype(jnp.bfloat16)


def local(
    queries,
    keys,
    values,
    selected,
    out_weight,
    residual,
    norm_gain,
    expert_ids,
    gate_weights,
    expert_home,
    w_gate,
    w_up,
    w_down,
):
    n_ctx = lax.axis_size("ctx")
    n_eg = lax.axis_size("eg")
    n_rep = lax.axis_size("rep")
    my_ctx = lax.axis_index("ctx")

    def fetch_panels():
        if n_rep == 1:
            return (w_gate[0], w_up[0], w_down[0])
        other_gate, other_up, other_down = swapped((w_gate, w_up, w_down), "rep", 0)
        first = lax.axis_index("rep") == 0
        gate_full = jnp.where(
            first,
            jnp.concatenate([w_gate[0], other_gate[0]], axis=1),
            jnp.concatenate([other_gate[0], w_gate[0]], axis=1),
        )
        up_full = jnp.where(
            first,
            jnp.concatenate([w_up[0], other_up[0]], axis=1),
            jnp.concatenate([other_up[0], w_up[0]], axis=1),
        )
        down_full = jnp.where(
            first,
            jnp.concatenate([w_down[0], other_down[0]], axis=0),
            jnp.concatenate([other_down[0], w_down[0]], axis=0),
        )
        return (gate_full, up_full, down_full)

    shard_blocks, slice_rows, kv_width = keys.shape
    pick_count = selected.shape[1]
    block_rows = slice_rows * n_eg
    my_eg = lax.axis_index("eg")
    both = jnp.concatenate([keys, values], axis=2)
    gathered = lax.all_gather(both[None], ("ctx", "eg"), axis=0, tiled=True)
    every_block = (
        gathered.reshape(n_ctx, n_eg, shard_blocks, slice_rows, 2 * kv_width)
        .transpose(0, 2, 1, 3, 4)
        .reshape(n_ctx * shard_blocks, block_rows, 2 * kv_width)
    )
    query_rows = queries.shape[0]
    my_block = (my_ctx * n_eg + my_eg) * query_rows // block_rows
    chosen_blocks = jnp.concatenate(
        [my_block[None].astype(jnp.int32), jnp.take(selected, my_block, axis=0)]
    )
    context = jnp.take(every_block, chosen_blocks, axis=0)
    context_keys = context[:, :, :kv_width]
    context_values = context[:, :, kv_width:]
    span = (1 + pick_count) * block_rows
    kv_heads = kv_width // HD
    attended = attend_rows(
        queries,
        context_keys.reshape(span, kv_heads, HD),
        context_values.reshape(span, kv_heads, HD),
    )
    tok_dev = residual.shape[0]
    pieces = {0: out_weight}
    for bit in reversed(range(n_eg.bit_length() - 1)):
        stride = 2**bit
        held = sorted(pieces)
        fetched = swapped(tuple(pieces[m] for m in held), "eg", bit)
        for m, piece in zip(held, fetched):
            pieces[m + stride] = piece
    weight_cols = jnp.concatenate([pieces[m] for m in range(n_eg)], axis=1)
    out_by_piece = jnp.dot(attended, weight_cols, preferred_element_type=jnp.float32).reshape(
        query_rows, n_eg, -1
    )
    piece_of_col = jnp.arange(n_eg, dtype=jnp.int32) ^ my_eg
    partial_out = jnp.take(out_by_piece, piece_of_col, axis=1).reshape(query_rows, -1)
    attn_out = lax.psum_scatter(
        partial_out.astype(jnp.bfloat16), "rep", scatter_dimension=0, tiled=True
    )
    stream = residual.astype(jnp.float32) + attn_out.astype(jnp.float32)
    meansq = jnp.mean(stream * stream, axis=1, keepdims=True)
    normed = (stream * lax.rsqrt(meansq + 1e-06) * norm_gain).astype(jnp.bfloat16)
    top_count = expert_ids.shape[1]
    slot_count = n_ctx * n_eg
    pair_count = tok_dev * top_count
    per_slot = pair_count // slot_count
    home_slot = jnp.take(expert_home, expert_ids.reshape(-1), axis=0)
    indicator = (home_slot[:, None] == jnp.arange(slot_count, dtype=jnp.int32)[None, :]).astype(
        jnp.int32
    )
    rank_in_slot = jnp.sum((jnp.cumsum(indicator, axis=0) - 1) * indicator, axis=1)
    position = home_slot * per_slot + rank_in_slot
    source_pair = (
        jnp.zeros((pair_count,), jnp.int32)
        .at[position]
        .set(jnp.arange(pair_count, dtype=jnp.int32))
    )
    partner = fetch_panels()
    if slot_count <= 4 * top_count:
        my_slot = my_ctx * n_eg + my_eg
        width = normed.shape[1]
        id_cols = jnp.full((tok_dev, 128), -1.0, jnp.bfloat16)
        id_cols = id_cols.at[:, :top_count].set(expert_ids.astype(jnp.bfloat16))
        packed = jnp.concatenate([normed, id_cols], axis=1)
        all_packed = lax.all_gather(packed, ("ctx", "eg"), axis=0, tiled=True)
        all_normed = all_packed[:, :width]
        all_ids = all_packed[:, width : width + top_count].astype(jnp.int32)
        expert_count = expert_home.shape[0]
        my_expert = jnp.sum(
            jnp.where(expert_home == my_slot, jnp.arange(expert_count, dtype=jnp.int32), 0)
        )
        hits = jnp.any(all_ids == my_expert, axis=1)
        hits = hits.reshape(slot_count, tok_dev).astype(jnp.int32)
        rank = jnp.cumsum(hits, axis=1) - 1
        chosen = jnp.logical_and(
            hits[:, None, :] == 1,
            rank[:, None, :] == jnp.arange(per_slot, dtype=jnp.int32)[None, :, None],
        )
        local_row = jnp.sum(
            chosen.astype(jnp.int32) * jnp.arange(tok_dev, dtype=jnp.int32)[None, None, :], axis=2
        )
        src_rows = local_row + jnp.arange(slot_count, dtype=jnp.int32)[:, None] * tok_dev
        flat_rows = jnp.take(all_normed, src_rows.reshape(-1), axis=0)
    else:
        outbound = jnp.take(normed, source_pair // top_count, axis=0).reshape(
            slot_count, per_slot, -1
        )
        arrived = lax.all_to_all(outbound, ("ctx", "eg"), split_axis=0, concat_axis=0, tiled=True)
        flat_rows = arrived.reshape(-1, arrived.shape[2])
    produced = expert_apply(flat_rows, partner[0], partner[1], partner[2])
    returned = lax.all_to_all(
        produced.reshape(slot_count, per_slot, -1),
        ("ctx", "eg"),
        split_axis=0,
        concat_axis=0,
        tiled=True,
    )
    answers = jnp.take(returned.reshape(pair_count, -1), position, axis=0).reshape(
        tok_dev, top_count, -1
    )
    combined = gate_weights[:, 0:1] * answers[:, 0].astype(jnp.float32)
    for choice_slot in range(1, top_count):
        combined = combined + gate_weights[:, choice_slot : choice_slot + 1] * answers[
            :, choice_slot
        ].astype(jnp.float32)
    moe_out = combined.astype(jnp.bfloat16)
    return (attn_out, moe_out)


def solution(mesh):
    return jax.shard_map(
        local,
        mesh=mesh,
        in_specs=(
            P(("groups", "ctx", "eg"), "rep"),
            P(("groups", "ctx"), "eg", "rep"),
            P(("groups", "ctx"), "eg", "rep"),
            P("groups", None),
            P("rep", "eg"),
            P(("groups", "ctx", "eg", "rep"), None),
            P(),
            P(("groups", "ctx", "eg", "rep"), None),
            P(("groups", "ctx", "eg", "rep"), None),
            P(),
            P(("ctx", "eg"), None, "rep"),
            P(("ctx", "eg"), None, "rep"),
            P(("ctx", "eg"), "rep", None),
        ),
        out_specs=(
            P(("groups", "ctx", "eg", "rep"), None),
            P(("groups", "ctx", "eg", "rep"), None),
        ),
        check_vma=False,
    )
```

```python
import math

import jax
import jax.numpy as jnp
from jax import lax
from jax.sharding import PartitionSpec as P

HD = 128


def swapped(value, axis, bit):
    mask = 2**bit
    pairs = [(source, source ^ mask) for source in range(lax.axis_size(axis))]
    return lax.ppermute(value, axis, pairs)


def attend_pair(query_pair, key_rows, value_rows, inverse_root):
    logits = (
        jnp.einsum("rkgd,nkd->krgn", query_pair, key_rows, preferred_element_type=jnp.float32)
        * inverse_root
    )
    largest = jnp.max(logits, axis=-1, keepdims=True)
    raised = jnp.exp(logits - largest)
    denominator = jnp.sum(raised, axis=-1, keepdims=True)
    weights_low = (raised / denominator).astype(jnp.bfloat16)
    blended = jnp.einsum(
        "krgn,nkd->rkgd", weights_low, value_rows, preferred_element_type=jnp.float32
    )
    return blended.astype(jnp.bfloat16)


def attend_rows(queries_flat, key_rows, value_rows):
    row_count = queries_flat.shape[0]
    kv_heads = key_rows.shape[1]
    per_group = queries_flat.shape[1] // (kv_heads * HD)
    arranged = queries_flat.reshape(row_count, kv_heads, per_group // 2, 2, HD)
    inverse_root = 1.0 / math.sqrt(HD)

    def one_pair(pair_index):
        query_pair = lax.dynamic_index_in_dim(arranged, pair_index, 2, keepdims=False)
        return attend_pair(query_pair, key_rows, value_rows, inverse_root)

    stacked = lax.map(one_pair, jnp.arange(per_group // 2, dtype=jnp.int32))
    return jnp.moveaxis(stacked, 0, 2).reshape(row_count, kv_heads * per_group * HD)


def expert_apply(rows_in, gate_full, up_full, down_full):
    gate_act = jnp.dot(rows_in, gate_full, preferred_element_type=jnp.float32)
    up_act = jnp.dot(rows_in, up_full, preferred_element_type=jnp.float32)
    activation = (jax.nn.silu(gate_act) * up_act).astype(jnp.bfloat16)
    return jnp.dot(activation, down_full, preferred_element_type=jnp.float32).astype(jnp.bfloat16)


def local(
    queries,
    keys,
    values,
    selected,
    out_weight,
    residual,
    norm_gain,
    expert_ids,
    gate_weights,
    expert_home,
    w_gate,
    w_up,
    w_down,
):
    n_ctx = lax.axis_size("ctx")
    n_eg = lax.axis_size("eg")
    n_rep = lax.axis_size("rep")
    my_ctx = lax.axis_index("ctx")

    def fetch_panels():
        if n_rep == 1:
            return (w_gate[0], w_up[0], w_down[0])
        other_gate, other_up, other_down = swapped((w_gate, w_up, w_down), "rep", 0)
        first = lax.axis_index("rep") == 0
        gate_full = jnp.where(
            first,
            jnp.concatenate([w_gate[0], other_gate[0]], axis=1),
            jnp.concatenate([other_gate[0], w_gate[0]], axis=1),
        )
        up_full = jnp.where(
            first,
            jnp.concatenate([w_up[0], other_up[0]], axis=1),
            jnp.concatenate([other_up[0], w_up[0]], axis=1),
        )
        down_full = jnp.where(
            first,
            jnp.concatenate([w_down[0], other_down[0]], axis=0),
            jnp.concatenate([other_down[0], w_down[0]], axis=0),
        )
        return (gate_full, up_full, down_full)

    shard_blocks, slice_rows, kv_width = keys.shape
    pick_count = selected.shape[1]
    block_rows = slice_rows * n_eg
    my_eg = lax.axis_index("eg")
    both = jnp.concatenate([keys, values], axis=2)
    gathered = lax.all_gather(both[None], ("ctx", "eg"), axis=0, tiled=True)
    every_block = (
        gathered.reshape(n_ctx, n_eg, shard_blocks, slice_rows, 2 * kv_width)
        .transpose(0, 2, 1, 3, 4)
        .reshape(n_ctx * shard_blocks, block_rows, 2 * kv_width)
    )
    query_rows = queries.shape[0]
    my_block = (my_ctx * n_eg + my_eg) * query_rows // block_rows
    chosen_blocks = jnp.concatenate(
        [my_block[None].astype(jnp.int32), jnp.take(selected, my_block, axis=0)]
    )
    context = jnp.take(every_block, chosen_blocks, axis=0)
    context_keys = context[:, :, :kv_width]
    context_values = context[:, :, kv_width:]
    span = (1 + pick_count) * block_rows
    kv_heads = kv_width // HD
    attended = attend_rows(
        queries,
        context_keys.reshape(span, kv_heads, HD),
        context_values.reshape(span, kv_heads, HD),
    )
    tok_dev = residual.shape[0]
    pieces = {0: out_weight}
    for bit in reversed(range(n_eg.bit_length() - 1)):
        stride = 2**bit
        held = sorted(pieces)
        if len(held) > 1:
            barrier_out = lax.optimization_barrier((tuple(pieces[m] for m in held), attended))
            pieces = dict(zip(held, barrier_out[0]))
            attended = barrier_out[1]
        fetched = swapped(tuple(pieces[m] for m in held), "eg", bit)
        for m, piece in zip(held, fetched):
            pieces[m + stride] = piece
    weight_cols = jnp.concatenate([pieces[m] for m in range(n_eg)], axis=1)
    out_by_piece = jnp.dot(attended, weight_cols, preferred_element_type=jnp.float32).reshape(
        query_rows, n_eg, -1
    )
    piece_of_col = jnp.arange(n_eg, dtype=jnp.int32) ^ my_eg
    partial_out = jnp.take(out_by_piece, piece_of_col, axis=1).reshape(query_rows, -1)
    attn_out = lax.psum_scatter(
        partial_out.astype(jnp.bfloat16), "rep", scatter_dimension=0, tiled=True
    )
    stream = residual.astype(jnp.float32) + attn_out.astype(jnp.float32)
    meansq = jnp.mean(stream * stream, axis=1, keepdims=True)
    normed = (stream * lax.rsqrt(meansq + 1e-06) * norm_gain).astype(jnp.bfloat16)
    top_count = expert_ids.shape[1]
    slot_count = n_ctx * n_eg
    pair_count = tok_dev * top_count
    per_slot = pair_count // slot_count
    home_slot = jnp.take(expert_home, expert_ids.reshape(-1), axis=0)
    indicator = (home_slot[:, None] == jnp.arange(slot_count, dtype=jnp.int32)[None, :]).astype(
        jnp.int32
    )
    rank_in_slot = jnp.sum((jnp.cumsum(indicator, axis=0) - 1) * indicator, axis=1)
    position = home_slot * per_slot + rank_in_slot
    source_pair = (
        jnp.zeros((pair_count,), jnp.int32)
        .at[position]
        .set(jnp.arange(pair_count, dtype=jnp.int32))
    )
    partner = fetch_panels()
    if slot_count <= 4 * top_count:
        my_slot = my_ctx * n_eg + my_eg
        width = normed.shape[1]
        id_cols = jnp.full((tok_dev, 128), -1.0, jnp.bfloat16)
        id_cols = id_cols.at[:, :top_count].set(expert_ids.astype(jnp.bfloat16))
        packed = jnp.concatenate([normed, id_cols], axis=1)
        all_packed = lax.all_gather(packed, ("ctx", "eg"), axis=0, tiled=True)
        all_normed = all_packed[:, :width]
        all_ids = all_packed[:, width : width + top_count].astype(jnp.int32)
        expert_count = expert_home.shape[0]
        my_expert = jnp.sum(
            jnp.where(expert_home == my_slot, jnp.arange(expert_count, dtype=jnp.int32), 0)
        )
        hits = jnp.any(all_ids == my_expert, axis=1)
        hits = hits.reshape(slot_count, tok_dev).astype(jnp.int32)
        rank = jnp.cumsum(hits, axis=1) - 1
        chosen = jnp.logical_and(
            hits[:, None, :] == 1,
            rank[:, None, :] == jnp.arange(per_slot, dtype=jnp.int32)[None, :, None],
        )
        local_row = jnp.sum(
            chosen.astype(jnp.int32) * jnp.arange(tok_dev, dtype=jnp.int32)[None, None, :], axis=2
        )
        src_rows = local_row + jnp.arange(slot_count, dtype=jnp.int32)[:, None] * tok_dev
        pad_rows = ((0, all_packed.shape[1] - width), (0, 0))
        gate_act = jnp.dot(
            all_packed, jnp.pad(partner[0], pad_rows), preferred_element_type=jnp.float32
        )
        up_act = jnp.dot(
            all_packed, jnp.pad(partner[1], pad_rows), preferred_element_type=jnp.float32
        )
        activation = (jax.nn.silu(gate_act) * up_act).astype(jnp.bfloat16)
        picked = jnp.take(activation, src_rows.reshape(-1), axis=0)
        produced = jnp.dot(picked, partner[2], preferred_element_type=jnp.float32).astype(
            jnp.bfloat16
        )
    else:
        outbound = jnp.take(normed, source_pair // top_count, axis=0).reshape(
            slot_count, per_slot, -1
        )
        arrived = lax.all_to_all(outbound, ("ctx", "eg"), split_axis=0, concat_axis=0, tiled=True)
        flat_rows = arrived.reshape(-1, arrived.shape[2])
        produced = expert_apply(flat_rows, partner[0], partner[1], partner[2])
    returned = lax.all_to_all(
        produced.reshape(slot_count, per_slot, -1),
        ("ctx", "eg"),
        split_axis=0,
        concat_axis=0,
        tiled=True,
    )
    returned_rows = returned.reshape(pair_count, -1)
    placed = position.reshape(tok_dev, top_count)[:, :, None] == jnp.arange(
        pair_count, dtype=jnp.int32
    )[None, None, :]
    mixing = jnp.sum(jnp.where(placed, gate_weights[:, :, None], 0.0), axis=1)
    combined = jnp.zeros((tok_dev, returned_rows.shape[1]), jnp.float32)
    remainder = mixing
    for _ in range(3):
        part = remainder.astype(jnp.bfloat16)
        remainder = remainder - part.astype(jnp.float32)
        combined = combined + jnp.dot(part, returned_rows, preferred_element_type=jnp.float32)
    moe_out = combined.astype(jnp.bfloat16)
    return (attn_out, moe_out)


def solution(mesh):
    return jax.shard_map(
        local,
        mesh=mesh,
        in_specs=(
            P(("groups", "ctx", "eg"), "rep"),
            P(("groups", "ctx"), "eg", "rep"),
            P(("groups", "ctx"), "eg", "rep"),
            P("groups", None),
            P("rep", "eg"),
            P(("groups", "ctx", "eg", "rep"), None),
            P(),
            P(("groups", "ctx", "eg", "rep"), None),
            P(("groups", "ctx", "eg", "rep"), None),
            P(),
            P(("ctx", "eg"), None, "rep"),
            P(("ctx", "eg"), None, "rep"),
            P(("ctx", "eg"), "rep", None),
        ),
        out_specs=(
            P(("groups", "ctx", "eg", "rep"), None),
            P(("groups", "ctx", "eg", "rep"), None),
        ),
        check_vma=False,
    )
```

```python
import math

import jax
import jax.numpy as jnp
from jax import lax
from jax.sharding import PartitionSpec as P

HD = 128


EG = ("ex", "ec")


def size_of(axes):
    return math.prod(lax.axis_size(axis) for axis in axes)


def index_of(axes):
    index = 0
    for axis in axes:
        index = index * lax.axis_size(axis) + lax.axis_index(axis)
    return index


def swapped(value, axis, bit):
    mask = 2**bit
    axes = axis if isinstance(axis, tuple) else (axis,)
    pairs = [(source, source ^ mask) for source in range(size_of(axes))]
    return lax.ppermute(value, axis, pairs)


def attend_pair(query_pair, key_rows, value_rows, inverse_root):
    logits = (
        jnp.einsum("rkgd,nkd->krgn", query_pair, key_rows, preferred_element_type=jnp.float32)
        * inverse_root
    )
    largest = jnp.max(logits, axis=-1, keepdims=True)
    raised = jnp.exp(logits - largest)
    denominator = jnp.sum(raised, axis=-1, keepdims=True)
    weights_low = (raised / denominator).astype(jnp.bfloat16)
    blended = jnp.einsum(
        "krgn,nkd->rkgd", weights_low, value_rows, preferred_element_type=jnp.float32
    )
    return blended.astype(jnp.bfloat16)


def attend_rows(queries_flat, key_rows, value_rows):
    row_count = queries_flat.shape[0]
    kv_heads = key_rows.shape[1]
    per_group = queries_flat.shape[1] // (kv_heads * HD)
    arranged = queries_flat.reshape(row_count, kv_heads, per_group // 2, 2, HD)
    inverse_root = 1.0 / math.sqrt(HD)

    def one_pair(pair_index):
        query_pair = lax.dynamic_index_in_dim(arranged, pair_index, 2, keepdims=False)
        return attend_pair(query_pair, key_rows, value_rows, inverse_root)

    stacked = lax.map(one_pair, jnp.arange(per_group // 2, dtype=jnp.int32))
    return jnp.moveaxis(stacked, 0, 2).reshape(row_count, kv_heads * per_group * HD)


def expert_apply(rows_in, gate_full, up_full, down_full):
    gate_act = jnp.dot(rows_in, gate_full, preferred_element_type=jnp.float32)
    up_act = jnp.dot(rows_in, up_full, preferred_element_type=jnp.float32)
    activation = (jax.nn.silu(gate_act) * up_act).astype(jnp.bfloat16)
    return jnp.dot(activation, down_full, preferred_element_type=jnp.float32).astype(jnp.bfloat16)


def local(
    queries,
    keys,
    values,
    selected,
    out_weight,
    residual,
    norm_gain,
    expert_ids,
    gate_weights,
    expert_home,
    w_gate,
    w_up,
    w_down,
):
    n_ctx = lax.axis_size("ctx")
    n_eg = size_of(EG)
    n_ec = lax.axis_size("ec")
    n_ex = lax.axis_size("ex")
    n_rep = lax.axis_size("rep")
    my_ctx = lax.axis_index("ctx")

    def fetch_panels():
        if n_rep == 1:
            return (w_gate[0], w_up[0], w_down[0])
        other_gate, other_up, other_down = swapped((w_gate, w_up, w_down), "rep", 0)
        first = lax.axis_index("rep") == 0
        gate_full = jnp.where(
            first,
            jnp.concatenate([w_gate[0], other_gate[0]], axis=1),
            jnp.concatenate([other_gate[0], w_gate[0]], axis=1),
        )
        up_full = jnp.where(
            first,
            jnp.concatenate([w_up[0], other_up[0]], axis=1),
            jnp.concatenate([other_up[0], w_up[0]], axis=1),
        )
        down_full = jnp.where(
            first,
            jnp.concatenate([w_down[0], other_down[0]], axis=0),
            jnp.concatenate([other_down[0], w_down[0]], axis=0),
        )
        return (gate_full, up_full, down_full)

    shard_blocks, slice_rows, kv_width = keys.shape
    pick_count = selected.shape[1]
    block_rows = slice_rows * n_eg
    my_eg = index_of(EG)
    both = jnp.concatenate([keys, values], axis=2)
    gathered = lax.all_gather(both[None], ("ctx", "ex"), axis=0, tiled=True)
    gathered = lax.all_gather(gathered[None], "ec", axis=0, tiled=True)
    out_weight, gathered = lax.optimization_barrier((out_weight, gathered))
    every_block = (
        gathered.reshape(n_ec, n_ctx, n_ex, shard_blocks, slice_rows, 2 * kv_width)
        .transpose(1, 3, 2, 0, 4, 5)
        .reshape(n_ctx * shard_blocks, block_rows, 2 * kv_width)
    )
    query_rows = queries.shape[0]
    my_block = (my_ctx * n_eg + my_eg) * query_rows // block_rows
    chosen_blocks = jnp.concatenate(
        [my_block[None].astype(jnp.int32), jnp.take(selected, my_block, axis=0)]
    )
    context = jnp.take(every_block, chosen_blocks, axis=0)
    context_keys = context[:, :, :kv_width]
    context_values = context[:, :, kv_width:]
    span = (1 + pick_count) * block_rows
    kv_heads = kv_width // HD
    attended = attend_rows(
        queries,
        context_keys.reshape(span, kv_heads, HD),
        context_values.reshape(span, kv_heads, HD),
    )
    tok_dev = residual.shape[0]
    pieces = {0: out_weight}
    for bit in reversed(range(n_eg.bit_length() - 1)):
        stride = 2**bit
        held = sorted(pieces)
        if len(held) > 1:
            barrier_out = lax.optimization_barrier((tuple(pieces[m] for m in held), attended))
            pieces = dict(zip(held, barrier_out[0]))
            attended = barrier_out[1]
        fetched = swapped(tuple(pieces[m] for m in held), EG, bit)
        for m, piece in zip(held, fetched):
            pieces[m + stride] = piece
    weight_cols = jnp.concatenate([pieces[m] for m in range(n_eg)], axis=1)
    out_by_piece = jnp.dot(attended, weight_cols, preferred_element_type=jnp.float32).reshape(
        query_rows, n_eg, -1
    )
    piece_of_col = jnp.arange(n_eg, dtype=jnp.int32) ^ my_eg
    partial_out = jnp.take(out_by_piece, piece_of_col, axis=1).reshape(query_rows, -1)
    attn_out = lax.psum_scatter(
        partial_out.astype(jnp.bfloat16), "rep", scatter_dimension=0, tiled=True
    )
    stream = residual.astype(jnp.float32) + attn_out.astype(jnp.float32)
    meansq = jnp.mean(stream * stream, axis=1, keepdims=True)
    normed = (stream * lax.rsqrt(meansq + 1e-06) * norm_gain).astype(jnp.bfloat16)
    top_count = expert_ids.shape[1]
    slot_count = n_ctx * n_eg
    pair_count = tok_dev * top_count
    per_slot = pair_count // slot_count
    home_slot = jnp.take(expert_home, expert_ids.reshape(-1), axis=0)
    indicator = (home_slot[:, None] == jnp.arange(slot_count, dtype=jnp.int32)[None, :]).astype(
        jnp.int32
    )
    rank_in_slot = jnp.sum((jnp.cumsum(indicator, axis=0) - 1) * indicator, axis=1)
    position = home_slot * per_slot + rank_in_slot
    source_pair = (
        jnp.zeros((pair_count,), jnp.int32)
        .at[position]
        .set(jnp.arange(pair_count, dtype=jnp.int32))
    )
    partner = fetch_panels()
    if slot_count <= 4 * top_count:
        my_slot = my_ctx * n_eg + my_eg
        width = normed.shape[1]
        id_cols = jnp.full((tok_dev, 128), -1.0, jnp.bfloat16)
        id_cols = id_cols.at[:, :top_count].set(expert_ids.astype(jnp.bfloat16))
        packed = jnp.concatenate([normed, id_cols], axis=1)
        all_packed = lax.all_gather(packed, ("ctx", "ex"), axis=0, tiled=True)
        all_packed = lax.all_gather(all_packed, "ec", axis=0, tiled=True)
        all_normed = all_packed[:, :width]
        all_ids = all_packed[:, width : width + top_count].astype(jnp.int32)
        expert_count = expert_home.shape[0]
        my_expert = jnp.sum(
            jnp.where(expert_home == my_slot, jnp.arange(expert_count, dtype=jnp.int32), 0)
        )
        hits = jnp.any(all_ids == my_expert, axis=1)
        hits = (
            hits.reshape(n_ec, n_ctx * n_ex, tok_dev)
            .transpose(1, 0, 2)
            .reshape(slot_count, tok_dev)
            .astype(jnp.int32)
        )
        rank = jnp.cumsum(hits, axis=1) - 1
        chosen = jnp.logical_and(
            hits[:, None, :] == 1,
            rank[:, None, :] == jnp.arange(per_slot, dtype=jnp.int32)[None, :, None],
        )
        local_row = jnp.sum(
            chosen.astype(jnp.int32) * jnp.arange(tok_dev, dtype=jnp.int32)[None, None, :], axis=2
        )
        slot_ids = jnp.arange(slot_count, dtype=jnp.int32)
        row_base = (slot_ids % n_ec) * (n_ctx * n_ex * tok_dev) + (slot_ids // n_ec) * tok_dev
        src_rows = local_row + row_base[:, None]
        pad_rows = ((0, all_packed.shape[1] - width), (0, 0))
        gate_act = jnp.dot(
            all_packed, jnp.pad(partner[0], pad_rows), preferred_element_type=jnp.float32
        )
        up_act = jnp.dot(
            all_packed, jnp.pad(partner[1], pad_rows), preferred_element_type=jnp.float32
        )
        activation = (jax.nn.silu(gate_act) * up_act).astype(jnp.bfloat16)
        picked = jnp.take(activation, src_rows.reshape(-1), axis=0)
        produced = jnp.dot(picked, partner[2], preferred_element_type=jnp.float32).astype(
            jnp.bfloat16
        )
    else:
        outbound = jnp.take(normed, source_pair // top_count, axis=0).reshape(
            slot_count, per_slot, -1
        )
        arrived = lax.all_to_all(outbound, ("ctx",) + EG, split_axis=0, concat_axis=0, tiled=True)
        flat_rows = arrived.reshape(-1, arrived.shape[2])
        produced = expert_apply(flat_rows, partner[0], partner[1], partner[2])
    returned = lax.all_to_all(
        produced.reshape(slot_count, per_slot, -1),
        ("ctx",) + EG,
        split_axis=0,
        concat_axis=0,
        tiled=True,
    )
    returned_rows = returned.reshape(pair_count, -1)
    placed = position.reshape(tok_dev, top_count)[:, :, None] == jnp.arange(
        pair_count, dtype=jnp.int32
    )[None, None, :]
    mixing = jnp.sum(jnp.where(placed, gate_weights[:, :, None], 0.0), axis=1)
    combined = jnp.zeros((tok_dev, returned_rows.shape[1]), jnp.float32)
    remainder = mixing
    for _ in range(3):
        part = remainder.astype(jnp.bfloat16)
        remainder = remainder - part.astype(jnp.float32)
        combined = combined + jnp.dot(part, returned_rows, preferred_element_type=jnp.float32)
    moe_out = combined.astype(jnp.bfloat16)
    return (attn_out, moe_out)


def solution(mesh):
    devices = mesh.devices
    groups, ctx, eg, rep = devices.shape
    low = 2 if eg % 2 == 0 else 1
    split_mesh = jax.sharding.Mesh(
        devices.reshape(groups, ctx, eg // low, low, rep), ("groups", "ctx") + EG + ("rep",)
    )
    rows = ("groups", "ctx") + EG + ("rep",)
    return jax.shard_map(
        local,
        mesh=split_mesh,
        in_specs=(
            P(("groups", "ctx") + EG, "rep"),
            P(("groups", "ctx"), EG, "rep"),
            P(("groups", "ctx"), EG, "rep"),
            P("groups", None),
            P("rep", EG),
            P(rows, None),
            P(),
            P(rows, None),
            P(rows, None),
            P(),
            P(("ctx",) + EG, None, "rep"),
            P(("ctx",) + EG, None, "rep"),
            P(("ctx",) + EG, "rep", None),
        ),
        out_specs=(P(rows, None), P(rows, None)),
        check_vma=False,
    )
```

```python
import math

import jax
import jax.numpy as jnp
from jax import lax
from jax.sharding import PartitionSpec as P

HD = 128


def swapped(value, axis, bit):
    mask = 2**bit
    pairs = [(source, source ^ mask) for source in range(lax.axis_size(axis))]
    return lax.ppermute(value, axis, pairs)


def attend_rows(queries_flat, key_rows, value_rows):
    row_count = queries_flat.shape[0]
    kv_heads = key_rows.shape[1]
    per_group = queries_flat.shape[1] // (kv_heads * HD)
    inverse_root = 1.0 / math.sqrt(HD)
    arranged = queries_flat.reshape(row_count, kv_heads, per_group, HD).transpose(1, 2, 0, 3)
    logits = (
        jnp.einsum("kgrd,nkd->kgrn", arranged, key_rows, preferred_element_type=jnp.float32)
        * inverse_root
    )
    largest = jnp.max(logits, axis=-1, keepdims=True)
    raised = jnp.exp(logits - largest)
    denominator = jnp.sum(raised, axis=-1, keepdims=True)
    weights_low = (raised / denominator).astype(jnp.bfloat16)
    blended = jnp.einsum(
        "kgrn,nkd->rkgd", weights_low, value_rows, preferred_element_type=jnp.float32
    )
    return blended.astype(jnp.bfloat16).reshape(row_count, kv_heads * per_group * HD)


def expert_apply(rows_in, gate_full, up_full, down_full):
    gate_act = jnp.dot(rows_in, gate_full, preferred_element_type=jnp.float32)
    up_act = jnp.dot(rows_in, up_full, preferred_element_type=jnp.float32)
    activation = (jax.nn.silu(gate_act) * up_act).astype(jnp.bfloat16)
    return jnp.dot(activation, down_full, preferred_element_type=jnp.float32).astype(jnp.bfloat16)


def local(
    queries,
    keys,
    values,
    selected,
    out_weight,
    residual,
    norm_gain,
    expert_ids,
    gate_weights,
    expert_home,
    w_gate,
    w_up,
    w_down,
):
    n_ctx = lax.axis_size("ctx")
    n_eg = lax.axis_size("eg")
    n_rep = lax.axis_size("rep")
    my_ctx = lax.axis_index("ctx")

    def fetch_panels():
        if n_rep == 1:
            return (w_gate[0], w_up[0], w_down[0])
        other_gate, other_up, other_down = swapped((w_gate, w_up, w_down), "rep", 0)
        first = lax.axis_index("rep") == 0
        gate_full = jnp.where(
            first,
            jnp.concatenate([w_gate[0], other_gate[0]], axis=1),
            jnp.concatenate([other_gate[0], w_gate[0]], axis=1),
        )
        up_full = jnp.where(
            first,
            jnp.concatenate([w_up[0], other_up[0]], axis=1),
            jnp.concatenate([other_up[0], w_up[0]], axis=1),
        )
        down_full = jnp.where(
            first,
            jnp.concatenate([w_down[0], other_down[0]], axis=0),
            jnp.concatenate([other_down[0], w_down[0]], axis=0),
        )
        return (gate_full, up_full, down_full)

    shard_blocks, slice_rows, kv_width = keys.shape
    pick_count = selected.shape[1]
    block_rows = slice_rows * n_eg
    my_eg = lax.axis_index("eg")
    both = jnp.concatenate([keys, values], axis=2)
    gathered = lax.all_gather(both[None], ("ctx", "eg"), axis=0, tiled=True)
    every_block = (
        gathered.reshape(n_ctx, n_eg, shard_blocks, slice_rows, 2 * kv_width)
        .transpose(0, 2, 1, 3, 4)
        .reshape(n_ctx * shard_blocks, block_rows, 2 * kv_width)
    )
    query_rows = queries.shape[0]
    my_block = (my_ctx * n_eg + my_eg) * query_rows // block_rows
    chosen_blocks = jnp.concatenate(
        [my_block[None].astype(jnp.int32), jnp.take(selected, my_block, axis=0)]
    )
    context = jnp.take(every_block, chosen_blocks, axis=0)
    context_keys = context[:, :, :kv_width]
    context_values = context[:, :, kv_width:]
    span = (1 + pick_count) * block_rows
    kv_heads = kv_width // HD
    attended = attend_rows(
        queries,
        context_keys.reshape(span, kv_heads, HD),
        context_values.reshape(span, kv_heads, HD),
    )
    tok_dev = residual.shape[0]
    pieces = {0: out_weight}
    for bit in reversed(range(n_eg.bit_length() - 1)):
        stride = 2**bit
        held = sorted(pieces)
        if len(held) > 1:
            barrier_out = lax.optimization_barrier((tuple(pieces[m] for m in held), attended))
            pieces = dict(zip(held, barrier_out[0]))
            attended = barrier_out[1]
        fetched = swapped(tuple(pieces[m] for m in held), "eg", bit)
        for m, piece in zip(held, fetched):
            pieces[m + stride] = piece
    weight_cols = jnp.concatenate([pieces[m] for m in range(n_eg)], axis=1)
    out_by_piece = jnp.dot(attended, weight_cols, preferred_element_type=jnp.float32).reshape(
        query_rows, n_eg, -1
    )
    piece_of_col = jnp.arange(n_eg, dtype=jnp.int32) ^ my_eg
    partial_out = jnp.take(out_by_piece, piece_of_col, axis=1).reshape(query_rows, -1)
    attn_out = lax.psum_scatter(
        partial_out.astype(jnp.bfloat16), "rep", scatter_dimension=0, tiled=True
    )
    stream = residual.astype(jnp.float32) + attn_out.astype(jnp.float32)
    meansq = jnp.mean(stream * stream, axis=1, keepdims=True)
    normed = (stream * lax.rsqrt(meansq + 1e-06) * norm_gain).astype(jnp.bfloat16)
    top_count = expert_ids.shape[1]
    slot_count = n_ctx * n_eg
    pair_count = tok_dev * top_count
    per_slot = pair_count // slot_count
    home_slot = jnp.take(expert_home, expert_ids.reshape(-1), axis=0)
    indicator = (home_slot[:, None] == jnp.arange(slot_count, dtype=jnp.int32)[None, :]).astype(
        jnp.int32
    )
    rank_in_slot = jnp.sum((jnp.cumsum(indicator, axis=0) - 1) * indicator, axis=1)
    position = home_slot * per_slot + rank_in_slot
    source_pair = (
        jnp.zeros((pair_count,), jnp.int32)
        .at[position]
        .set(jnp.arange(pair_count, dtype=jnp.int32))
    )
    partner = fetch_panels()
    if slot_count <= 4 * top_count:
        my_slot = my_ctx * n_eg + my_eg
        width = normed.shape[1]
        id_cols = jnp.full((tok_dev, 128), -1.0, jnp.bfloat16)
        id_cols = id_cols.at[:, :top_count].set(expert_ids.astype(jnp.bfloat16))
        packed = jnp.concatenate([normed, id_cols], axis=1)
        all_packed = lax.all_gather(packed, ("ctx", "eg"), axis=0, tiled=True)
        all_normed = all_packed[:, :width]
        all_ids = all_packed[:, width : width + top_count].astype(jnp.int32)
        expert_count = expert_home.shape[0]
        my_expert = jnp.sum(
            jnp.where(expert_home == my_slot, jnp.arange(expert_count, dtype=jnp.int32), 0)
        )
        hits = jnp.any(all_ids == my_expert, axis=1)
        hits = hits.reshape(slot_count, tok_dev).astype(jnp.int32)
        rank = jnp.cumsum(hits, axis=1) - 1
        chosen = jnp.logical_and(
            hits[:, None, :] == 1,
            rank[:, None, :] == jnp.arange(per_slot, dtype=jnp.int32)[None, :, None],
        )
        local_row = jnp.sum(
            chosen.astype(jnp.int32) * jnp.arange(tok_dev, dtype=jnp.int32)[None, None, :], axis=2
        )
        src_rows = local_row + jnp.arange(slot_count, dtype=jnp.int32)[:, None] * tok_dev
        pad_rows = ((0, all_packed.shape[1] - width), (0, 0))
        gate_act = jnp.dot(
            all_packed, jnp.pad(partner[0], pad_rows), preferred_element_type=jnp.float32
        )
        up_act = jnp.dot(
            all_packed, jnp.pad(partner[1], pad_rows), preferred_element_type=jnp.float32
        )
        activation = (jax.nn.silu(gate_act) * up_act).astype(jnp.bfloat16)
        picked = jnp.take(activation, src_rows.reshape(-1), axis=0)
        produced = jnp.dot(picked, partner[2], preferred_element_type=jnp.float32).astype(
            jnp.bfloat16
        )
    else:
        outbound = jnp.take(normed, source_pair // top_count, axis=0).reshape(
            slot_count, per_slot, -1
        )
        arrived = lax.all_to_all(outbound, ("ctx", "eg"), split_axis=0, concat_axis=0, tiled=True)
        flat_rows = arrived.reshape(-1, arrived.shape[2])
        produced = expert_apply(flat_rows, partner[0], partner[1], partner[2])
    returned = lax.all_to_all(
        produced.reshape(slot_count, per_slot, -1),
        ("ctx", "eg"),
        split_axis=0,
        concat_axis=0,
        tiled=True,
    )
    returned_rows = returned.reshape(pair_count, -1)
    placed = position.reshape(tok_dev, top_count)[:, :, None] == jnp.arange(
        pair_count, dtype=jnp.int32
    )[None, None, :]
    mixing = jnp.sum(jnp.where(placed, gate_weights[:, :, None], 0.0), axis=1)
    combined = jnp.zeros((tok_dev, returned_rows.shape[1]), jnp.float32)
    remainder = mixing
    for _ in range(3):
        part = remainder.astype(jnp.bfloat16)
        remainder = remainder - part.astype(jnp.float32)
        combined = combined + jnp.dot(part, returned_rows, preferred_element_type=jnp.float32)
    moe_out = combined.astype(jnp.bfloat16)
    return (attn_out, moe_out)


def solution(mesh):
    return jax.shard_map(
        local,
        mesh=mesh,
        in_specs=(
            P(("groups", "ctx", "eg"), "rep"),
            P(("groups", "ctx"), "eg", "rep"),
            P(("groups", "ctx"), "eg", "rep"),
            P("groups", None),
            P("rep", "eg"),
            P(("groups", "ctx", "eg", "rep"), None),
            P(),
            P(("groups", "ctx", "eg", "rep"), None),
            P(("groups", "ctx", "eg", "rep"), None),
            P(),
            P(("ctx", "eg"), None, "rep"),
            P(("ctx", "eg"), None, "rep"),
            P(("ctx", "eg"), "rep", None),
        ),
        out_specs=(
            P(("groups", "ctx", "eg", "rep"), None),
            P(("groups", "ctx", "eg", "rep"), None),
        ),
        check_vma=False,
    )
```

```python
import math

import jax
import jax.numpy as jnp
from jax import lax
from jax.sharding import PartitionSpec as P

HD = 128


def swapped(value, axis, bit):
    mask = 2**bit
    pairs = [(source, source ^ mask) for source in range(lax.axis_size(axis))]
    return lax.ppermute(value, axis, pairs)


def attend_rows(queries_flat, key_rows, value_rows):
    row_count = queries_flat.shape[0]
    kv_heads = key_rows.shape[1]
    per_group = queries_flat.shape[1] // (kv_heads * HD)
    inverse_root = 1.0 / math.sqrt(HD)
    arranged = queries_flat.reshape(row_count, kv_heads, per_group, HD).transpose(1, 2, 0, 3)
    logits = (
        jnp.einsum("kgrd,nkd->kgrn", arranged, key_rows, preferred_element_type=jnp.float32)
        * inverse_root
    )
    largest = jnp.max(logits, axis=-1, keepdims=True)
    raised = jnp.exp(logits - largest)
    denominator = jnp.sum(raised, axis=-1, keepdims=True)
    weights_low = (raised / denominator).astype(jnp.bfloat16)
    blended = jnp.einsum(
        "kgrn,nkd->rkgd", weights_low, value_rows, preferred_element_type=jnp.float32
    )
    return blended.astype(jnp.bfloat16).reshape(row_count, kv_heads * per_group * HD)


def expert_apply(rows_in, gate_full, up_full, down_full):
    gate_act = jnp.dot(rows_in, gate_full, preferred_element_type=jnp.float32)
    up_act = jnp.dot(rows_in, up_full, preferred_element_type=jnp.float32)
    activation = (jax.nn.silu(gate_act) * up_act).astype(jnp.bfloat16)
    return jnp.dot(activation, down_full, preferred_element_type=jnp.float32).astype(jnp.bfloat16)


def local(
    queries,
    keys,
    values,
    selected,
    out_weight,
    residual,
    norm_gain,
    expert_ids,
    gate_weights,
    expert_home,
    w_gate,
    w_up,
    w_down,
):
    n_ctx = lax.axis_size("ctx")
    n_eg = lax.axis_size("eg")
    n_rep = lax.axis_size("rep")
    my_ctx = lax.axis_index("ctx")

    def fetch_panels():
        if n_rep == 1:
            return (w_gate[0], w_up[0], w_down[0])
        other_gate, other_up, other_down = swapped((w_gate, w_up, w_down), "rep", 0)
        first = lax.axis_index("rep") == 0
        gate_full = jnp.where(
            first,
            jnp.concatenate([w_gate[0], other_gate[0]], axis=1),
            jnp.concatenate([other_gate[0], w_gate[0]], axis=1),
        )
        up_full = jnp.where(
            first,
            jnp.concatenate([w_up[0], other_up[0]], axis=1),
            jnp.concatenate([other_up[0], w_up[0]], axis=1),
        )
        down_full = jnp.where(
            first,
            jnp.concatenate([w_down[0], other_down[0]], axis=0),
            jnp.concatenate([other_down[0], w_down[0]], axis=0),
        )
        return (gate_full, up_full, down_full)

    shard_blocks, slice_rows, kv_width = keys.shape
    pick_count = selected.shape[1]
    block_rows = slice_rows * n_eg
    my_eg = lax.axis_index("eg")
    both = jnp.concatenate([keys, values], axis=2)
    copies = jnp.broadcast_to(both[None], (n_ctx * n_eg,) + both.shape)
    gathered = lax.all_to_all(copies, ("ctx", "eg"), split_axis=0, concat_axis=0, tiled=True)
    every_block = (
        gathered.reshape(n_ctx, n_eg, shard_blocks, slice_rows, 2 * kv_width)
        .transpose(0, 2, 1, 3, 4)
        .reshape(n_ctx * shard_blocks, block_rows, 2 * kv_width)
    )
    query_rows = queries.shape[0]
    my_block = (my_ctx * n_eg + my_eg) * query_rows // block_rows
    chosen_blocks = jnp.concatenate(
        [my_block[None].astype(jnp.int32), jnp.take(selected, my_block, axis=0)]
    )
    context = jnp.take(every_block, chosen_blocks, axis=0)
    context_keys = context[:, :, :kv_width]
    context_values = context[:, :, kv_width:]
    span = (1 + pick_count) * block_rows
    kv_heads = kv_width // HD
    attended = attend_rows(
        queries,
        context_keys.reshape(span, kv_heads, HD),
        context_values.reshape(span, kv_heads, HD),
    )
    tok_dev = residual.shape[0]
    pieces = {0: out_weight}
    for bit in reversed(range(n_eg.bit_length() - 1)):
        stride = 2**bit
        held = sorted(pieces)
        if len(held) > 1:
            barrier_out = lax.optimization_barrier((tuple(pieces[m] for m in held), attended))
            pieces = dict(zip(held, barrier_out[0]))
            attended = barrier_out[1]
        fetched = swapped(tuple(pieces[m] for m in held), "eg", bit)
        for m, piece in zip(held, fetched):
            pieces[m + stride] = piece
    weight_cols = jnp.concatenate([pieces[m] for m in range(n_eg)], axis=1)
    out_by_piece = jnp.dot(attended, weight_cols, preferred_element_type=jnp.float32).reshape(
        query_rows, n_eg, -1
    )
    piece_of_col = jnp.arange(n_eg, dtype=jnp.int32) ^ my_eg
    partial_out = jnp.take(out_by_piece, piece_of_col, axis=1).reshape(query_rows, -1)
    attn_out = lax.psum_scatter(
        partial_out.astype(jnp.bfloat16), "rep", scatter_dimension=0, tiled=True
    )
    stream = residual.astype(jnp.float32) + attn_out.astype(jnp.float32)
    meansq = jnp.mean(stream * stream, axis=1, keepdims=True)
    normed = (stream * lax.rsqrt(meansq + 1e-06) * norm_gain).astype(jnp.bfloat16)
    top_count = expert_ids.shape[1]
    slot_count = n_ctx * n_eg
    pair_count = tok_dev * top_count
    per_slot = pair_count // slot_count
    home_slot = jnp.take(expert_home, expert_ids.reshape(-1), axis=0)
    indicator = (home_slot[:, None] == jnp.arange(slot_count, dtype=jnp.int32)[None, :]).astype(
        jnp.int32
    )
    rank_in_slot = jnp.sum((jnp.cumsum(indicator, axis=0) - 1) * indicator, axis=1)
    position = home_slot * per_slot + rank_in_slot
    source_pair = (
        jnp.zeros((pair_count,), jnp.int32)
        .at[position]
        .set(jnp.arange(pair_count, dtype=jnp.int32))
    )
    partner = fetch_panels()
    if slot_count <= 4 * top_count:
        my_slot = my_ctx * n_eg + my_eg
        width = normed.shape[1]
        id_cols = jnp.full((tok_dev, 128), -1.0, jnp.bfloat16)
        id_cols = id_cols.at[:, :top_count].set(expert_ids.astype(jnp.bfloat16))
        packed = jnp.concatenate([normed, id_cols], axis=1)
        all_packed = lax.all_gather(packed, ("ctx", "eg"), axis=0, tiled=True)
        all_normed = all_packed[:, :width]
        all_ids = all_packed[:, width : width + top_count].astype(jnp.int32)
        expert_count = expert_home.shape[0]
        my_expert = jnp.sum(
            jnp.where(expert_home == my_slot, jnp.arange(expert_count, dtype=jnp.int32), 0)
        )
        hits = jnp.any(all_ids == my_expert, axis=1)
        hits = hits.reshape(slot_count, tok_dev).astype(jnp.int32)
        rank = jnp.cumsum(hits, axis=1) - 1
        chosen = jnp.logical_and(
            hits[:, None, :] == 1,
            rank[:, None, :] == jnp.arange(per_slot, dtype=jnp.int32)[None, :, None],
        )
        local_row = jnp.sum(
            chosen.astype(jnp.int32) * jnp.arange(tok_dev, dtype=jnp.int32)[None, None, :], axis=2
        )
        src_rows = local_row + jnp.arange(slot_count, dtype=jnp.int32)[:, None] * tok_dev
        pad_rows = ((0, all_packed.shape[1] - width), (0, 0))
        gate_act = jnp.dot(
            all_packed, jnp.pad(partner[0], pad_rows), preferred_element_type=jnp.float32
        )
        up_act = jnp.dot(
            all_packed, jnp.pad(partner[1], pad_rows), preferred_element_type=jnp.float32
        )
        activation = (jax.nn.silu(gate_act) * up_act).astype(jnp.bfloat16)
        picked = jnp.take(activation, src_rows.reshape(-1), axis=0)
        produced = jnp.dot(picked, partner[2], preferred_element_type=jnp.float32).astype(
            jnp.bfloat16
        )
    else:
        outbound = jnp.take(normed, source_pair // top_count, axis=0).reshape(
            slot_count, per_slot, -1
        )
        arrived = lax.all_to_all(outbound, ("ctx", "eg"), split_axis=0, concat_axis=0, tiled=True)
        flat_rows = arrived.reshape(-1, arrived.shape[2])
        produced = expert_apply(flat_rows, partner[0], partner[1], partner[2])
    returned = lax.all_to_all(
        produced.reshape(slot_count, per_slot, -1),
        ("ctx", "eg"),
        split_axis=0,
        concat_axis=0,
        tiled=True,
    )
    returned_rows = returned.reshape(pair_count, -1)
    placed = position.reshape(tok_dev, top_count)[:, :, None] == jnp.arange(
        pair_count, dtype=jnp.int32
    )[None, None, :]
    mixing = jnp.sum(jnp.where(placed, gate_weights[:, :, None], 0.0), axis=1)
    combined = jnp.zeros((tok_dev, returned_rows.shape[1]), jnp.float32)
    remainder = mixing
    for _ in range(3):
        part = remainder.astype(jnp.bfloat16)
        remainder = remainder - part.astype(jnp.float32)
        combined = combined + jnp.dot(part, returned_rows, preferred_element_type=jnp.float32)
    moe_out = combined.astype(jnp.bfloat16)
    return (attn_out, moe_out)


def solution(mesh):
    return jax.shard_map(
        local,
        mesh=mesh,
        in_specs=(
            P(("groups", "ctx", "eg"), "rep"),
            P(("groups", "ctx"), "eg", "rep"),
            P(("groups", "ctx"), "eg", "rep"),
            P("groups", None),
            P("rep", "eg"),
            P(("groups", "ctx", "eg", "rep"), None),
            P(),
            P(("groups", "ctx", "eg", "rep"), None),
            P(("groups", "ctx", "eg", "rep"), None),
            P(),
            P(("ctx", "eg"), None, "rep"),
            P(("ctx", "eg"), None, "rep"),
            P(("ctx", "eg"), "rep", None),
        ),
        out_specs=(
            P(("groups", "ctx", "eg", "rep"), None),
            P(("groups", "ctx", "eg", "rep"), None),
        ),
        check_vma=False,
    )
```

```python
import math

import jax
import jax.numpy as jnp
from jax import lax
from jax.sharding import PartitionSpec as P

HD = 128


def swapped(value, axis, bit):
    mask = 2**bit
    pairs = [(source, source ^ mask) for source in range(lax.axis_size(axis))]
    return lax.ppermute(value, axis, pairs)


def attend_rows(queries_flat, key_rows, value_rows):
    row_count = queries_flat.shape[0]
    kv_heads = key_rows.shape[1]
    per_group = queries_flat.shape[1] // (kv_heads * HD)
    inverse_root = 1.0 / math.sqrt(HD)
    arranged = queries_flat.reshape(row_count, kv_heads, per_group, HD).transpose(1, 2, 0, 3)
    logits = (
        jnp.einsum("kgrd,nkd->kgrn", arranged, key_rows, preferred_element_type=jnp.float32)
        * inverse_root
    )
    largest = jnp.max(logits, axis=-1, keepdims=True)
    raised = jnp.exp(logits - largest)
    denominator = jnp.sum(raised, axis=-1, keepdims=True)
    weights_low = (raised / denominator).astype(jnp.bfloat16)
    blended = jnp.einsum(
        "kgrn,nkd->rkgd", weights_low, value_rows, preferred_element_type=jnp.float32
    )
    return blended.astype(jnp.bfloat16).reshape(row_count, kv_heads * per_group * HD)


def expert_apply(rows_in, gate_full, up_full, down_full):
    gate_act = jnp.dot(rows_in, gate_full, preferred_element_type=jnp.float32)
    up_act = jnp.dot(rows_in, up_full, preferred_element_type=jnp.float32)
    activation = (jax.nn.silu(gate_act) * up_act).astype(jnp.bfloat16)
    return jnp.dot(activation, down_full, preferred_element_type=jnp.float32).astype(jnp.bfloat16)


def local(
    queries,
    keys,
    values,
    selected,
    out_weight,
    residual,
    norm_gain,
    expert_ids,
    gate_weights,
    expert_home,
    w_gate,
    w_up,
    w_down,
):
    n_ctx = lax.axis_size("ctx")
    n_eg = lax.axis_size("eg")
    n_rep = lax.axis_size("rep")
    my_ctx = lax.axis_index("ctx")

    def fetch_panels():
        if n_rep == 1:
            return (w_gate[0], w_up[0], w_down[0])
        other_gate, other_up, other_down = swapped((w_gate, w_up, w_down), "rep", 0)
        first = lax.axis_index("rep") == 0
        gate_full = jnp.where(
            first,
            jnp.concatenate([w_gate[0], other_gate[0]], axis=1),
            jnp.concatenate([other_gate[0], w_gate[0]], axis=1),
        )
        up_full = jnp.where(
            first,
            jnp.concatenate([w_up[0], other_up[0]], axis=1),
            jnp.concatenate([other_up[0], w_up[0]], axis=1),
        )
        down_full = jnp.where(
            first,
            jnp.concatenate([w_down[0], other_down[0]], axis=0),
            jnp.concatenate([other_down[0], w_down[0]], axis=0),
        )
        return (gate_full, up_full, down_full)

    shard_blocks, slice_rows, kv_width = keys.shape
    pick_count = selected.shape[1]
    block_rows = slice_rows * n_eg
    my_eg = lax.axis_index("eg")
    both = jnp.concatenate([keys, values], axis=2)
    gathered = lax.all_gather(both[None], ("ctx", "eg"), axis=0, tiled=True)
    every_block = (
        gathered.reshape(n_ctx, n_eg, shard_blocks, slice_rows, 2 * kv_width)
        .transpose(0, 2, 1, 3, 4)
        .reshape(n_ctx * shard_blocks, block_rows, 2 * kv_width)
    )
    query_rows = queries.shape[0]
    my_block = (my_ctx * n_eg + my_eg) * query_rows // block_rows
    chosen_blocks = jnp.concatenate(
        [my_block[None].astype(jnp.int32), jnp.take(selected, my_block, axis=0)]
    )
    context = jnp.take(every_block, chosen_blocks, axis=0)
    context_keys = context[:, :, :kv_width]
    context_values = context[:, :, kv_width:]
    span = (1 + pick_count) * block_rows
    kv_heads = kv_width // HD
    attended = attend_rows(
        queries,
        context_keys.reshape(span, kv_heads, HD),
        context_values.reshape(span, kv_heads, HD),
    )
    tok_dev = residual.shape[0]
    pieces = {0: out_weight}
    for bit in reversed(range(n_eg.bit_length() - 1)):
        stride = 2**bit
        held = sorted(pieces)
        if len(held) > 1:
            barrier_out = lax.optimization_barrier((tuple(pieces[m] for m in held), attended))
            pieces = dict(zip(held, barrier_out[0]))
            attended = barrier_out[1]
        fetched = swapped(tuple(pieces[m] for m in held), "eg", bit)
        for m, piece in zip(held, fetched):
            pieces[m + stride] = piece
    weight_cols = jnp.concatenate([pieces[m] for m in range(n_eg)], axis=1)
    out_by_piece = jnp.dot(attended, weight_cols, preferred_element_type=jnp.float32).reshape(
        query_rows, n_eg, -1
    )
    piece_of_col = jnp.arange(n_eg, dtype=jnp.int32) ^ my_eg
    partial_out = jnp.take(out_by_piece, piece_of_col, axis=1).reshape(query_rows, -1)
    attn_out = lax.psum_scatter(
        partial_out.astype(jnp.bfloat16), "rep", scatter_dimension=0, tiled=True
    )
    stream = residual.astype(jnp.float32) + attn_out.astype(jnp.float32)
    meansq = jnp.mean(stream * stream, axis=1, keepdims=True)
    normed = (stream * lax.rsqrt(meansq + 1e-06) * norm_gain).astype(jnp.bfloat16)
    top_count = expert_ids.shape[1]
    slot_count = n_ctx * n_eg
    pair_count = tok_dev * top_count
    per_slot = pair_count // slot_count
    home_slot = jnp.take(expert_home, expert_ids.reshape(-1), axis=0)
    indicator = (home_slot[:, None] == jnp.arange(slot_count, dtype=jnp.int32)[None, :]).astype(
        jnp.int32
    )
    rank_in_slot = jnp.sum((jnp.cumsum(indicator, axis=0) - 1) * indicator, axis=1)
    position = home_slot * per_slot + rank_in_slot
    source_pair = (
        jnp.zeros((pair_count,), jnp.int32)
        .at[position]
        .set(jnp.arange(pair_count, dtype=jnp.int32))
    )
    partner = fetch_panels()
    if slot_count <= 4 * top_count:
        my_slot = my_ctx * n_eg + my_eg
        width = normed.shape[1]
        id_cols = jnp.full((tok_dev, 128), -1.0, jnp.bfloat16)
        id_cols = id_cols.at[:, :top_count].set(expert_ids.astype(jnp.bfloat16))
        lead = width // 2
        packed = jnp.concatenate([normed[:, :lead], id_cols], axis=1)
        all_packed = lax.all_gather(packed, ("ctx", "eg"), axis=0, tiled=True)
        trailing = jnp.take(normed[:, lead:], source_pair // top_count, axis=0).reshape(
            slot_count, per_slot, width - lead
        )
        arrived = lax.all_to_all(trailing, ("ctx", "eg"), split_axis=0, concat_axis=0, tiled=True)
        all_ids = all_packed[:, lead : lead + top_count].astype(jnp.int32)
        expert_count = expert_home.shape[0]
        my_expert = jnp.sum(
            jnp.where(expert_home == my_slot, jnp.arange(expert_count, dtype=jnp.int32), 0)
        )
        hits = jnp.any(all_ids == my_expert, axis=1)
        hits = hits.reshape(slot_count, tok_dev).astype(jnp.int32)
        rank = jnp.cumsum(hits, axis=1) - 1
        chosen = jnp.logical_and(
            hits[:, None, :] == 1,
            rank[:, None, :] == jnp.arange(per_slot, dtype=jnp.int32)[None, :, None],
        )
        local_row = jnp.sum(
            chosen.astype(jnp.int32) * jnp.arange(tok_dev, dtype=jnp.int32)[None, None, :], axis=2
        )
        src_rows = local_row + jnp.arange(slot_count, dtype=jnp.int32)[:, None] * tok_dev
        leading = jnp.take(all_packed[:, :lead], src_rows.reshape(-1), axis=0)
        flat_rows = jnp.concatenate([leading, arrived.reshape(pair_count, width - lead)], axis=1)
        produced = expert_apply(flat_rows, partner[0], partner[1], partner[2])
    else:
        outbound = jnp.take(normed, source_pair // top_count, axis=0).reshape(
            slot_count, per_slot, -1
        )
        arrived = lax.all_to_all(outbound, ("ctx", "eg"), split_axis=0, concat_axis=0, tiled=True)
        flat_rows = arrived.reshape(-1, arrived.shape[2])
        produced = expert_apply(flat_rows, partner[0], partner[1], partner[2])
    returned = lax.all_to_all(
        produced.reshape(slot_count, per_slot, -1),
        ("ctx", "eg"),
        split_axis=0,
        concat_axis=0,
        tiled=True,
    )
    returned_rows = returned.reshape(pair_count, -1)
    placed = position.reshape(tok_dev, top_count)[:, :, None] == jnp.arange(
        pair_count, dtype=jnp.int32
    )[None, None, :]
    mixing = jnp.sum(jnp.where(placed, gate_weights[:, :, None], 0.0), axis=1)
    combined = jnp.zeros((tok_dev, returned_rows.shape[1]), jnp.float32)
    remainder = mixing
    for _ in range(3):
        part = remainder.astype(jnp.bfloat16)
        remainder = remainder - part.astype(jnp.float32)
        combined = combined + jnp.dot(part, returned_rows, preferred_element_type=jnp.float32)
    moe_out = combined.astype(jnp.bfloat16)
    return (attn_out, moe_out)


def solution(mesh):
    return jax.shard_map(
        local,
        mesh=mesh,
        in_specs=(
            P(("groups", "ctx", "eg"), "rep"),
            P(("groups", "ctx"), "eg", "rep"),
            P(("groups", "ctx"), "eg", "rep"),
            P("groups", None),
            P("rep", "eg"),
            P(("groups", "ctx", "eg", "rep"), None),
            P(),
            P(("groups", "ctx", "eg", "rep"), None),
            P(("groups", "ctx", "eg", "rep"), None),
            P(),
            P(("ctx", "eg"), None, "rep"),
            P(("ctx", "eg"), None, "rep"),
            P(("ctx", "eg"), "rep", None),
        ),
        out_specs=(
            P(("groups", "ctx", "eg", "rep"), None),
            P(("groups", "ctx", "eg", "rep"), None),
        ),
        check_vma=False,
    )
```

```python
import math

import jax
import jax.numpy as jnp
from jax import lax
from jax.sharding import PartitionSpec as P

HD = 128


def swapped(value, axis, bit):
    mask = 2**bit
    pairs = [(source, source ^ mask) for source in range(lax.axis_size(axis))]
    return lax.ppermute(value, axis, pairs)


def attend_rows(queries_flat, key_rows, value_rows):
    row_count = queries_flat.shape[0]
    kv_heads = key_rows.shape[1]
    per_group = queries_flat.shape[1] // (kv_heads * HD)
    inverse_root = 1.0 / math.sqrt(HD)
    arranged = queries_flat.reshape(row_count, kv_heads, per_group, HD).transpose(1, 2, 0, 3)
    logits = (
        jnp.einsum("kgrd,nkd->kgrn", arranged, key_rows, preferred_element_type=jnp.float32)
        * inverse_root
    )
    largest = jnp.max(logits, axis=-1, keepdims=True)
    raised = jnp.exp(logits - largest)
    denominator = jnp.sum(raised, axis=-1, keepdims=True)
    weights_low = (raised / denominator).astype(jnp.bfloat16)
    blended = jnp.einsum(
        "kgrn,nkd->rkgd", weights_low, value_rows, preferred_element_type=jnp.float32
    )
    return blended.astype(jnp.bfloat16).reshape(row_count, kv_heads * per_group * HD)


def expert_apply(rows_in, gate_full, up_full, down_full):
    gate_act = jnp.dot(rows_in, gate_full, preferred_element_type=jnp.float32)
    up_act = jnp.dot(rows_in, up_full, preferred_element_type=jnp.float32)
    activation = (jax.nn.silu(gate_act) * up_act).astype(jnp.bfloat16)
    return jnp.dot(activation, down_full, preferred_element_type=jnp.float32).astype(jnp.bfloat16)


def local(
    queries,
    keys,
    values,
    selected,
    out_weight,
    residual,
    norm_gain,
    expert_ids,
    gate_weights,
    expert_home,
    w_gate,
    w_up,
    w_down,
):
    n_ctx = lax.axis_size("ctx")
    n_eg = lax.axis_size("eg")
    n_rep = lax.axis_size("rep")
    my_ctx = lax.axis_index("ctx")

    def fetch_panels():
        if n_rep == 1:
            return (w_gate[0], w_up[0], w_down[0])
        other_gate, other_up, other_down = swapped((w_gate, w_up, w_down), "rep", 0)
        first = lax.axis_index("rep") == 0
        gate_full = jnp.where(
            first,
            jnp.concatenate([w_gate[0], other_gate[0]], axis=1),
            jnp.concatenate([other_gate[0], w_gate[0]], axis=1),
        )
        up_full = jnp.where(
            first,
            jnp.concatenate([w_up[0], other_up[0]], axis=1),
            jnp.concatenate([other_up[0], w_up[0]], axis=1),
        )
        down_full = jnp.where(
            first,
            jnp.concatenate([w_down[0], other_down[0]], axis=0),
            jnp.concatenate([other_down[0], w_down[0]], axis=0),
        )
        return (gate_full, up_full, down_full)

    shard_blocks, slice_rows, kv_width = keys.shape
    pick_count = selected.shape[1]
    block_rows = slice_rows * n_eg
    my_eg = lax.axis_index("eg")
    both = jnp.concatenate([keys, values], axis=2)
    query_rows = queries.shape[0]
    my_block = (my_ctx * n_eg + my_eg) * query_rows // block_rows
    chosen_blocks = jnp.concatenate(
        [my_block[None].astype(jnp.int32), jnp.take(selected, my_block, axis=0)]
    )
    if n_ctx * n_eg <= 16:
        received = []
        for ctx_step in range(n_ctx):
            for eg_flip in range(n_eg):
                if ctx_step == 0 and eg_flip == 0:
                    received.append(both)
                    continue
                pairs = [
                    (c * n_eg + e, ((c + ctx_step) % n_ctx) * n_eg + (e ^ eg_flip))
                    for c in range(n_ctx)
                    for e in range(n_eg)
                ]
                received.append(lax.ppermute(both, ("ctx", "eg"), pairs))
        stacked = jnp.stack(received).reshape(
            n_ctx, n_eg, shard_blocks, slice_rows, 2 * kv_width
        )
        source_ctx = chosen_blocks // shard_blocks
        by_block = jnp.take(stacked, (my_ctx - source_ctx) % n_ctx, axis=0)
        by_block = jnp.take(by_block, jnp.arange(n_eg, dtype=jnp.int32) ^ my_eg, axis=1)
        inner = chosen_blocks % shard_blocks
        context = jnp.take_along_axis(
            by_block, inner[:, None, None, None, None], axis=2
        ).reshape(1 + pick_count, block_rows, 2 * kv_width)
    else:
        gathered = lax.all_gather(both[None], ("ctx", "eg"), axis=0, tiled=True)
        every_block = (
            gathered.reshape(n_ctx, n_eg, shard_blocks, slice_rows, 2 * kv_width)
            .transpose(0, 2, 1, 3, 4)
            .reshape(n_ctx * shard_blocks, block_rows, 2 * kv_width)
        )
        context = jnp.take(every_block, chosen_blocks, axis=0)
    context_keys = context[:, :, :kv_width]
    context_values = context[:, :, kv_width:]
    span = (1 + pick_count) * block_rows
    kv_heads = kv_width // HD
    attended = attend_rows(
        queries,
        context_keys.reshape(span, kv_heads, HD),
        context_values.reshape(span, kv_heads, HD),
    )
    tok_dev = residual.shape[0]
    pieces = {0: out_weight}
    for bit in reversed(range(n_eg.bit_length() - 1)):
        stride = 2**bit
        held = sorted(pieces)
        if len(held) > 1:
            barrier_out = lax.optimization_barrier((tuple(pieces[m] for m in held), attended))
            pieces = dict(zip(held, barrier_out[0]))
            attended = barrier_out[1]
        fetched = swapped(tuple(pieces[m] for m in held), "eg", bit)
        for m, piece in zip(held, fetched):
            pieces[m + stride] = piece
    weight_cols = jnp.concatenate([pieces[m] for m in range(n_eg)], axis=1)
    out_by_piece = jnp.dot(attended, weight_cols, preferred_element_type=jnp.float32).reshape(
        query_rows, n_eg, -1
    )
    piece_of_col = jnp.arange(n_eg, dtype=jnp.int32) ^ my_eg
    partial_out = jnp.take(out_by_piece, piece_of_col, axis=1).reshape(query_rows, -1)
    attn_out = lax.psum_scatter(
        partial_out.astype(jnp.bfloat16), "rep", scatter_dimension=0, tiled=True
    )
    stream = residual.astype(jnp.float32) + attn_out.astype(jnp.float32)
    meansq = jnp.mean(stream * stream, axis=1, keepdims=True)
    normed = (stream * lax.rsqrt(meansq + 1e-06) * norm_gain).astype(jnp.bfloat16)
    top_count = expert_ids.shape[1]
    slot_count = n_ctx * n_eg
    pair_count = tok_dev * top_count
    per_slot = pair_count // slot_count
    home_slot = jnp.take(expert_home, expert_ids.reshape(-1), axis=0)
    indicator = (home_slot[:, None] == jnp.arange(slot_count, dtype=jnp.int32)[None, :]).astype(
        jnp.int32
    )
    rank_in_slot = jnp.sum((jnp.cumsum(indicator, axis=0) - 1) * indicator, axis=1)
    position = home_slot * per_slot + rank_in_slot
    source_pair = (
        jnp.zeros((pair_count,), jnp.int32)
        .at[position]
        .set(jnp.arange(pair_count, dtype=jnp.int32))
    )
    partner = fetch_panels()
    if slot_count <= 4 * top_count:
        my_slot = my_ctx * n_eg + my_eg
        width = normed.shape[1]
        id_cols = jnp.full((tok_dev, 128), -1.0, jnp.bfloat16)
        id_cols = id_cols.at[:, :top_count].set(expert_ids.astype(jnp.bfloat16))
        packed = jnp.concatenate([normed, id_cols], axis=1)
        all_packed = lax.all_gather(packed, ("ctx", "eg"), axis=0, tiled=True)
        all_normed = all_packed[:, :width]
        all_ids = all_packed[:, width : width + top_count].astype(jnp.int32)
        expert_count = expert_home.shape[0]
        my_expert = jnp.sum(
            jnp.where(expert_home == my_slot, jnp.arange(expert_count, dtype=jnp.int32), 0)
        )
        hits = jnp.any(all_ids == my_expert, axis=1)
        hits = hits.reshape(slot_count, tok_dev).astype(jnp.int32)
        rank = jnp.cumsum(hits, axis=1) - 1
        chosen = jnp.logical_and(
            hits[:, None, :] == 1,
            rank[:, None, :] == jnp.arange(per_slot, dtype=jnp.int32)[None, :, None],
        )
        local_row = jnp.sum(
            chosen.astype(jnp.int32) * jnp.arange(tok_dev, dtype=jnp.int32)[None, None, :], axis=2
        )
        src_rows = local_row + jnp.arange(slot_count, dtype=jnp.int32)[:, None] * tok_dev
        pad_rows = ((0, all_packed.shape[1] - width), (0, 0))
        gate_act = jnp.dot(
            all_packed, jnp.pad(partner[0], pad_rows), preferred_element_type=jnp.float32
        )
        up_act = jnp.dot(
            all_packed, jnp.pad(partner[1], pad_rows), preferred_element_type=jnp.float32
        )
        activation = (jax.nn.silu(gate_act) * up_act).astype(jnp.bfloat16)
        pick_matrix = (
            src_rows.reshape(-1)[:, None]
            == jnp.arange(activation.shape[0], dtype=jnp.int32)[None, :]
        ).astype(jnp.bfloat16)
        picked = jnp.dot(pick_matrix, activation, preferred_element_type=jnp.float32).astype(
            jnp.bfloat16
        )
        produced = jnp.dot(picked, partner[2], preferred_element_type=jnp.float32).astype(
            jnp.bfloat16
        )
    else:
        outbound = jnp.take(normed, source_pair // top_count, axis=0).reshape(
            slot_count, per_slot, -1
        )
        arrived = lax.all_to_all(outbound, ("ctx", "eg"), split_axis=0, concat_axis=0, tiled=True)
        flat_rows = arrived.reshape(-1, arrived.shape[2])
        produced = expert_apply(flat_rows, partner[0], partner[1], partner[2])
    returned = lax.all_to_all(
        produced.reshape(slot_count, per_slot, -1),
        ("ctx", "eg"),
        split_axis=0,
        concat_axis=0,
        tiled=True,
    )
    returned_rows = returned.reshape(pair_count, -1)
    placed = position.reshape(tok_dev, top_count)[:, :, None] == jnp.arange(
        pair_count, dtype=jnp.int32
    )[None, None, :]
    mixing = jnp.sum(jnp.where(placed, gate_weights[:, :, None], 0.0), axis=1)
    combined = jnp.zeros((tok_dev, returned_rows.shape[1]), jnp.float32)
    remainder = mixing
    for _ in range(3):
        part = remainder.astype(jnp.bfloat16)
        remainder = remainder - part.astype(jnp.float32)
        combined = combined + jnp.dot(part, returned_rows, preferred_element_type=jnp.float32)
    moe_out = combined.astype(jnp.bfloat16)
    return (attn_out, moe_out)


def solution(mesh):
    return jax.shard_map(
        local,
        mesh=mesh,
        in_specs=(
            P(("groups", "ctx", "eg"), "rep"),
            P(("groups", "ctx"), "eg", "rep"),
            P(("groups", "ctx"), "eg", "rep"),
            P("groups", None),
            P("rep", "eg"),
            P(("groups", "ctx", "eg", "rep"), None),
            P(),
            P(("groups", "ctx", "eg", "rep"), None),
            P(("groups", "ctx", "eg", "rep"), None),
            P(),
            P(("ctx", "eg"), None, "rep"),
            P(("ctx", "eg"), None, "rep"),
            P(("ctx", "eg"), "rep", None),
        ),
        out_specs=(
            P(("groups", "ctx", "eg", "rep"), None),
            P(("groups", "ctx", "eg", "rep"), None),
        ),
        check_vma=False,
    )
```

```python
import math

import jax
import jax.numpy as jnp
from jax import lax
from jax.sharding import PartitionSpec as P

HD = 128


def swapped(value, axis, bit):
    mask = 2**bit
    pairs = [(source, source ^ mask) for source in range(lax.axis_size(axis))]
    return lax.ppermute(value, axis, pairs)


def attend_rows(queries_flat, key_rows, value_rows):
    row_count = queries_flat.shape[0]
    kv_heads = key_rows.shape[1]
    per_group = queries_flat.shape[1] // (kv_heads * HD)
    inverse_root = 1.0 / math.sqrt(HD)
    arranged = queries_flat.reshape(row_count, kv_heads, per_group, HD).transpose(1, 2, 0, 3)
    logits = (
        jnp.einsum("kgrd,nkd->kgrn", arranged, key_rows, preferred_element_type=jnp.float32)
        * inverse_root
    )
    largest = jnp.max(logits, axis=-1, keepdims=True)
    raised = jnp.exp(logits - largest)
    denominator = jnp.sum(raised, axis=-1, keepdims=True)
    weights_low = (raised / denominator).astype(jnp.bfloat16)
    blended = jnp.einsum(
        "kgrn,nkd->rkgd", weights_low, value_rows, preferred_element_type=jnp.float32
    )
    return blended.astype(jnp.bfloat16).reshape(row_count, kv_heads * per_group * HD)


def expert_apply(rows_in, gate_full, up_full, down_full):
    gate_act = jnp.dot(rows_in, gate_full, preferred_element_type=jnp.float32)
    up_act = jnp.dot(rows_in, up_full, preferred_element_type=jnp.float32)
    activation = (jax.nn.silu(gate_act) * up_act).astype(jnp.bfloat16)
    return jnp.dot(activation, down_full, preferred_element_type=jnp.float32).astype(jnp.bfloat16)


def local(
    queries,
    keys,
    values,
    selected,
    out_weight,
    residual,
    norm_gain,
    expert_ids,
    gate_weights,
    expert_home,
    w_gate,
    w_up,
    w_down,
):
    n_ctx = lax.axis_size("ctx")
    n_eg = lax.axis_size("eg")
    n_rep = lax.axis_size("rep")
    my_ctx = lax.axis_index("ctx")

    def fetch_panels():
        if n_rep == 1:
            return (w_gate[0], w_up[0], w_down[0])
        other_gate, other_up, other_down = swapped((w_gate, w_up, w_down), "rep", 0)
        first = lax.axis_index("rep") == 0
        gate_full = jnp.where(
            first,
            jnp.concatenate([w_gate[0], other_gate[0]], axis=1),
            jnp.concatenate([other_gate[0], w_gate[0]], axis=1),
        )
        up_full = jnp.where(
            first,
            jnp.concatenate([w_up[0], other_up[0]], axis=1),
            jnp.concatenate([other_up[0], w_up[0]], axis=1),
        )
        down_full = jnp.where(
            first,
            jnp.concatenate([w_down[0], other_down[0]], axis=0),
            jnp.concatenate([other_down[0], w_down[0]], axis=0),
        )
        return (gate_full, up_full, down_full)

    shard_blocks, slice_rows, kv_width = keys.shape
    pick_count = selected.shape[1]
    block_rows = slice_rows * n_eg
    my_eg = lax.axis_index("eg")
    both = jnp.concatenate([keys, values], axis=2)
    gathered = lax.all_gather(both[None], ("ctx", "eg"), axis=0, tiled=True)
    tok_dev = residual.shape[0]
    top_count = expert_ids.shape[1]
    slot_count = n_ctx * n_eg
    pair_count = tok_dev * top_count
    per_slot = pair_count // slot_count
    home_slot = jnp.take(expert_home, expert_ids.reshape(-1), axis=0)
    indicator = (home_slot[:, None] == jnp.arange(slot_count, dtype=jnp.int32)[None, :]).astype(
        jnp.int32
    )
    rank_in_slot = jnp.sum((jnp.cumsum(indicator, axis=0) - 1) * indicator, axis=1)
    position = home_slot * per_slot + rank_in_slot
    source_pair = (
        jnp.zeros((pair_count,), jnp.int32)
        .at[position]
        .set(jnp.arange(pair_count, dtype=jnp.int32))
    )
    (source_pair, position), gathered = lax.optimization_barrier(
        ((source_pair, position), gathered)
    )
    every_block = (
        gathered.reshape(n_ctx, n_eg, shard_blocks, slice_rows, 2 * kv_width)
        .transpose(0, 2, 1, 3, 4)
        .reshape(n_ctx * shard_blocks, block_rows, 2 * kv_width)
    )
    query_rows = queries.shape[0]
    my_block = (my_ctx * n_eg + my_eg) * query_rows // block_rows
    chosen_blocks = jnp.concatenate(
        [my_block[None].astype(jnp.int32), jnp.take(selected, my_block, axis=0)]
    )
    context = jnp.take(every_block, chosen_blocks, axis=0)
    context_keys = context[:, :, :kv_width]
    context_values = context[:, :, kv_width:]
    span = (1 + pick_count) * block_rows
    kv_heads = kv_width // HD
    attended = attend_rows(
        queries,
        context_keys.reshape(span, kv_heads, HD),
        context_values.reshape(span, kv_heads, HD),
    )
    tok_dev = residual.shape[0]
    pieces = {0: out_weight}
    for bit in reversed(range(n_eg.bit_length() - 1)):
        stride = 2**bit
        held = sorted(pieces)
        if len(held) > 1:
            barrier_out = lax.optimization_barrier((tuple(pieces[m] for m in held), attended))
            pieces = dict(zip(held, barrier_out[0]))
            attended = barrier_out[1]
        fetched = swapped(tuple(pieces[m] for m in held), "eg", bit)
        for m, piece in zip(held, fetched):
            pieces[m + stride] = piece
    weight_cols = jnp.concatenate([pieces[m] for m in range(n_eg)], axis=1)
    out_by_piece = jnp.dot(attended, weight_cols, preferred_element_type=jnp.float32).reshape(
        query_rows, n_eg, -1
    )
    piece_of_col = jnp.arange(n_eg, dtype=jnp.int32) ^ my_eg
    partial_out = jnp.take(out_by_piece, piece_of_col, axis=1).reshape(query_rows, -1)
    attn_out = lax.psum_scatter(
        partial_out.astype(jnp.bfloat16), "rep", scatter_dimension=0, tiled=True
    )
    stream = residual.astype(jnp.float32) + attn_out.astype(jnp.float32)
    meansq = jnp.mean(stream * stream, axis=1, keepdims=True)
    normed = (stream * lax.rsqrt(meansq + 1e-06) * norm_gain).astype(jnp.bfloat16)
    partner = fetch_panels()
    if slot_count < 0:
        my_slot = my_ctx * n_eg + my_eg
        width = normed.shape[1]
        id_cols = jnp.full((tok_dev, 128), -1.0, jnp.bfloat16)
        id_cols = id_cols.at[:, :top_count].set(expert_ids.astype(jnp.bfloat16))
        packed = jnp.concatenate([normed, id_cols], axis=1)
        all_packed = lax.all_gather(packed, ("ctx", "eg"), axis=0, tiled=True)
        all_normed = all_packed[:, :width]
        all_ids = all_packed[:, width : width + top_count].astype(jnp.int32)
        expert_count = expert_home.shape[0]
        my_expert = jnp.sum(
            jnp.where(expert_home == my_slot, jnp.arange(expert_count, dtype=jnp.int32), 0)
        )
        hits = jnp.any(all_ids == my_expert, axis=1)
        hits = hits.reshape(slot_count, tok_dev).astype(jnp.int32)
        rank = jnp.cumsum(hits, axis=1) - 1
        chosen = jnp.logical_and(
            hits[:, None, :] == 1,
            rank[:, None, :] == jnp.arange(per_slot, dtype=jnp.int32)[None, :, None],
        )
        local_row = jnp.sum(
            chosen.astype(jnp.int32) * jnp.arange(tok_dev, dtype=jnp.int32)[None, None, :], axis=2
        )
        src_rows = local_row + jnp.arange(slot_count, dtype=jnp.int32)[:, None] * tok_dev
        pad_rows = ((0, all_packed.shape[1] - width), (0, 0))
        gate_act = jnp.dot(
            all_packed, jnp.pad(partner[0], pad_rows), preferred_element_type=jnp.float32
        )
        up_act = jnp.dot(
            all_packed, jnp.pad(partner[1], pad_rows), preferred_element_type=jnp.float32
        )
        activation = (jax.nn.silu(gate_act) * up_act).astype(jnp.bfloat16)
        picked = jnp.take(activation, src_rows.reshape(-1), axis=0)
        produced = jnp.dot(picked, partner[2], preferred_element_type=jnp.float32).astype(
            jnp.bfloat16
        )
    else:
        outbound = jnp.take(normed, source_pair // top_count, axis=0).reshape(
            slot_count, per_slot, -1
        )
        arrived = lax.all_to_all(outbound, ("ctx", "eg"), split_axis=0, concat_axis=0, tiled=True)
        flat_rows = arrived.reshape(-1, arrived.shape[2])
        produced = expert_apply(flat_rows, partner[0], partner[1], partner[2])
    returned = lax.all_to_all(
        produced.reshape(slot_count, per_slot, -1),
        ("ctx", "eg"),
        split_axis=0,
        concat_axis=0,
        tiled=True,
    )
    returned_rows = returned.reshape(pair_count, -1)
    placed = position.reshape(tok_dev, top_count)[:, :, None] == jnp.arange(
        pair_count, dtype=jnp.int32
    )[None, None, :]
    mixing = jnp.sum(jnp.where(placed, gate_weights[:, :, None], 0.0), axis=1)
    combined = jnp.zeros((tok_dev, returned_rows.shape[1]), jnp.float32)
    remainder = mixing
    for _ in range(3):
        part = remainder.astype(jnp.bfloat16)
        remainder = remainder - part.astype(jnp.float32)
        combined = combined + jnp.dot(part, returned_rows, preferred_element_type=jnp.float32)
    moe_out = combined.astype(jnp.bfloat16)
    return (attn_out, moe_out)


def solution(mesh):
    return jax.shard_map(
        local,
        mesh=mesh,
        in_specs=(
            P(("groups", "ctx", "eg"), "rep"),
            P(("groups", "ctx"), "eg", "rep"),
            P(("groups", "ctx"), "eg", "rep"),
            P("groups", None),
            P("rep", "eg"),
            P(("groups", "ctx", "eg", "rep"), None),
            P(),
            P(("groups", "ctx", "eg", "rep"), None),
            P(("groups", "ctx", "eg", "rep"), None),
            P(),
            P(("ctx", "eg"), None, "rep"),
            P(("ctx", "eg"), None, "rep"),
            P(("ctx", "eg"), "rep", None),
        ),
        out_specs=(
            P(("groups", "ctx", "eg", "rep"), None),
            P(("groups", "ctx", "eg", "rep"), None),
        ),
        check_vma=False,
    )
```

```python
import math

import jax
import jax.numpy as jnp
from jax import lax
from jax.sharding import PartitionSpec as P

HD = 128


def swapped(value, axis, bit):
    mask = 2**bit
    pairs = [(source, source ^ mask) for source in range(lax.axis_size(axis))]
    return lax.ppermute(value, axis, pairs)


def attend_rows(queries_flat, key_rows, value_rows):
    row_count = queries_flat.shape[0]
    kv_heads = key_rows.shape[1]
    per_group = queries_flat.shape[1] // (kv_heads * HD)
    inverse_root = 1.0 / math.sqrt(HD)
    arranged = queries_flat.reshape(row_count, kv_heads, per_group, HD).transpose(1, 2, 0, 3)
    logits = (
        jnp.einsum("kgrd,nkd->kgrn", arranged, key_rows, preferred_element_type=jnp.float32)
        * inverse_root
    )
    largest = jnp.max(logits, axis=-1, keepdims=True)
    raised = jnp.exp(logits - largest)
    denominator = jnp.sum(raised, axis=-1, keepdims=True)
    weights_low = (raised / denominator).astype(jnp.bfloat16)
    blended = jnp.einsum(
        "kgrn,nkd->rkgd", weights_low, value_rows, preferred_element_type=jnp.float32
    )
    return blended.astype(jnp.bfloat16).reshape(row_count, kv_heads * per_group * HD)


def expert_apply(rows_in, gate_full, up_full, down_full):
    gate_act = jnp.dot(rows_in, gate_full, preferred_element_type=jnp.float32)
    up_act = jnp.dot(rows_in, up_full, preferred_element_type=jnp.float32)
    activation = (jax.nn.silu(gate_act) * up_act).astype(jnp.bfloat16)
    return jnp.dot(activation, down_full, preferred_element_type=jnp.float32).astype(jnp.bfloat16)


def local(
    queries,
    keys,
    values,
    selected,
    out_weight,
    residual,
    norm_gain,
    expert_ids,
    gate_weights,
    expert_home,
    w_gate,
    w_up,
    w_down,
):
    n_ctx = lax.axis_size("ctx")
    n_eg = lax.axis_size("eg")
    n_rep = lax.axis_size("rep")
    my_ctx = lax.axis_index("ctx")

    def fetch_panels():
        if n_rep == 1:
            return (w_gate[0], w_up[0], w_down[0])
        other_gate, other_up, other_down = swapped((w_gate, w_up, w_down), "rep", 0)
        first = lax.axis_index("rep") == 0
        gate_full = jnp.where(
            first,
            jnp.concatenate([w_gate[0], other_gate[0]], axis=1),
            jnp.concatenate([other_gate[0], w_gate[0]], axis=1),
        )
        up_full = jnp.where(
            first,
            jnp.concatenate([w_up[0], other_up[0]], axis=1),
            jnp.concatenate([other_up[0], w_up[0]], axis=1),
        )
        down_full = jnp.where(
            first,
            jnp.concatenate([w_down[0], other_down[0]], axis=0),
            jnp.concatenate([other_down[0], w_down[0]], axis=0),
        )
        return (gate_full, up_full, down_full)

    shard_blocks, slice_rows, kv_width = keys.shape
    pick_count = selected.shape[1]
    block_rows = slice_rows * n_eg
    my_eg = lax.axis_index("eg")
    both = jnp.concatenate([keys, values], axis=2)
    gathered = lax.all_gather(both[None], ("ctx", "eg"), axis=0, tiled=True)
    every_block = (
        gathered.reshape(n_ctx, n_eg, shard_blocks, slice_rows, 2 * kv_width)
        .transpose(0, 2, 1, 3, 4)
        .reshape(n_ctx * shard_blocks, block_rows, 2 * kv_width)
    )
    query_rows = queries.shape[0]
    my_block = (my_ctx * n_eg + my_eg) * query_rows // block_rows
    chosen_blocks = jnp.concatenate(
        [my_block[None].astype(jnp.int32), jnp.take(selected, my_block, axis=0)]
    )
    context = jnp.take(every_block, chosen_blocks, axis=0)
    context_keys = context[:, :, :kv_width]
    context_values = context[:, :, kv_width:]
    span = (1 + pick_count) * block_rows
    kv_heads = kv_width // HD
    attended = attend_rows(
        queries,
        context_keys.reshape(span, kv_heads, HD),
        context_values.reshape(span, kv_heads, HD),
    )
    tok_dev = residual.shape[0]
    pieces = {0: out_weight}
    for bit in reversed(range(n_eg.bit_length() - 1)):
        stride = 2**bit
        held = sorted(pieces)
        if len(held) > 1:
            barrier_out = lax.optimization_barrier((tuple(pieces[m] for m in held), attended))
            pieces = dict(zip(held, barrier_out[0]))
            attended = barrier_out[1]
        fetched = swapped(tuple(pieces[m] for m in held), "eg", bit)
        for m, piece in zip(held, fetched):
            pieces[m + stride] = piece
    weight_cols = jnp.concatenate([pieces[m] for m in range(n_eg)], axis=1)
    out_by_piece = jnp.dot(attended, weight_cols, preferred_element_type=jnp.float32).reshape(
        query_rows, n_eg, -1
    )
    piece_of_col = jnp.arange(n_eg, dtype=jnp.int32) ^ my_eg
    partial_out = jnp.take(out_by_piece, piece_of_col, axis=1).reshape(query_rows, -1)
    attn_out = lax.psum_scatter(
        partial_out.astype(jnp.bfloat16), "rep", scatter_dimension=0, tiled=True
    )
    stream = residual.astype(jnp.float32) + attn_out.astype(jnp.float32)
    meansq = jnp.mean(stream * stream, axis=1, keepdims=True)
    normed = (stream * lax.rsqrt(meansq + 1e-06) * norm_gain).astype(jnp.bfloat16)
    top_count = expert_ids.shape[1]
    slot_count = n_ctx * n_eg
    pair_count = tok_dev * top_count
    per_slot = pair_count // slot_count
    home_slot = jnp.take(expert_home, expert_ids.reshape(-1), axis=0)
    indicator = (home_slot[:, None] == jnp.arange(slot_count, dtype=jnp.int32)[None, :]).astype(
        jnp.int32
    )
    rank_in_slot = jnp.sum((jnp.cumsum(indicator, axis=0) - 1) * indicator, axis=1)
    position = home_slot * per_slot + rank_in_slot
    source_pair = (
        jnp.zeros((pair_count,), jnp.int32)
        .at[position]
        .set(jnp.arange(pair_count, dtype=jnp.int32))
    )
    partner = fetch_panels()
    if slot_count <= 4 * top_count:
        my_slot = my_ctx * n_eg + my_eg
        width = normed.shape[1]
        id_cols = jnp.full((tok_dev, 128), -1.0, jnp.bfloat16)
        id_cols = id_cols.at[:, :top_count].set(expert_ids.astype(jnp.bfloat16))
        packed = jnp.concatenate([normed, id_cols], axis=1)
        all_packed = lax.all_gather(packed, ("ctx", "eg"), axis=0, tiled=True)
        all_normed = all_packed[:, :width]
        all_ids = all_packed[:, width : width + top_count].astype(jnp.int32)
        expert_count = expert_home.shape[0]
        my_expert = jnp.sum(
            jnp.where(expert_home == my_slot, jnp.arange(expert_count, dtype=jnp.int32), 0)
        )
        hits = jnp.any(all_ids == my_expert, axis=1)
        hits = hits.reshape(slot_count, tok_dev).astype(jnp.int32)
        rank = jnp.cumsum(hits, axis=1) - 1
        chosen = jnp.logical_and(
            hits[:, None, :] == 1,
            rank[:, None, :] == jnp.arange(per_slot, dtype=jnp.int32)[None, :, None],
        )
        local_row = jnp.sum(
            chosen.astype(jnp.int32) * jnp.arange(tok_dev, dtype=jnp.int32)[None, None, :], axis=2
        )
        src_rows = local_row + jnp.arange(slot_count, dtype=jnp.int32)[:, None] * tok_dev
        pad_rows = ((0, all_packed.shape[1] - width), (0, 0))
        hidden = partner[0].shape[1]
        gate_up = jnp.pad(jnp.concatenate([partner[0], partner[1]], axis=1), pad_rows)
        both_act = jnp.dot(all_packed, gate_up, preferred_element_type=jnp.float32)
        gate_act = both_act[:, :hidden]
        up_act = both_act[:, hidden:]
        activation = (jax.nn.silu(gate_act) * up_act).astype(jnp.bfloat16)
        pick_matrix = (
            src_rows.reshape(-1)[:, None]
            == jnp.arange(activation.shape[0], dtype=jnp.int32)[None, :]
        ).astype(jnp.bfloat16)
        picked = jnp.dot(pick_matrix, activation, preferred_element_type=jnp.float32).astype(
            jnp.bfloat16
        )
        produced = jnp.dot(picked, partner[2], preferred_element_type=jnp.float32).astype(
            jnp.bfloat16
        )
    else:
        outbound = jnp.take(normed, source_pair // top_count, axis=0).reshape(
            slot_count, per_slot, -1
        )
        arrived = lax.all_to_all(outbound, ("ctx", "eg"), split_axis=0, concat_axis=0, tiled=True)
        flat_rows = arrived.reshape(-1, arrived.shape[2])
        produced = expert_apply(flat_rows, partner[0], partner[1], partner[2])
    returned = lax.all_to_all(
        produced.reshape(slot_count, per_slot, -1),
        ("ctx", "eg"),
        split_axis=0,
        concat_axis=0,
        tiled=True,
    )
    returned_rows = returned.reshape(pair_count, -1)
    placed = position.reshape(tok_dev, top_count)[:, :, None] == jnp.arange(
        pair_count, dtype=jnp.int32
    )[None, None, :]
    mixing = jnp.sum(jnp.where(placed, gate_weights[:, :, None], 0.0), axis=1)
    combined = jnp.zeros((tok_dev, returned_rows.shape[1]), jnp.float32)
    remainder = mixing
    for _ in range(3):
        part = remainder.astype(jnp.bfloat16)
        remainder = remainder - part.astype(jnp.float32)
        combined = combined + jnp.dot(part, returned_rows, preferred_element_type=jnp.float32)
    moe_out = combined.astype(jnp.bfloat16)
    return (attn_out, moe_out)


def solution(mesh):
    return jax.shard_map(
        local,
        mesh=mesh,
        in_specs=(
            P(("groups", "ctx", "eg"), "rep"),
            P(("groups", "ctx"), "eg", "rep"),
            P(("groups", "ctx"), "eg", "rep"),
            P("groups", None),
            P("rep", "eg"),
            P(("groups", "ctx", "eg", "rep"), None),
            P(),
            P(("groups", "ctx", "eg", "rep"), None),
            P(("groups", "ctx", "eg", "rep"), None),
            P(),
            P(("ctx", "eg"), None, "rep"),
            P(("ctx", "eg"), None, "rep"),
            P(("ctx", "eg"), "rep", None),
        ),
        out_specs=(
            P(("groups", "ctx", "eg", "rep"), None),
            P(("groups", "ctx", "eg", "rep"), None),
        ),
        check_vma=False,
    )
```

```python
import math

import jax
import jax.numpy as jnp
from jax import lax
from jax.experimental import pallas as pl
from jax.sharding import PartitionSpec as P

HD = 128


def swapped(value, axis, bit):
    mask = 2**bit
    pairs = [(source, source ^ mask) for source in range(lax.axis_size(axis))]
    return lax.ppermute(value, axis, pairs)


def attention_kernel(query_ref, key_ref, value_ref, out_ref):
    inverse_root = 1.0 / math.sqrt(HD)
    key_block = key_ref[...]
    value_block = value_ref[...]
    for head in range(query_ref.shape[1] // HD):
        query_head = query_ref[:, head * HD : (head + 1) * HD]
        logits = (
            lax.dot_general(
                query_head,
                key_block,
                (((1,), (1,)), ((), ())),
                preferred_element_type=jnp.float32,
            )
            * inverse_root
        )
        largest = jnp.max(logits, axis=-1, keepdims=True)
        raised = jnp.exp(logits - largest)
        denominator = jnp.sum(raised, axis=-1, keepdims=True)
        weights_low = (raised / denominator).astype(jnp.bfloat16)
        blended = jnp.dot(weights_low, value_block, preferred_element_type=jnp.float32)
        out_ref[:, head * HD : (head + 1) * HD] = blended.astype(out_ref.dtype)


def attend_rows(queries_flat, key_rows, value_rows, interpret=False):
    row_count = queries_flat.shape[0]
    span, kv_heads, _ = key_rows.shape
    group_width = queries_flat.shape[1] // kv_heads
    return pl.pallas_call(
        attention_kernel,
        grid=(kv_heads,),
        in_specs=[
            pl.BlockSpec((row_count, group_width), lambda k: (0, k)),
            pl.BlockSpec((span, HD), lambda k: (0, k)),
            pl.BlockSpec((span, HD), lambda k: (0, k)),
        ],
        out_specs=pl.BlockSpec((row_count, group_width), lambda k: (0, k)),
        out_shape=jax.ShapeDtypeStruct(queries_flat.shape, jnp.bfloat16),
        interpret=interpret,
    )(queries_flat, key_rows.reshape(span, -1), value_rows.reshape(span, -1))


def expert_apply(rows_in, gate_full, up_full, down_full):
    gate_act = jnp.dot(rows_in, gate_full, preferred_element_type=jnp.float32)
    up_act = jnp.dot(rows_in, up_full, preferred_element_type=jnp.float32)
    activation = (jax.nn.silu(gate_act) * up_act).astype(jnp.bfloat16)
    return jnp.dot(activation, down_full, preferred_element_type=jnp.float32).astype(jnp.bfloat16)


def local(
    queries,
    keys,
    values,
    selected,
    out_weight,
    residual,
    norm_gain,
    expert_ids,
    gate_weights,
    expert_home,
    w_gate,
    w_up,
    w_down,
):
    n_ctx = lax.axis_size("ctx")
    n_eg = lax.axis_size("eg")
    n_rep = lax.axis_size("rep")
    my_ctx = lax.axis_index("ctx")

    def fetch_panels():
        if n_rep == 1:
            return (w_gate[0], w_up[0], w_down[0])
        other_gate, other_up, other_down = swapped((w_gate, w_up, w_down), "rep", 0)
        first = lax.axis_index("rep") == 0
        gate_full = jnp.where(
            first,
            jnp.concatenate([w_gate[0], other_gate[0]], axis=1),
            jnp.concatenate([other_gate[0], w_gate[0]], axis=1),
        )
        up_full = jnp.where(
            first,
            jnp.concatenate([w_up[0], other_up[0]], axis=1),
            jnp.concatenate([other_up[0], w_up[0]], axis=1),
        )
        down_full = jnp.where(
            first,
            jnp.concatenate([w_down[0], other_down[0]], axis=0),
            jnp.concatenate([other_down[0], w_down[0]], axis=0),
        )
        return (gate_full, up_full, down_full)

    shard_blocks, slice_rows, kv_width = keys.shape
    pick_count = selected.shape[1]
    block_rows = slice_rows * n_eg
    my_eg = lax.axis_index("eg")
    both = jnp.concatenate([keys, values], axis=2)
    gathered = lax.all_gather(both[None], ("ctx", "eg"), axis=0, tiled=True)
    every_block = (
        gathered.reshape(n_ctx, n_eg, shard_blocks, slice_rows, 2 * kv_width)
        .transpose(0, 2, 1, 3, 4)
        .reshape(n_ctx * shard_blocks, block_rows, 2 * kv_width)
    )
    query_rows = queries.shape[0]
    my_block = (my_ctx * n_eg + my_eg) * query_rows // block_rows
    chosen_blocks = jnp.concatenate(
        [my_block[None].astype(jnp.int32), jnp.take(selected, my_block, axis=0)]
    )
    context = jnp.take(every_block, chosen_blocks, axis=0)
    context_keys = context[:, :, :kv_width]
    context_values = context[:, :, kv_width:]
    span = (1 + pick_count) * block_rows
    kv_heads = kv_width // HD
    attended = attend_rows(
        queries,
        context_keys.reshape(span, kv_heads, HD),
        context_values.reshape(span, kv_heads, HD),
    )
    tok_dev = residual.shape[0]
    pieces = {0: out_weight}
    for bit in reversed(range(n_eg.bit_length() - 1)):
        stride = 2**bit
        held = sorted(pieces)
        if len(held) > 1:
            barrier_out = lax.optimization_barrier((tuple(pieces[m] for m in held), attended))
            pieces = dict(zip(held, barrier_out[0]))
            attended = barrier_out[1]
        fetched = swapped(tuple(pieces[m] for m in held), "eg", bit)
        for m, piece in zip(held, fetched):
            pieces[m + stride] = piece
    weight_cols = jnp.concatenate([pieces[m] for m in range(n_eg)], axis=1)
    out_by_piece = jnp.dot(attended, weight_cols, preferred_element_type=jnp.float32).reshape(
        query_rows, n_eg, -1
    )
    piece_of_col = jnp.arange(n_eg, dtype=jnp.int32) ^ my_eg
    partial_out = jnp.take(out_by_piece, piece_of_col, axis=1).reshape(query_rows, -1)
    attn_out = lax.psum_scatter(
        partial_out.astype(jnp.bfloat16), "rep", scatter_dimension=0, tiled=True
    )
    stream = residual.astype(jnp.float32) + attn_out.astype(jnp.float32)
    meansq = jnp.mean(stream * stream, axis=1, keepdims=True)
    normed = (stream * lax.rsqrt(meansq + 1e-06) * norm_gain).astype(jnp.bfloat16)
    top_count = expert_ids.shape[1]
    slot_count = n_ctx * n_eg
    pair_count = tok_dev * top_count
    per_slot = pair_count // slot_count
    home_slot = jnp.take(expert_home, expert_ids.reshape(-1), axis=0)
    indicator = (home_slot[:, None] == jnp.arange(slot_count, dtype=jnp.int32)[None, :]).astype(
        jnp.int32
    )
    rank_in_slot = jnp.sum((jnp.cumsum(indicator, axis=0) - 1) * indicator, axis=1)
    position = home_slot * per_slot + rank_in_slot
    source_pair = (
        jnp.zeros((pair_count,), jnp.int32)
        .at[position]
        .set(jnp.arange(pair_count, dtype=jnp.int32))
    )
    partner = fetch_panels()
    if slot_count <= 4 * top_count:
        my_slot = my_ctx * n_eg + my_eg
        width = normed.shape[1]
        id_cols = jnp.full((tok_dev, 128), -1.0, jnp.bfloat16)
        id_cols = id_cols.at[:, :top_count].set(expert_ids.astype(jnp.bfloat16))
        packed = jnp.concatenate([normed, id_cols], axis=1)
        all_packed = lax.all_gather(packed, ("ctx", "eg"), axis=0, tiled=True)
        all_normed = all_packed[:, :width]
        all_ids = all_packed[:, width : width + top_count].astype(jnp.int32)
        expert_count = expert_home.shape[0]
        my_expert = jnp.sum(
            jnp.where(expert_home == my_slot, jnp.arange(expert_count, dtype=jnp.int32), 0)
        )
        hits = jnp.any(all_ids == my_expert, axis=1)
        hits = hits.reshape(slot_count, tok_dev).astype(jnp.int32)
        rank = jnp.cumsum(hits, axis=1) - 1
        chosen = jnp.logical_and(
            hits[:, None, :] == 1,
            rank[:, None, :] == jnp.arange(per_slot, dtype=jnp.int32)[None, :, None],
        )
        local_row = jnp.sum(
            chosen.astype(jnp.int32) * jnp.arange(tok_dev, dtype=jnp.int32)[None, None, :], axis=2
        )
        src_rows = local_row + jnp.arange(slot_count, dtype=jnp.int32)[:, None] * tok_dev
        pad_rows = ((0, all_packed.shape[1] - width), (0, 0))
        hidden = partner[0].shape[1]
        gate_up = jnp.pad(jnp.concatenate([partner[0], partner[1]], axis=1), pad_rows)
        both_act = jnp.dot(all_packed, gate_up, preferred_element_type=jnp.float32)
        gate_act = both_act[:, :hidden]
        up_act = both_act[:, hidden:]
        activation = (jax.nn.silu(gate_act) * up_act).astype(jnp.bfloat16)
        pick_matrix = (
            src_rows.reshape(-1)[:, None]
            == jnp.arange(activation.shape[0], dtype=jnp.int32)[None, :]
        ).astype(jnp.bfloat16)
        picked = jnp.dot(pick_matrix, activation, preferred_element_type=jnp.float32).astype(
            jnp.bfloat16
        )
        produced = jnp.dot(picked, partner[2], preferred_element_type=jnp.float32).astype(
            jnp.bfloat16
        )
    else:
        outbound = jnp.take(normed, source_pair // top_count, axis=0).reshape(
            slot_count, per_slot, -1
        )
        arrived = lax.all_to_all(outbound, ("ctx", "eg"), split_axis=0, concat_axis=0, tiled=True)
        flat_rows = arrived.reshape(-1, arrived.shape[2])
        produced = expert_apply(flat_rows, partner[0], partner[1], partner[2])
    returned = lax.all_to_all(
        produced.reshape(slot_count, per_slot, -1),
        ("ctx", "eg"),
        split_axis=0,
        concat_axis=0,
        tiled=True,
    )
    returned_rows = returned.reshape(pair_count, -1)
    placed = position.reshape(tok_dev, top_count)[:, :, None] == jnp.arange(
        pair_count, dtype=jnp.int32
    )[None, None, :]
    mixing = jnp.sum(jnp.where(placed, gate_weights[:, :, None], 0.0), axis=1)
    combined = jnp.zeros((tok_dev, returned_rows.shape[1]), jnp.float32)
    remainder = mixing
    for _ in range(3):
        part = remainder.astype(jnp.bfloat16)
        remainder = remainder - part.astype(jnp.float32)
        combined = combined + jnp.dot(part, returned_rows, preferred_element_type=jnp.float32)
    moe_out = combined.astype(jnp.bfloat16)
    return (attn_out, moe_out)


def solution(mesh):
    return jax.shard_map(
        local,
        mesh=mesh,
        in_specs=(
            P(("groups", "ctx", "eg"), "rep"),
            P(("groups", "ctx"), "eg", "rep"),
            P(("groups", "ctx"), "eg", "rep"),
            P("groups", None),
            P("rep", "eg"),
            P(("groups", "ctx", "eg", "rep"), None),
            P(),
            P(("groups", "ctx", "eg", "rep"), None),
            P(("groups", "ctx", "eg", "rep"), None),
            P(),
            P(("ctx", "eg"), None, "rep"),
            P(("ctx", "eg"), None, "rep"),
            P(("ctx", "eg"), "rep", None),
        ),
        out_specs=(
            P(("groups", "ctx", "eg", "rep"), None),
            P(("groups", "ctx", "eg", "rep"), None),
        ),
        check_vma=False,
    )
```

```python
import math

import jax
import jax.numpy as jnp
from jax import lax
from jax.experimental import pallas as pl
from jax.sharding import PartitionSpec as P

HD = 128


def swapped(value, axis, bit):
    mask = 2**bit
    pairs = [(source, source ^ mask) for source in range(lax.axis_size(axis))]
    return lax.ppermute(value, axis, pairs)


def attention_kernel(query_ref, key_ref, value_ref, out_ref):
    inverse_root = 1.0 / math.sqrt(HD)
    key_block = key_ref[...]
    value_block = value_ref[...]
    for head in range(query_ref.shape[1] // HD):
        query_head = query_ref[:, head * HD : (head + 1) * HD]
        logits = (
            jnp.dot(query_head, key_block, preferred_element_type=jnp.float32) * inverse_root
        )
        largest = jnp.max(logits, axis=-1, keepdims=True)
        raised = jnp.exp(logits - largest)
        denominator = jnp.sum(raised, axis=-1, keepdims=True)
        weights_low = (raised * (1.0 / denominator)).astype(jnp.bfloat16)
        blended = jnp.dot(weights_low, value_block, preferred_element_type=jnp.float32)
        out_ref[:, head * HD : (head + 1) * HD] = blended.astype(out_ref.dtype)


def attend_rows(queries_flat, key_rows, value_rows, interpret=False):
    row_count = queries_flat.shape[0]
    span, kv_heads, _ = key_rows.shape
    group_width = queries_flat.shape[1] // kv_heads
    return pl.pallas_call(
        attention_kernel,
        grid=(kv_heads,),
        in_specs=[
            pl.BlockSpec((row_count, group_width), lambda k: (0, k)),
            pl.BlockSpec((HD, span), lambda k: (k, 0)),
            pl.BlockSpec((span, HD), lambda k: (0, k)),
        ],
        out_specs=pl.BlockSpec((row_count, group_width), lambda k: (0, k)),
        out_shape=jax.ShapeDtypeStruct(queries_flat.shape, jnp.bfloat16),
        interpret=interpret,
    )(queries_flat, key_rows.reshape(span, -1).T, value_rows.reshape(span, -1))


def expert_apply(rows_in, gate_full, up_full, down_full):
    gate_act = jnp.dot(rows_in, gate_full, preferred_element_type=jnp.float32)
    up_act = jnp.dot(rows_in, up_full, preferred_element_type=jnp.float32)
    activation = (jax.nn.silu(gate_act) * up_act).astype(jnp.bfloat16)
    return jnp.dot(activation, down_full, preferred_element_type=jnp.float32).astype(jnp.bfloat16)


def local(
    queries,
    keys,
    values,
    selected,
    out_weight,
    residual,
    norm_gain,
    expert_ids,
    gate_weights,
    expert_home,
    w_gate,
    w_up,
    w_down,
):
    n_ctx = lax.axis_size("ctx")
    n_eg = lax.axis_size("eg")
    n_rep = lax.axis_size("rep")
    my_ctx = lax.axis_index("ctx")

    def fetch_panels():
        if n_rep == 1:
            return (w_gate[0], w_up[0], w_down[0])
        other_gate, other_up, other_down = swapped((w_gate, w_up, w_down), "rep", 0)
        first = lax.axis_index("rep") == 0
        gate_full = jnp.where(
            first,
            jnp.concatenate([w_gate[0], other_gate[0]], axis=1),
            jnp.concatenate([other_gate[0], w_gate[0]], axis=1),
        )
        up_full = jnp.where(
            first,
            jnp.concatenate([w_up[0], other_up[0]], axis=1),
            jnp.concatenate([other_up[0], w_up[0]], axis=1),
        )
        down_full = jnp.where(
            first,
            jnp.concatenate([w_down[0], other_down[0]], axis=0),
            jnp.concatenate([other_down[0], w_down[0]], axis=0),
        )
        return (gate_full, up_full, down_full)

    shard_blocks, slice_rows, kv_width = keys.shape
    pick_count = selected.shape[1]
    block_rows = slice_rows * n_eg
    my_eg = lax.axis_index("eg")
    both = jnp.concatenate([keys, values], axis=2)
    gathered = lax.all_gather(both[None], ("ctx", "eg"), axis=0, tiled=True)
    every_block = (
        gathered.reshape(n_ctx, n_eg, shard_blocks, slice_rows, 2 * kv_width)
        .transpose(0, 2, 1, 3, 4)
        .reshape(n_ctx * shard_blocks, block_rows, 2 * kv_width)
    )
    query_rows = queries.shape[0]
    my_block = (my_ctx * n_eg + my_eg) * query_rows // block_rows
    chosen_blocks = jnp.concatenate(
        [my_block[None].astype(jnp.int32), jnp.take(selected, my_block, axis=0)]
    )
    context = jnp.take(every_block, chosen_blocks, axis=0)
    context_keys = context[:, :, :kv_width]
    context_values = context[:, :, kv_width:]
    span = (1 + pick_count) * block_rows
    kv_heads = kv_width // HD
    attended = attend_rows(
        queries,
        context_keys.reshape(span, kv_heads, HD),
        context_values.reshape(span, kv_heads, HD),
    )
    tok_dev = residual.shape[0]
    pieces = {0: out_weight}
    for bit in reversed(range(n_eg.bit_length() - 1)):
        stride = 2**bit
        held = sorted(pieces)
        if len(held) > 1:
            barrier_out = lax.optimization_barrier((tuple(pieces[m] for m in held), attended))
            pieces = dict(zip(held, barrier_out[0]))
            attended = barrier_out[1]
        fetched = swapped(tuple(pieces[m] for m in held), "eg", bit)
        for m, piece in zip(held, fetched):
            pieces[m + stride] = piece
    weight_cols = jnp.concatenate([pieces[m] for m in range(n_eg)], axis=1)
    out_by_piece = jnp.dot(attended, weight_cols, preferred_element_type=jnp.float32).reshape(
        query_rows, n_eg, -1
    )
    piece_of_col = jnp.arange(n_eg, dtype=jnp.int32) ^ my_eg
    partial_out = jnp.take(out_by_piece, piece_of_col, axis=1).reshape(query_rows, -1)
    attn_out = lax.psum_scatter(
        partial_out.astype(jnp.bfloat16), "rep", scatter_dimension=0, tiled=True
    )
    stream = residual.astype(jnp.float32) + attn_out.astype(jnp.float32)
    meansq = jnp.mean(stream * stream, axis=1, keepdims=True)
    normed = (stream * lax.rsqrt(meansq + 1e-06) * norm_gain).astype(jnp.bfloat16)
    top_count = expert_ids.shape[1]
    slot_count = n_ctx * n_eg
    pair_count = tok_dev * top_count
    per_slot = pair_count // slot_count
    home_slot = jnp.take(expert_home, expert_ids.reshape(-1), axis=0)
    indicator = (home_slot[:, None] == jnp.arange(slot_count, dtype=jnp.int32)[None, :]).astype(
        jnp.int32
    )
    rank_in_slot = jnp.sum((jnp.cumsum(indicator, axis=0) - 1) * indicator, axis=1)
    position = home_slot * per_slot + rank_in_slot
    source_pair = (
        jnp.zeros((pair_count,), jnp.int32)
        .at[position]
        .set(jnp.arange(pair_count, dtype=jnp.int32))
    )
    partner = fetch_panels()
    if slot_count <= 4 * top_count:
        my_slot = my_ctx * n_eg + my_eg
        width = normed.shape[1]
        id_cols = jnp.full((tok_dev, 128), -1.0, jnp.bfloat16)
        id_cols = id_cols.at[:, :top_count].set(expert_ids.astype(jnp.bfloat16))
        packed = jnp.concatenate([normed, id_cols], axis=1)
        all_packed = lax.all_gather(packed, ("ctx", "eg"), axis=0, tiled=True)
        all_normed = all_packed[:, :width]
        all_ids = all_packed[:, width : width + top_count].astype(jnp.int32)
        expert_count = expert_home.shape[0]
        my_expert = jnp.sum(
            jnp.where(expert_home == my_slot, jnp.arange(expert_count, dtype=jnp.int32), 0)
        )
        hits = jnp.any(all_ids == my_expert, axis=1)
        hits = hits.reshape(slot_count, tok_dev).astype(jnp.int32)
        rank = jnp.cumsum(hits, axis=1) - 1
        chosen = jnp.logical_and(
            hits[:, None, :] == 1,
            rank[:, None, :] == jnp.arange(per_slot, dtype=jnp.int32)[None, :, None],
        )
        local_row = jnp.sum(
            chosen.astype(jnp.int32) * jnp.arange(tok_dev, dtype=jnp.int32)[None, None, :], axis=2
        )
        src_rows = local_row + jnp.arange(slot_count, dtype=jnp.int32)[:, None] * tok_dev
        pad_rows = ((0, all_packed.shape[1] - width), (0, 0))
        hidden = partner[0].shape[1]
        gate_up = jnp.pad(jnp.concatenate([partner[0], partner[1]], axis=1), pad_rows)
        both_act = jnp.dot(all_packed, gate_up, preferred_element_type=jnp.float32)
        gate_act = both_act[:, :hidden]
        up_act = both_act[:, hidden:]
        activation = (jax.nn.silu(gate_act) * up_act).astype(jnp.bfloat16)
        pick_matrix = (
            src_rows.reshape(-1)[:, None]
            == jnp.arange(activation.shape[0], dtype=jnp.int32)[None, :]
        ).astype(jnp.bfloat16)
        picked = jnp.dot(pick_matrix, activation, preferred_element_type=jnp.float32).astype(
            jnp.bfloat16
        )
        produced = jnp.dot(picked, partner[2], preferred_element_type=jnp.float32).astype(
            jnp.bfloat16
        )
    else:
        outbound = jnp.take(normed, source_pair // top_count, axis=0).reshape(
            slot_count, per_slot, -1
        )
        arrived = lax.all_to_all(outbound, ("ctx", "eg"), split_axis=0, concat_axis=0, tiled=True)
        flat_rows = arrived.reshape(-1, arrived.shape[2])
        produced = expert_apply(flat_rows, partner[0], partner[1], partner[2])
    returned = lax.all_to_all(
        produced.reshape(slot_count, per_slot, -1),
        ("ctx", "eg"),
        split_axis=0,
        concat_axis=0,
        tiled=True,
    )
    returned_rows = returned.reshape(pair_count, -1)
    placed = position.reshape(tok_dev, top_count)[:, :, None] == jnp.arange(
        pair_count, dtype=jnp.int32
    )[None, None, :]
    mixing = jnp.sum(jnp.where(placed, gate_weights[:, :, None], 0.0), axis=1)
    combined = jnp.zeros((tok_dev, returned_rows.shape[1]), jnp.float32)
    remainder = mixing
    for _ in range(3):
        part = remainder.astype(jnp.bfloat16)
        remainder = remainder - part.astype(jnp.float32)
        combined = combined + jnp.dot(part, returned_rows, preferred_element_type=jnp.float32)
    moe_out = combined.astype(jnp.bfloat16)
    return (attn_out, moe_out)


def solution(mesh):
    return jax.shard_map(
        local,
        mesh=mesh,
        in_specs=(
            P(("groups", "ctx", "eg"), "rep"),
            P(("groups", "ctx"), "eg", "rep"),
            P(("groups", "ctx"), "eg", "rep"),
            P("groups", None),
            P("rep", "eg"),
            P(("groups", "ctx", "eg", "rep"), None),
            P(),
            P(("groups", "ctx", "eg", "rep"), None),
            P(("groups", "ctx", "eg", "rep"), None),
            P(),
            P(("ctx", "eg"), None, "rep"),
            P(("ctx", "eg"), None, "rep"),
            P(("ctx", "eg"), "rep", None),
        ),
        out_specs=(
            P(("groups", "ctx", "eg", "rep"), None),
            P(("groups", "ctx", "eg", "rep"), None),
        ),
        check_vma=False,
    )
```

```python
import math

import jax
import jax.numpy as jnp
from jax import lax
from jax.experimental import pallas as pl
from jax.sharding import PartitionSpec as P

HD = 128


def swapped(value, axis, bit):
    mask = 2**bit
    pairs = [(source, source ^ mask) for source in range(lax.axis_size(axis))]
    return lax.ppermute(value, axis, pairs)


def attention_kernel(query_ref, key_ref, value_ref, out_ref):
    inverse_root = 1.0 / math.sqrt(HD)
    key_block = key_ref[...]
    value_block = value_ref[...]
    for head in range(query_ref.shape[1] // HD):
        query_head = query_ref[:, head * HD : (head + 1) * HD]
        logits = (
            lax.dot_general(
                query_head,
                key_block,
                (((1,), (1,)), ((), ())),
                preferred_element_type=jnp.float32,
            )
            * inverse_root
        )
        largest = jnp.max(logits, axis=-1, keepdims=True)
        raised = jnp.exp(logits - largest)
        denominator = jnp.sum(raised, axis=-1, keepdims=True)
        weights_low = (raised / denominator).astype(jnp.bfloat16)
        blended = jnp.dot(weights_low, value_block, preferred_element_type=jnp.float32)
        out_ref[:, head * HD : (head + 1) * HD] = blended.astype(out_ref.dtype)


def attend_rows(queries_flat, key_rows, value_rows, interpret=False):
    row_count = queries_flat.shape[0]
    span, kv_heads, _ = key_rows.shape
    group_width = queries_flat.shape[1] // kv_heads
    return pl.pallas_call(
        attention_kernel,
        grid=(kv_heads,),
        in_specs=[
            pl.BlockSpec((row_count, group_width), lambda k: (0, k)),
            pl.BlockSpec((span, HD), lambda k: (0, k)),
            pl.BlockSpec((span, HD), lambda k: (0, k)),
        ],
        out_specs=pl.BlockSpec((row_count, group_width), lambda k: (0, k)),
        out_shape=jax.ShapeDtypeStruct(queries_flat.shape, jnp.bfloat16),
        interpret=interpret,
    )(queries_flat, key_rows.reshape(span, -1), value_rows.reshape(span, -1))


def expert_apply(rows_in, gate_full, up_full, down_full):
    gate_act = jnp.dot(rows_in, gate_full, preferred_element_type=jnp.float32)
    up_act = jnp.dot(rows_in, up_full, preferred_element_type=jnp.float32)
    activation = (jax.nn.silu(gate_act) * up_act).astype(jnp.bfloat16)
    return jnp.dot(activation, down_full, preferred_element_type=jnp.float32).astype(jnp.bfloat16)


def local(
    queries,
    keys,
    values,
    selected,
    out_weight,
    residual,
    norm_gain,
    expert_ids,
    gate_weights,
    expert_home,
    w_gate,
    w_up,
    w_down,
):
    n_ctx = lax.axis_size("ctx")
    n_eg = lax.axis_size("eg")
    n_rep = lax.axis_size("rep")
    my_ctx = lax.axis_index("ctx")

    def fetch_panels():
        if n_rep == 1:
            return (w_gate[0], w_up[0], w_down[0])
        other_gate, other_up, other_down = swapped((w_gate, w_up, w_down), "rep", 0)
        first = lax.axis_index("rep") == 0
        gate_full = jnp.where(
            first,
            jnp.concatenate([w_gate[0], other_gate[0]], axis=1),
            jnp.concatenate([other_gate[0], w_gate[0]], axis=1),
        )
        up_full = jnp.where(
            first,
            jnp.concatenate([w_up[0], other_up[0]], axis=1),
            jnp.concatenate([other_up[0], w_up[0]], axis=1),
        )
        down_full = jnp.where(
            first,
            jnp.concatenate([w_down[0], other_down[0]], axis=0),
            jnp.concatenate([other_down[0], w_down[0]], axis=0),
        )
        return (gate_full, up_full, down_full)

    shard_blocks, slice_rows, kv_width = keys.shape
    pick_count = selected.shape[1]
    block_rows = slice_rows * n_eg
    my_eg = lax.axis_index("eg")
    both = jnp.concatenate([keys, values], axis=2)
    gathered = lax.all_gather(both[None], ("ctx", "eg"), axis=0, tiled=True)
    every_block = (
        gathered.reshape(n_ctx, n_eg, shard_blocks, slice_rows, 2 * kv_width)
        .transpose(0, 2, 1, 3, 4)
        .reshape(n_ctx * shard_blocks, block_rows, 2 * kv_width)
    )
    query_rows = queries.shape[0]
    my_block = (my_ctx * n_eg + my_eg) * query_rows // block_rows
    chosen_blocks = jnp.concatenate(
        [my_block[None].astype(jnp.int32), jnp.take(selected, my_block, axis=0)]
    )
    context = jnp.take(every_block, chosen_blocks, axis=0)
    context_keys = context[:, :, :kv_width]
    context_values = context[:, :, kv_width:]
    span = (1 + pick_count) * block_rows
    kv_heads = kv_width // HD
    attended = attend_rows(
        queries,
        context_keys.reshape(span, kv_heads, HD),
        context_values.reshape(span, kv_heads, HD),
    )
    tok_dev = residual.shape[0]
    pieces = {0: out_weight}
    for bit in reversed(range(n_eg.bit_length() - 1)):
        stride = 2**bit
        held = sorted(pieces)
        if len(held) > 1:
            barrier_out = lax.optimization_barrier((tuple(pieces[m] for m in held), attended))
            pieces = dict(zip(held, barrier_out[0]))
            attended = barrier_out[1]
        fetched = swapped(tuple(pieces[m] for m in held), "eg", bit)
        for m, piece in zip(held, fetched):
            pieces[m + stride] = piece
    weight_cols = jnp.concatenate([pieces[m] for m in range(n_eg)], axis=1)
    out_by_piece = jnp.dot(attended, weight_cols, preferred_element_type=jnp.float32).reshape(
        query_rows, n_eg, -1
    )
    piece_of_col = jnp.arange(n_eg, dtype=jnp.int32) ^ my_eg
    partial_out = jnp.take(out_by_piece, piece_of_col, axis=1).reshape(query_rows, -1)
    attn_out = lax.psum_scatter(
        partial_out.astype(jnp.bfloat16), "rep", scatter_dimension=0, tiled=True
    )
    stream = residual.astype(jnp.float32) + attn_out.astype(jnp.float32)
    meansq = jnp.mean(stream * stream, axis=1, keepdims=True)
    normed = (stream * lax.rsqrt(meansq + 1e-06) * norm_gain).astype(jnp.bfloat16)
    top_count = expert_ids.shape[1]
    slot_count = n_ctx * n_eg
    pair_count = tok_dev * top_count
    per_slot = pair_count // slot_count
    home_slot = jnp.take(expert_home, expert_ids.reshape(-1), axis=0)
    indicator = (home_slot[:, None] == jnp.arange(slot_count, dtype=jnp.int32)[None, :]).astype(
        jnp.int32
    )
    rank_in_slot = jnp.sum((jnp.cumsum(indicator, axis=0) - 1) * indicator, axis=1)
    position = home_slot * per_slot + rank_in_slot
    source_pair = (
        jnp.zeros((pair_count,), jnp.int32)
        .at[position]
        .set(jnp.arange(pair_count, dtype=jnp.int32))
    )
    partner = fetch_panels()
    if slot_count <= 4 * top_count:
        my_slot = my_ctx * n_eg + my_eg
        width = normed.shape[1]
        id_cols = jnp.full((tok_dev, 128), -1.0, jnp.bfloat16)
        id_cols = id_cols.at[:, :top_count].set(expert_ids.astype(jnp.bfloat16))
        packed = jnp.concatenate([normed, id_cols], axis=1)
        all_packed = lax.all_gather(packed, ("ctx", "eg"), axis=0, tiled=True)
        all_normed = all_packed[:, :width]
        all_ids = all_packed[:, width : width + top_count].astype(jnp.int32)
        expert_count = expert_home.shape[0]
        my_expert = jnp.sum(
            jnp.where(expert_home == my_slot, jnp.arange(expert_count, dtype=jnp.int32), 0)
        )
        hits = jnp.any(all_ids == my_expert, axis=1)
        hits = hits.reshape(slot_count, tok_dev).astype(jnp.int32)
        rank = jnp.cumsum(hits, axis=1) - 1
        chosen = jnp.logical_and(
            hits[:, None, :] == 1,
            rank[:, None, :] == jnp.arange(per_slot, dtype=jnp.int32)[None, :, None],
        )
        local_row = jnp.sum(
            chosen.astype(jnp.int32) * jnp.arange(tok_dev, dtype=jnp.int32)[None, None, :], axis=2
        )
        src_rows = local_row + jnp.arange(slot_count, dtype=jnp.int32)[:, None] * tok_dev
        pad_rows = ((0, all_packed.shape[1] - width), (0, 0))
        hidden = partner[0].shape[1]
        gate_up = jnp.pad(jnp.concatenate([partner[0], partner[1]], axis=1), pad_rows)
        both_act = jnp.dot(all_packed, gate_up, preferred_element_type=jnp.float32)
        gate_act = both_act[:, :hidden]
        up_act = both_act[:, hidden:]
        activation = (jax.nn.silu(gate_act) * up_act).astype(jnp.bfloat16)
        pick_matrix = (
            src_rows.reshape(-1)[:, None]
            == jnp.arange(activation.shape[0], dtype=jnp.int32)[None, :]
        ).astype(jnp.bfloat16)
        picked = jnp.dot(pick_matrix, activation, preferred_element_type=jnp.float32).astype(
            jnp.bfloat16
        )
        produced = jnp.dot(picked, partner[2], preferred_element_type=jnp.float32).astype(
            jnp.bfloat16
        )
    else:
        outbound = jnp.take(normed, source_pair // top_count, axis=0).reshape(
            slot_count, per_slot, -1
        )
        arrived = lax.all_to_all(outbound, ("ctx", "eg"), split_axis=0, concat_axis=0, tiled=True)
        flat_rows = arrived.reshape(-1, arrived.shape[2])
        produced = expert_apply(flat_rows, partner[0], partner[1], partner[2])
    returned = lax.all_to_all(
        produced.reshape(slot_count, per_slot, -1),
        ("ctx", "eg"),
        split_axis=0,
        concat_axis=0,
        tiled=True,
    )
    returned_rows = returned.reshape(pair_count, -1)
    placed = position.reshape(tok_dev, top_count)[:, :, None] == jnp.arange(
        pair_count, dtype=jnp.int32
    )[None, None, :]
    mixing = jnp.sum(jnp.where(placed, gate_weights[:, :, None], 0.0), axis=1)
    combined = jnp.zeros((tok_dev, returned_rows.shape[1]), jnp.float32)
    remainder = mixing
    for _ in range(2):
        part = remainder.astype(jnp.bfloat16)
        remainder = remainder - part.astype(jnp.float32)
        combined = combined + jnp.dot(part, returned_rows, preferred_element_type=jnp.float32)
    moe_out = combined.astype(jnp.bfloat16)
    return (attn_out, moe_out)


def solution(mesh):
    return jax.shard_map(
        local,
        mesh=mesh,
        in_specs=(
            P(("groups", "ctx", "eg"), "rep"),
            P(("groups", "ctx"), "eg", "rep"),
            P(("groups", "ctx"), "eg", "rep"),
            P("groups", None),
            P("rep", "eg"),
            P(("groups", "ctx", "eg", "rep"), None),
            P(),
            P(("groups", "ctx", "eg", "rep"), None),
            P(("groups", "ctx", "eg", "rep"), None),
            P(),
            P(("ctx", "eg"), None, "rep"),
            P(("ctx", "eg"), None, "rep"),
            P(("ctx", "eg"), "rep", None),
        ),
        out_specs=(
            P(("groups", "ctx", "eg", "rep"), None),
            P(("groups", "ctx", "eg", "rep"), None),
        ),
        check_vma=False,
    )
```

```python
import math

import jax
import jax.numpy as jnp
from jax import lax
from jax.experimental import pallas as pl
from jax.sharding import PartitionSpec as P

HD = 128


def swapped(value, axis, bit):
    mask = 2**bit
    pairs = [(source, source ^ mask) for source in range(lax.axis_size(axis))]
    return lax.ppermute(value, axis, pairs)


def attention_kernel(query_ref, key_ref, value_ref, out_ref):
    inverse_root = 1.0 / math.sqrt(HD)
    key_block = key_ref[...]
    value_block = value_ref[...]
    for head in range(query_ref.shape[1] // HD):
        query_head = query_ref[:, head * HD : (head + 1) * HD]
        logits = (
            lax.dot_general(
                query_head,
                key_block,
                (((1,), (1,)), ((), ())),
                preferred_element_type=jnp.float32,
            )
            * inverse_root
        )
        largest = jnp.max(logits, axis=-1, keepdims=True)
        raised = jnp.exp(logits - largest)
        denominator = jnp.sum(raised, axis=-1, keepdims=True)
        weights_low = (raised / denominator).astype(jnp.bfloat16)
        blended = jnp.dot(weights_low, value_block, preferred_element_type=jnp.float32)
        out_ref[:, head * HD : (head + 1) * HD] = blended.astype(out_ref.dtype)


def attend_rows(queries_flat, key_rows, value_rows, interpret=False):
    row_count = queries_flat.shape[0]
    span, kv_heads, _ = key_rows.shape
    group_width = queries_flat.shape[1] // kv_heads
    return pl.pallas_call(
        attention_kernel,
        grid=(kv_heads,),
        in_specs=[
            pl.BlockSpec((row_count, group_width), lambda k: (0, k)),
            pl.BlockSpec((span, HD), lambda k: (0, k)),
            pl.BlockSpec((span, HD), lambda k: (0, k)),
        ],
        out_specs=pl.BlockSpec((row_count, group_width), lambda k: (0, k)),
        out_shape=jax.ShapeDtypeStruct(queries_flat.shape, jnp.bfloat16),
        interpret=interpret,
    )(queries_flat, key_rows.reshape(span, -1), value_rows.reshape(span, -1))


def expert_apply(rows_in, gate_full, up_full, down_full):
    gate_act = jnp.dot(rows_in, gate_full, preferred_element_type=jnp.float32)
    up_act = jnp.dot(rows_in, up_full, preferred_element_type=jnp.float32)
    activation = (jax.nn.silu(gate_act) * up_act).astype(jnp.bfloat16)
    return jnp.dot(activation, down_full, preferred_element_type=jnp.float32).astype(jnp.bfloat16)


def local(
    queries,
    keys,
    values,
    selected,
    out_weight,
    residual,
    norm_gain,
    expert_ids,
    gate_weights,
    expert_home,
    w_gate,
    w_up,
    w_down,
):
    n_ctx = lax.axis_size("ctx")
    n_eg = lax.axis_size("eg")
    n_rep = lax.axis_size("rep")
    my_ctx = lax.axis_index("ctx")

    def fetch_panels():
        if n_rep == 1:
            return (w_gate[0], w_up[0], w_down[0])
        other_gate, other_up, other_down = swapped((w_gate, w_up, w_down), "rep", 0)
        first = lax.axis_index("rep") == 0
        gate_full = jnp.where(
            first,
            jnp.concatenate([w_gate[0], other_gate[0]], axis=1),
            jnp.concatenate([other_gate[0], w_gate[0]], axis=1),
        )
        up_full = jnp.where(
            first,
            jnp.concatenate([w_up[0], other_up[0]], axis=1),
            jnp.concatenate([other_up[0], w_up[0]], axis=1),
        )
        down_full = jnp.where(
            first,
            jnp.concatenate([w_down[0], other_down[0]], axis=0),
            jnp.concatenate([other_down[0], w_down[0]], axis=0),
        )
        return (gate_full, up_full, down_full)

    shard_blocks, slice_rows, kv_width = keys.shape
    pick_count = selected.shape[1]
    block_rows = slice_rows * n_eg
    my_eg = lax.axis_index("eg")
    both = jnp.concatenate([keys, values], axis=2)
    gathered = lax.all_gather(both[None], ("ctx", "eg"), axis=0, tiled=True)
    every_block = (
        gathered.reshape(n_ctx, n_eg, shard_blocks, slice_rows, 2 * kv_width)
        .transpose(0, 2, 1, 3, 4)
        .reshape(n_ctx * shard_blocks, block_rows, 2 * kv_width)
    )
    query_rows = queries.shape[0]
    my_block = (my_ctx * n_eg + my_eg) * query_rows // block_rows
    chosen_blocks = jnp.concatenate(
        [my_block[None].astype(jnp.int32), jnp.take(selected, my_block, axis=0)]
    )
    context = jnp.take(every_block, chosen_blocks, axis=0)
    context_keys = context[:, :, :kv_width]
    context_values = context[:, :, kv_width:]
    span = (1 + pick_count) * block_rows
    kv_heads = kv_width // HD
    attended = attend_rows(
        queries,
        context_keys.reshape(span, kv_heads, HD),
        context_values.reshape(span, kv_heads, HD),
    )
    tok_dev = residual.shape[0]
    pieces = {0: out_weight}
    for bit in reversed(range(n_eg.bit_length() - 1)):
        stride = 2**bit
        held = sorted(pieces)
        if len(held) > 1:
            barrier_out = lax.optimization_barrier((tuple(pieces[m] for m in held), attended))
            pieces = dict(zip(held, barrier_out[0]))
            attended = barrier_out[1]
        fetched = swapped(tuple(pieces[m] for m in held), "eg", bit)
        for m, piece in zip(held, fetched):
            pieces[m + stride] = piece
    weight_cols = jnp.concatenate([pieces[m] for m in range(n_eg)], axis=1)
    out_by_piece = jnp.dot(attended, weight_cols, preferred_element_type=jnp.float32).reshape(
        query_rows, n_eg, -1
    )
    piece_of_col = jnp.arange(n_eg, dtype=jnp.int32) ^ my_eg
    partial_out = jnp.take(out_by_piece, piece_of_col, axis=1).reshape(query_rows, -1)
    attn_out = lax.psum_scatter(
        partial_out.astype(jnp.bfloat16), "rep", scatter_dimension=0, tiled=True
    )
    stream = residual.astype(jnp.float32) + attn_out.astype(jnp.float32)
    meansq = jnp.mean(stream * stream, axis=1, keepdims=True)
    normed = (stream * lax.rsqrt(meansq + 1e-06) * norm_gain).astype(jnp.bfloat16)
    top_count = expert_ids.shape[1]
    slot_count = n_ctx * n_eg
    pair_count = tok_dev * top_count
    per_slot = pair_count // slot_count
    home_slot = jnp.take(expert_home, expert_ids.reshape(-1), axis=0)
    indicator = (home_slot[:, None] == jnp.arange(slot_count, dtype=jnp.int32)[None, :]).astype(
        jnp.int32
    )
    rank_in_slot = jnp.sum((jnp.cumsum(indicator, axis=0) - 1) * indicator, axis=1)
    position = home_slot * per_slot + rank_in_slot
    source_pair = (
        jnp.zeros((pair_count,), jnp.int32)
        .at[position]
        .set(jnp.arange(pair_count, dtype=jnp.int32))
    )
    partner = fetch_panels()
    if slot_count <= 4 * top_count:
        my_slot = my_ctx * n_eg + my_eg
        width = normed.shape[1]
        id_cols = jnp.full((tok_dev, 128), -1.0, jnp.bfloat16)
        id_cols = id_cols.at[:, :top_count].set(expert_ids.astype(jnp.bfloat16))
        packed = jnp.concatenate([normed, id_cols], axis=1)
        all_packed = lax.all_gather(packed, ("ctx", "eg"), axis=0, tiled=True)
        all_normed = all_packed[:, :width]
        all_ids = all_packed[:, width : width + top_count].astype(jnp.int32)
        expert_count = expert_home.shape[0]
        my_expert = jnp.sum(
            jnp.where(expert_home == my_slot, jnp.arange(expert_count, dtype=jnp.int32), 0)
        )
        hits = jnp.any(all_ids == my_expert, axis=1)
        hits = hits.reshape(slot_count, tok_dev).astype(jnp.int32)
        rank = jnp.cumsum(hits, axis=1) - 1
        chosen = jnp.logical_and(
            hits[:, None, :] == 1,
            rank[:, None, :] == jnp.arange(per_slot, dtype=jnp.int32)[None, :, None],
        )
        local_row = jnp.sum(
            chosen.astype(jnp.int32) * jnp.arange(tok_dev, dtype=jnp.int32)[None, None, :], axis=2
        )
        src_rows = local_row + jnp.arange(slot_count, dtype=jnp.int32)[:, None] * tok_dev
        pad_rows = ((0, all_packed.shape[1] - width), (0, 0))
        hidden = partner[0].shape[1]
        gate_up = jnp.pad(jnp.concatenate([partner[0], partner[1]], axis=1), pad_rows)
        both_act = jnp.dot(all_packed, gate_up, preferred_element_type=jnp.float32)
        gate_act = both_act[:, :hidden]
        up_act = both_act[:, hidden:]
        activation = (jax.nn.silu(gate_act) * up_act).astype(jnp.bfloat16)
        pick_matrix = (
            src_rows.reshape(-1)[:, None]
            == jnp.arange(activation.shape[0], dtype=jnp.int32)[None, :]
        ).astype(jnp.bfloat16)
        picked = jnp.dot(pick_matrix, activation, preferred_element_type=jnp.float32).astype(
            jnp.bfloat16
        )
        produced = jnp.dot(picked, partner[2], preferred_element_type=jnp.float32).astype(
            jnp.bfloat16
        )
    else:
        outbound = jnp.take(normed, source_pair // top_count, axis=0).reshape(
            slot_count, per_slot, -1
        )
        arrived = lax.all_to_all(outbound, ("ctx", "eg"), split_axis=0, concat_axis=0, tiled=True)
        flat_rows = arrived.reshape(-1, arrived.shape[2])
        produced = expert_apply(flat_rows, partner[0], partner[1], partner[2])
    returned = lax.all_to_all(
        produced.reshape(slot_count, per_slot, -1),
        ("ctx", "eg"),
        split_axis=0,
        concat_axis=0,
        tiled=True,
    )
    returned_rows = returned.reshape(pair_count, -1)
    placed = position.reshape(tok_dev, top_count)[:, :, None] == jnp.arange(
        pair_count, dtype=jnp.int32
    )[None, None, :]
    mixing = jnp.sum(jnp.where(placed, gate_weights[:, :, None], 0.0), axis=1)
    high_part = mixing.astype(jnp.bfloat16)
    low_part = (mixing - high_part.astype(jnp.float32)).astype(jnp.bfloat16)
    both_parts = jnp.concatenate([high_part, low_part], axis=0)
    stacked_out = jnp.dot(both_parts, returned_rows, preferred_element_type=jnp.float32)
    combined = stacked_out[:tok_dev] + stacked_out[tok_dev:]
    moe_out = combined.astype(jnp.bfloat16)
    return (attn_out, moe_out)


def solution(mesh):
    return jax.shard_map(
        local,
        mesh=mesh,
        in_specs=(
            P(("groups", "ctx", "eg"), "rep"),
            P(("groups", "ctx"), "eg", "rep"),
            P(("groups", "ctx"), "eg", "rep"),
            P("groups", None),
            P("rep", "eg"),
            P(("groups", "ctx", "eg", "rep"), None),
            P(),
            P(("groups", "ctx", "eg", "rep"), None),
            P(("groups", "ctx", "eg", "rep"), None),
            P(),
            P(("ctx", "eg"), None, "rep"),
            P(("ctx", "eg"), None, "rep"),
            P(("ctx", "eg"), "rep", None),
        ),
        out_specs=(
            P(("groups", "ctx", "eg", "rep"), None),
            P(("groups", "ctx", "eg", "rep"), None),
        ),
        check_vma=False,
    )
```

```python
import math

import jax
import jax.numpy as jnp
from jax import lax
from jax.experimental import pallas as pl
from jax.sharding import PartitionSpec as P

HD = 128


def swapped(value, axis, bit):
    mask = 2**bit
    pairs = [(source, source ^ mask) for source in range(lax.axis_size(axis))]
    return lax.ppermute(value, axis, pairs)


def attention_kernel(query_ref, key_ref, value_ref, out_ref):
    inverse_root = 1.0 / math.sqrt(HD)
    key_block = key_ref[...]
    value_block = value_ref[...]
    for head in range(query_ref.shape[1] // HD):
        query_head = query_ref[:, head * HD : (head + 1) * HD]
        logits = (
            lax.dot_general(
                query_head,
                key_block,
                (((1,), (1,)), ((), ())),
                preferred_element_type=jnp.float32,
            )
            * inverse_root
        )
        largest = jnp.max(logits, axis=-1, keepdims=True)
        raised = jnp.exp(logits - largest)
        denominator = jnp.sum(raised, axis=-1, keepdims=True)
        weights_low = (raised / denominator).astype(jnp.bfloat16)
        blended = jnp.dot(weights_low, value_block, preferred_element_type=jnp.float32)
        out_ref[:, head * HD : (head + 1) * HD] = blended.astype(out_ref.dtype)


def attend_rows(queries_flat, key_rows, value_rows, interpret=False):
    row_count = queries_flat.shape[0]
    span, kv_heads, _ = key_rows.shape
    group_width = queries_flat.shape[1] // kv_heads
    return pl.pallas_call(
        attention_kernel,
        grid=(kv_heads,),
        in_specs=[
            pl.BlockSpec((row_count, group_width), lambda k: (0, k)),
            pl.BlockSpec((span, HD), lambda k: (0, k)),
            pl.BlockSpec((span, HD), lambda k: (0, k)),
        ],
        out_specs=pl.BlockSpec((row_count, group_width), lambda k: (0, k)),
        out_shape=jax.ShapeDtypeStruct(queries_flat.shape, jnp.bfloat16),
        interpret=interpret,
    )(queries_flat, key_rows.reshape(span, -1), value_rows.reshape(span, -1))


def expert_apply(rows_in, gate_full, up_full, down_full):
    gate_act = jnp.dot(rows_in, gate_full, preferred_element_type=jnp.float32)
    up_act = jnp.dot(rows_in, up_full, preferred_element_type=jnp.float32)
    activation = (jax.nn.silu(gate_act) * up_act).astype(jnp.bfloat16)
    return jnp.dot(activation, down_full, preferred_element_type=jnp.float32).astype(jnp.bfloat16)


def local(
    queries,
    keys,
    values,
    selected,
    out_weight,
    residual,
    norm_gain,
    expert_ids,
    gate_weights,
    expert_home,
    w_gate,
    w_up,
    w_down,
):
    n_ctx = lax.axis_size("ctx")
    n_eg = lax.axis_size("eg")
    n_rep = lax.axis_size("rep")
    my_ctx = lax.axis_index("ctx")

    def fetch_panels():
        if n_rep == 1:
            return (w_gate[0], w_up[0], w_down[0])
        other_gate, other_up, other_down = swapped((w_gate, w_up, w_down), "rep", 0)
        first = lax.axis_index("rep") == 0
        gate_full = jnp.where(
            first,
            jnp.concatenate([w_gate[0], other_gate[0]], axis=1),
            jnp.concatenate([other_gate[0], w_gate[0]], axis=1),
        )
        up_full = jnp.where(
            first,
            jnp.concatenate([w_up[0], other_up[0]], axis=1),
            jnp.concatenate([other_up[0], w_up[0]], axis=1),
        )
        down_full = jnp.where(
            first,
            jnp.concatenate([w_down[0], other_down[0]], axis=0),
            jnp.concatenate([other_down[0], w_down[0]], axis=0),
        )
        return (gate_full, up_full, down_full)

    shard_blocks, slice_rows, kv_width = keys.shape
    pick_count = selected.shape[1]
    block_rows = slice_rows * n_eg
    my_eg = lax.axis_index("eg")
    both = jnp.concatenate([keys, values], axis=2)
    top_count = expert_ids.shape[1]
    use_gather = n_ctx * n_eg <= 4 * top_count
    if use_gather:
        flat_ids = expert_ids.reshape(-1).astype(jnp.bfloat16)
        id_count = flat_ids.shape[0]
        lane = shard_blocks * 2 * kv_width
        id_rows = -(-(-(-id_count // lane)) // 8) * 8
        id_slab = jnp.pad(flat_ids, (0, id_rows * lane - id_count)).reshape(
            shard_blocks, id_rows, 2 * kv_width
        )
        both = jnp.concatenate([both, id_slab], axis=1)
    gathered = lax.all_gather(both[None], ("ctx", "eg"), axis=0, tiled=True)
    if use_gather:
        all_ids = (
            gathered[:, :, slice_rows:, :]
            .reshape(n_ctx * n_eg, -1)[:, :id_count]
            .reshape(-1, top_count)
            .astype(jnp.int32)
        )
        gathered = gathered[:, :, :slice_rows, :]
    every_block = (
        gathered.reshape(n_ctx, n_eg, shard_blocks, slice_rows, 2 * kv_width)
        .transpose(0, 2, 1, 3, 4)
        .reshape(n_ctx * shard_blocks, block_rows, 2 * kv_width)
    )
    query_rows = queries.shape[0]
    my_block = (my_ctx * n_eg + my_eg) * query_rows // block_rows
    chosen_blocks = jnp.concatenate(
        [my_block[None].astype(jnp.int32), jnp.take(selected, my_block, axis=0)]
    )
    context = jnp.take(every_block, chosen_blocks, axis=0)
    context_keys = context[:, :, :kv_width]
    context_values = context[:, :, kv_width:]
    span = (1 + pick_count) * block_rows
    kv_heads = kv_width // HD
    attended = attend_rows(
        queries,
        context_keys.reshape(span, kv_heads, HD),
        context_values.reshape(span, kv_heads, HD),
    )
    tok_dev = residual.shape[0]
    pieces = {0: out_weight}
    for bit in reversed(range(n_eg.bit_length() - 1)):
        stride = 2**bit
        held = sorted(pieces)
        if len(held) > 1:
            barrier_out = lax.optimization_barrier((tuple(pieces[m] for m in held), attended))
            pieces = dict(zip(held, barrier_out[0]))
            attended = barrier_out[1]
        fetched = swapped(tuple(pieces[m] for m in held), "eg", bit)
        for m, piece in zip(held, fetched):
            pieces[m + stride] = piece
    weight_cols = jnp.concatenate([pieces[m] for m in range(n_eg)], axis=1)
    out_by_piece = jnp.dot(attended, weight_cols, preferred_element_type=jnp.float32).reshape(
        query_rows, n_eg, -1
    )
    piece_of_col = jnp.arange(n_eg, dtype=jnp.int32) ^ my_eg
    partial_out = jnp.take(out_by_piece, piece_of_col, axis=1).reshape(query_rows, -1)
    attn_out = lax.psum_scatter(
        partial_out.astype(jnp.bfloat16), "rep", scatter_dimension=0, tiled=True
    )
    stream = residual.astype(jnp.float32) + attn_out.astype(jnp.float32)
    meansq = jnp.mean(stream * stream, axis=1, keepdims=True)
    normed = (stream * lax.rsqrt(meansq + 1e-06) * norm_gain).astype(jnp.bfloat16)
    top_count = expert_ids.shape[1]
    slot_count = n_ctx * n_eg
    pair_count = tok_dev * top_count
    per_slot = pair_count // slot_count
    home_slot = jnp.take(expert_home, expert_ids.reshape(-1), axis=0)
    indicator = (home_slot[:, None] == jnp.arange(slot_count, dtype=jnp.int32)[None, :]).astype(
        jnp.int32
    )
    rank_in_slot = jnp.sum((jnp.cumsum(indicator, axis=0) - 1) * indicator, axis=1)
    position = home_slot * per_slot + rank_in_slot
    source_pair = (
        jnp.zeros((pair_count,), jnp.int32)
        .at[position]
        .set(jnp.arange(pair_count, dtype=jnp.int32))
    )
    partner = fetch_panels()
    if use_gather:
        my_slot = my_ctx * n_eg + my_eg
        all_packed = lax.all_gather(normed, ("ctx", "eg"), axis=0, tiled=True)
        expert_count = expert_home.shape[0]
        my_expert = jnp.sum(
            jnp.where(expert_home == my_slot, jnp.arange(expert_count, dtype=jnp.int32), 0)
        )
        hits = jnp.any(all_ids == my_expert, axis=1)
        hits = hits.reshape(slot_count, tok_dev).astype(jnp.int32)
        rank = jnp.cumsum(hits, axis=1) - 1
        chosen = jnp.logical_and(
            hits[:, None, :] == 1,
            rank[:, None, :] == jnp.arange(per_slot, dtype=jnp.int32)[None, :, None],
        )
        local_row = jnp.sum(
            chosen.astype(jnp.int32) * jnp.arange(tok_dev, dtype=jnp.int32)[None, None, :], axis=2
        )
        src_rows = local_row + jnp.arange(slot_count, dtype=jnp.int32)[:, None] * tok_dev
        hidden = partner[0].shape[1]
        gate_up = jnp.concatenate([partner[0], partner[1]], axis=1)
        both_act = jnp.dot(all_packed, gate_up, preferred_element_type=jnp.float32)
        gate_act = both_act[:, :hidden]
        up_act = both_act[:, hidden:]
        activation = (jax.nn.silu(gate_act) * up_act).astype(jnp.bfloat16)
        pick_matrix = (
            src_rows.reshape(-1)[:, None]
            == jnp.arange(activation.shape[0], dtype=jnp.int32)[None, :]
        ).astype(jnp.bfloat16)
        picked = jnp.dot(pick_matrix, activation, preferred_element_type=jnp.float32).astype(
            jnp.bfloat16
        )
        produced = jnp.dot(picked, partner[2], preferred_element_type=jnp.float32).astype(
            jnp.bfloat16
        )
    else:
        outbound = jnp.take(normed, source_pair // top_count, axis=0).reshape(
            slot_count, per_slot, -1
        )
        arrived = lax.all_to_all(outbound, ("ctx", "eg"), split_axis=0, concat_axis=0, tiled=True)
        flat_rows = arrived.reshape(-1, arrived.shape[2])
        produced = expert_apply(flat_rows, partner[0], partner[1], partner[2])
    returned = lax.all_to_all(
        produced.reshape(slot_count, per_slot, -1),
        ("ctx", "eg"),
        split_axis=0,
        concat_axis=0,
        tiled=True,
    )
    returned_rows = returned.reshape(pair_count, -1)
    placed = position.reshape(tok_dev, top_count)[:, :, None] == jnp.arange(
        pair_count, dtype=jnp.int32
    )[None, None, :]
    mixing = jnp.sum(jnp.where(placed, gate_weights[:, :, None], 0.0), axis=1)
    high_part = mixing.astype(jnp.bfloat16)
    low_part = (mixing - high_part.astype(jnp.float32)).astype(jnp.bfloat16)
    both_parts = jnp.concatenate([high_part, low_part], axis=0)
    stacked_out = jnp.dot(both_parts, returned_rows, preferred_element_type=jnp.float32)
    combined = stacked_out[:tok_dev] + stacked_out[tok_dev:]
    moe_out = combined.astype(jnp.bfloat16)
    return (attn_out, moe_out)


def solution(mesh):
    return jax.shard_map(
        local,
        mesh=mesh,
        in_specs=(
            P(("groups", "ctx", "eg"), "rep"),
            P(("groups", "ctx"), "eg", "rep"),
            P(("groups", "ctx"), "eg", "rep"),
            P("groups", None),
            P("rep", "eg"),
            P(("groups", "ctx", "eg", "rep"), None),
            P(),
            P(("groups", "ctx", "eg", "rep"), None),
            P(("groups", "ctx", "eg", "rep"), None),
            P(),
            P(("ctx", "eg"), None, "rep"),
            P(("ctx", "eg"), None, "rep"),
            P(("ctx", "eg"), "rep", None),
        ),
        out_specs=(
            P(("groups", "ctx", "eg", "rep"), None),
            P(("groups", "ctx", "eg", "rep"), None),
        ),
        check_vma=False,
    )
```

```python
import math

import jax
import jax.numpy as jnp
from jax import lax
from jax.experimental import pallas as pl
from jax.sharding import PartitionSpec as P

HD = 128


def swapped(value, axis, bit):
    mask = 2**bit
    pairs = [(source, source ^ mask) for source in range(lax.axis_size(axis))]
    return lax.ppermute(value, axis, pairs)


def attention_kernel(query_ref, key_ref, value_ref, out_ref):
    inverse_root = 1.0 / math.sqrt(HD)
    key_block = key_ref[...]
    value_block = value_ref[...]
    for head in range(query_ref.shape[1] // HD):
        query_head = query_ref[:, head * HD : (head + 1) * HD]
        logits = (
            lax.dot_general(
                query_head,
                key_block,
                (((1,), (1,)), ((), ())),
                preferred_element_type=jnp.float32,
            )
            * inverse_root
        )
        largest = jnp.max(logits, axis=-1, keepdims=True)
        raised = jnp.exp(logits - largest)
        denominator = jnp.sum(raised, axis=-1, keepdims=True)
        weights_low = (raised / denominator).astype(jnp.bfloat16)
        blended = jnp.dot(weights_low, value_block, preferred_element_type=jnp.float32)
        out_ref[:, head * HD : (head + 1) * HD] = blended.astype(out_ref.dtype)


def attend_rows(queries_flat, key_rows, value_rows, interpret=False):
    row_count = queries_flat.shape[0]
    span, kv_heads, _ = key_rows.shape
    group_width = queries_flat.shape[1] // kv_heads
    return pl.pallas_call(
        attention_kernel,
        grid=(kv_heads,),
        in_specs=[
            pl.BlockSpec((row_count, group_width), lambda k: (0, k)),
            pl.BlockSpec((span, HD), lambda k: (0, k)),
            pl.BlockSpec((span, HD), lambda k: (0, k)),
        ],
        out_specs=pl.BlockSpec((row_count, group_width), lambda k: (0, k)),
        out_shape=jax.ShapeDtypeStruct(queries_flat.shape, jnp.bfloat16),
        interpret=interpret,
    )(queries_flat, key_rows.reshape(span, -1), value_rows.reshape(span, -1))


def expert_apply(rows_in, gate_full, up_full, down_full):
    gate_act = jnp.dot(rows_in, gate_full, preferred_element_type=jnp.float32)
    up_act = jnp.dot(rows_in, up_full, preferred_element_type=jnp.float32)
    activation = (jax.nn.silu(gate_act) * up_act).astype(jnp.bfloat16)
    return jnp.dot(activation, down_full, preferred_element_type=jnp.float32).astype(jnp.bfloat16)


def local(
    queries,
    keys,
    values,
    selected,
    out_weight,
    residual,
    norm_gain,
    expert_ids,
    gate_weights,
    expert_home,
    w_gate,
    w_up,
    w_down,
):
    n_ctx = lax.axis_size("ctx")
    n_eg = lax.axis_size("eg")
    n_rep = lax.axis_size("rep")
    my_ctx = lax.axis_index("ctx")

    def fetch_panels():
        if n_rep == 1:
            return (w_gate[0], w_up[0], w_down[0])
        other_gate, other_up, other_down = swapped((w_gate, w_up, w_down), "rep", 0)
        first = lax.axis_index("rep") == 0
        gate_full = jnp.where(
            first,
            jnp.concatenate([w_gate[0], other_gate[0]], axis=1),
            jnp.concatenate([other_gate[0], w_gate[0]], axis=1),
        )
        up_full = jnp.where(
            first,
            jnp.concatenate([w_up[0], other_up[0]], axis=1),
            jnp.concatenate([other_up[0], w_up[0]], axis=1),
        )
        down_full = jnp.where(
            first,
            jnp.concatenate([w_down[0], other_down[0]], axis=0),
            jnp.concatenate([other_down[0], w_down[0]], axis=0),
        )
        return (gate_full, up_full, down_full)

    shard_blocks, slice_rows, kv_width = keys.shape
    pick_count = selected.shape[1]
    block_rows = slice_rows * n_eg
    my_eg = lax.axis_index("eg")
    both = jnp.concatenate([keys, values], axis=2)
    top_count = expert_ids.shape[1]
    use_gather = n_ctx * n_eg <= 4 * top_count
    if use_gather:
        flat_ids = expert_ids.reshape(-1).astype(jnp.bfloat16)
        id_count = flat_ids.shape[0]
        lane = shard_blocks * 2 * kv_width
        id_rows = -(-(-(-id_count // lane)) // 8) * 8
        id_slab = jnp.pad(flat_ids, (0, id_rows * lane - id_count)).reshape(
            shard_blocks, id_rows, 2 * kv_width
        )
        both = jnp.concatenate([both, id_slab], axis=1)
    gathered = lax.all_gather(both[None], ("ctx", "eg"), axis=0, tiled=True)
    if use_gather:
        all_ids = (
            gathered[:, :, slice_rows:, :]
            .reshape(n_ctx * n_eg, -1)[:, :id_count]
            .reshape(-1, top_count)
            .astype(jnp.int32)
        )
        gathered = gathered[:, :, :slice_rows, :]
    every_block = (
        gathered.reshape(n_ctx, n_eg, shard_blocks, slice_rows, 2 * kv_width)
        .transpose(0, 2, 1, 3, 4)
        .reshape(n_ctx * shard_blocks, block_rows, 2 * kv_width)
    )
    query_rows = queries.shape[0]
    my_block = (my_ctx * n_eg + my_eg) * query_rows // block_rows
    chosen_blocks = jnp.concatenate(
        [my_block[None].astype(jnp.int32), jnp.take(selected, my_block, axis=0)]
    )
    context = jnp.take(every_block, chosen_blocks, axis=0)
    span = (1 + pick_count) * block_rows
    kv_heads = kv_width // HD
    tok_dev = residual.shape[0]
    pieces = {0: out_weight}
    for bit in reversed(range(n_eg.bit_length() - 1)):
        stride = 2**bit
        held = sorted(pieces)
        if len(held) > 1:
            barrier_out = lax.optimization_barrier((tuple(pieces[m] for m in held), context))
            pieces = dict(zip(held, barrier_out[0]))
            context = barrier_out[1]
        fetched = swapped(tuple(pieces[m] for m in held), "eg", bit)
        for m, piece in zip(held, fetched):
            pieces[m + stride] = piece
    context_keys = context[:, :, :kv_width]
    context_values = context[:, :, kv_width:]
    attended = attend_rows(
        queries,
        context_keys.reshape(span, kv_heads, HD),
        context_values.reshape(span, kv_heads, HD),
    )
    weight_cols = jnp.concatenate([pieces[m] for m in range(n_eg)], axis=1)
    out_by_piece = jnp.dot(attended, weight_cols, preferred_element_type=jnp.float32).reshape(
        query_rows, n_eg, -1
    )
    piece_of_col = jnp.arange(n_eg, dtype=jnp.int32) ^ my_eg
    partial_out = jnp.take(out_by_piece, piece_of_col, axis=1).reshape(query_rows, -1)
    attn_out = lax.psum_scatter(
        partial_out.astype(jnp.bfloat16), "rep", scatter_dimension=0, tiled=True
    )
    stream = residual.astype(jnp.float32) + attn_out.astype(jnp.float32)
    meansq = jnp.mean(stream * stream, axis=1, keepdims=True)
    normed = (stream * lax.rsqrt(meansq + 1e-06) * norm_gain).astype(jnp.bfloat16)
    top_count = expert_ids.shape[1]
    slot_count = n_ctx * n_eg
    pair_count = tok_dev * top_count
    per_slot = pair_count // slot_count
    home_slot = jnp.take(expert_home, expert_ids.reshape(-1), axis=0)
    indicator = (home_slot[:, None] == jnp.arange(slot_count, dtype=jnp.int32)[None, :]).astype(
        jnp.int32
    )
    rank_in_slot = jnp.sum((jnp.cumsum(indicator, axis=0) - 1) * indicator, axis=1)
    position = home_slot * per_slot + rank_in_slot
    source_pair = (
        jnp.zeros((pair_count,), jnp.int32)
        .at[position]
        .set(jnp.arange(pair_count, dtype=jnp.int32))
    )
    partner = fetch_panels()
    if use_gather:
        my_slot = my_ctx * n_eg + my_eg
        all_packed = lax.all_gather(normed, ("ctx", "eg"), axis=0, tiled=True)
        expert_count = expert_home.shape[0]
        my_expert = jnp.sum(
            jnp.where(expert_home == my_slot, jnp.arange(expert_count, dtype=jnp.int32), 0)
        )
        hits = jnp.any(all_ids == my_expert, axis=1)
        hits = hits.reshape(slot_count, tok_dev).astype(jnp.int32)
        rank = jnp.cumsum(hits, axis=1) - 1
        chosen = jnp.logical_and(
            hits[:, None, :] == 1,
            rank[:, None, :] == jnp.arange(per_slot, dtype=jnp.int32)[None, :, None],
        )
        local_row = jnp.sum(
            chosen.astype(jnp.int32) * jnp.arange(tok_dev, dtype=jnp.int32)[None, None, :], axis=2
        )
        src_rows = local_row + jnp.arange(slot_count, dtype=jnp.int32)[:, None] * tok_dev
        hidden = partner[0].shape[1]
        gate_up = jnp.concatenate([partner[0], partner[1]], axis=1)
        both_act = jnp.dot(all_packed, gate_up, preferred_element_type=jnp.float32)
        gate_act = both_act[:, :hidden]
        up_act = both_act[:, hidden:]
        activation = (jax.nn.silu(gate_act) * up_act).astype(jnp.bfloat16)
        pick_matrix = (
            src_rows.reshape(-1)[:, None]
            == jnp.arange(activation.shape[0], dtype=jnp.int32)[None, :]
        ).astype(jnp.bfloat16)
        picked = jnp.dot(pick_matrix, activation, preferred_element_type=jnp.float32).astype(
            jnp.bfloat16
        )
        produced = jnp.dot(picked, partner[2], preferred_element_type=jnp.float32).astype(
            jnp.bfloat16
        )
    else:
        outbound = jnp.take(normed, source_pair // top_count, axis=0).reshape(
            slot_count, per_slot, -1
        )
        arrived = lax.all_to_all(outbound, ("ctx", "eg"), split_axis=0, concat_axis=0, tiled=True)
        flat_rows = arrived.reshape(-1, arrived.shape[2])
        produced = expert_apply(flat_rows, partner[0], partner[1], partner[2])
    returned = lax.all_to_all(
        produced.reshape(slot_count, per_slot, -1),
        ("ctx", "eg"),
        split_axis=0,
        concat_axis=0,
        tiled=True,
    )
    returned_rows = returned.reshape(pair_count, -1)
    placed = position.reshape(tok_dev, top_count)[:, :, None] == jnp.arange(
        pair_count, dtype=jnp.int32
    )[None, None, :]
    mixing = jnp.sum(jnp.where(placed, gate_weights[:, :, None], 0.0), axis=1)
    high_part = mixing.astype(jnp.bfloat16)
    low_part = (mixing - high_part.astype(jnp.float32)).astype(jnp.bfloat16)
    both_parts = jnp.concatenate([high_part, low_part], axis=0)
    stacked_out = jnp.dot(both_parts, returned_rows, preferred_element_type=jnp.float32)
    combined = stacked_out[:tok_dev] + stacked_out[tok_dev:]
    moe_out = combined.astype(jnp.bfloat16)
    return (attn_out, moe_out)


def solution(mesh):
    return jax.shard_map(
        local,
        mesh=mesh,
        in_specs=(
            P(("groups", "ctx", "eg"), "rep"),
            P(("groups", "ctx"), "eg", "rep"),
            P(("groups", "ctx"), "eg", "rep"),
            P("groups", None),
            P("rep", "eg"),
            P(("groups", "ctx", "eg", "rep"), None),
            P(),
            P(("groups", "ctx", "eg", "rep"), None),
            P(("groups", "ctx", "eg", "rep"), None),
            P(),
            P(("ctx", "eg"), None, "rep"),
            P(("ctx", "eg"), None, "rep"),
            P(("ctx", "eg"), "rep", None),
        ),
        out_specs=(
            P(("groups", "ctx", "eg", "rep"), None),
            P(("groups", "ctx", "eg", "rep"), None),
        ),
        check_vma=False,
    )
```

```python
import math

import jax
import jax.numpy as jnp
from jax import lax
from jax.experimental import pallas as pl
from jax.sharding import PartitionSpec as P

HD = 128


def swapped(value, axis, bit):
    mask = 2**bit
    pairs = [(source, source ^ mask) for source in range(lax.axis_size(axis))]
    return lax.ppermute(value, axis, pairs)


def attention_kernel(query_ref, key_ref, value_ref, out_ref):
    inverse_root = 1.0 / math.sqrt(HD)
    key_block = key_ref[...]
    value_block = value_ref[...]
    for head in range(query_ref.shape[1] // HD):
        query_head = query_ref[:, head * HD : (head + 1) * HD]
        logits = (
            lax.dot_general(
                query_head,
                key_block,
                (((1,), (1,)), ((), ())),
                preferred_element_type=jnp.float32,
            )
            * inverse_root
        )
        largest = jnp.max(logits, axis=-1, keepdims=True)
        raised = jnp.exp(logits - largest)
        denominator = jnp.sum(raised, axis=-1, keepdims=True)
        weights_low = (raised / denominator).astype(jnp.bfloat16)
        blended = jnp.dot(weights_low, value_block, preferred_element_type=jnp.float32)
        out_ref[:, head * HD : (head + 1) * HD] = blended.astype(out_ref.dtype)


def attend_rows(queries_flat, context, kv_heads, interpret=False):
    row_count = queries_flat.shape[0]
    span = context.shape[0]
    group_width = queries_flat.shape[1] // kv_heads
    return pl.pallas_call(
        attention_kernel,
        grid=(kv_heads,),
        in_specs=[
            pl.BlockSpec((row_count, group_width), lambda k: (0, k)),
            pl.BlockSpec((span, HD), lambda k: (0, k)),
            pl.BlockSpec((span, HD), lambda k: (0, kv_heads + k)),
        ],
        out_specs=pl.BlockSpec((row_count, group_width), lambda k: (0, k)),
        out_shape=jax.ShapeDtypeStruct(queries_flat.shape, jnp.bfloat16),
        interpret=interpret,
    )(queries_flat, context, context)


def expert_apply(rows_in, gate_full, up_full, down_full):
    gate_act = jnp.dot(rows_in, gate_full, preferred_element_type=jnp.float32)
    up_act = jnp.dot(rows_in, up_full, preferred_element_type=jnp.float32)
    activation = (jax.nn.silu(gate_act) * up_act).astype(jnp.bfloat16)
    return jnp.dot(activation, down_full, preferred_element_type=jnp.float32).astype(jnp.bfloat16)


def local(
    queries,
    keys,
    values,
    selected,
    out_weight,
    residual,
    norm_gain,
    expert_ids,
    gate_weights,
    expert_home,
    w_gate,
    w_up,
    w_down,
):
    n_ctx = lax.axis_size("ctx")
    n_eg = lax.axis_size("eg")
    n_rep = lax.axis_size("rep")
    my_ctx = lax.axis_index("ctx")

    def fetch_panels():
        if n_rep == 1:
            return (w_gate[0], w_up[0], w_down[0])
        other_gate, other_up, other_down = swapped((w_gate, w_up, w_down), "rep", 0)
        first = lax.axis_index("rep") == 0
        gate_full = jnp.where(
            first,
            jnp.concatenate([w_gate[0], other_gate[0]], axis=1),
            jnp.concatenate([other_gate[0], w_gate[0]], axis=1),
        )
        up_full = jnp.where(
            first,
            jnp.concatenate([w_up[0], other_up[0]], axis=1),
            jnp.concatenate([other_up[0], w_up[0]], axis=1),
        )
        down_full = jnp.where(
            first,
            jnp.concatenate([w_down[0], other_down[0]], axis=0),
            jnp.concatenate([other_down[0], w_down[0]], axis=0),
        )
        return (gate_full, up_full, down_full)

    shard_blocks, slice_rows, kv_width = keys.shape
    pick_count = selected.shape[1]
    block_rows = slice_rows * n_eg
    my_eg = lax.axis_index("eg")
    both = jnp.concatenate([keys, values], axis=2)
    top_count = expert_ids.shape[1]
    use_gather = n_ctx * n_eg <= 4 * top_count
    if use_gather:
        flat_ids = expert_ids.reshape(-1).astype(jnp.bfloat16)
        id_count = flat_ids.shape[0]
        lane = shard_blocks * 2 * kv_width
        id_rows = -(-(-(-id_count // lane)) // 8) * 8
        id_slab = jnp.pad(flat_ids, (0, id_rows * lane - id_count)).reshape(
            shard_blocks, id_rows, 2 * kv_width
        )
        both = jnp.concatenate([both, id_slab], axis=1)
    gathered = lax.all_gather(both[None], ("ctx", "eg"), axis=0, tiled=True)
    if use_gather:
        all_ids = (
            gathered[:, :, slice_rows:, :]
            .reshape(n_ctx * n_eg, -1)[:, :id_count]
            .reshape(-1, top_count)
            .astype(jnp.int32)
        )
    held_rows = gathered.shape[2]
    by_shard = gathered.reshape(n_ctx, n_eg, shard_blocks, held_rows, 2 * kv_width)
    query_rows = queries.shape[0]
    my_block = (my_ctx * n_eg + my_eg) * query_rows // block_rows
    chosen_blocks = jnp.concatenate(
        [my_block[None].astype(jnp.int32), jnp.take(selected, my_block, axis=0)]
    )
    picked_shards = jnp.take(by_shard, chosen_blocks // shard_blocks, axis=0)
    picked_shards = jnp.take_along_axis(
        picked_shards, (chosen_blocks % shard_blocks)[:, None, None, None, None], axis=2
    )
    context = picked_shards[:, :, 0, :slice_rows, :].reshape(-1, 2 * kv_width)
    span = (1 + pick_count) * block_rows
    kv_heads = kv_width // HD
    tok_dev = residual.shape[0]
    pieces = {0: out_weight}
    for bit in reversed(range(n_eg.bit_length() - 1)):
        stride = 2**bit
        held = sorted(pieces)
        if len(held) > 1:
            barrier_out = lax.optimization_barrier((tuple(pieces[m] for m in held), context))
            pieces = dict(zip(held, barrier_out[0]))
            context = barrier_out[1]
        fetched = swapped(tuple(pieces[m] for m in held), "eg", bit)
        for m, piece in zip(held, fetched):
            pieces[m + stride] = piece
    attended = attend_rows(queries, context, kv_heads)
    weight_cols = jnp.concatenate([pieces[m] for m in range(n_eg)], axis=1)
    out_by_piece = jnp.dot(attended, weight_cols, preferred_element_type=jnp.float32).reshape(
        query_rows, n_eg, -1
    )
    piece_of_col = jnp.arange(n_eg, dtype=jnp.int32) ^ my_eg
    partial_out = jnp.take(out_by_piece, piece_of_col, axis=1).reshape(query_rows, -1)
    attn_out = lax.psum_scatter(
        partial_out.astype(jnp.bfloat16), "rep", scatter_dimension=0, tiled=True
    )
    stream = residual.astype(jnp.float32) + attn_out.astype(jnp.float32)
    meansq = jnp.mean(stream * stream, axis=1, keepdims=True)
    normed = (stream * lax.rsqrt(meansq + 1e-06) * norm_gain).astype(jnp.bfloat16)
    top_count = expert_ids.shape[1]
    slot_count = n_ctx * n_eg
    pair_count = tok_dev * top_count
    per_slot = pair_count // slot_count
    home_slot = jnp.take(expert_home, expert_ids.reshape(-1), axis=0)
    indicator = (home_slot[:, None] == jnp.arange(slot_count, dtype=jnp.int32)[None, :]).astype(
        jnp.int32
    )
    rank_in_slot = jnp.sum((jnp.cumsum(indicator, axis=0) - 1) * indicator, axis=1)
    position = home_slot * per_slot + rank_in_slot
    source_pair = (
        jnp.zeros((pair_count,), jnp.int32)
        .at[position]
        .set(jnp.arange(pair_count, dtype=jnp.int32))
    )
    partner = fetch_panels()
    if use_gather:
        my_slot = my_ctx * n_eg + my_eg
        all_packed = lax.all_gather(normed, ("ctx", "eg"), axis=0, tiled=True)
        expert_count = expert_home.shape[0]
        my_expert = jnp.sum(
            jnp.where(expert_home == my_slot, jnp.arange(expert_count, dtype=jnp.int32), 0)
        )
        hits = jnp.any(all_ids == my_expert, axis=1)
        hits = hits.reshape(slot_count, tok_dev).astype(jnp.int32)
        rank = jnp.cumsum(hits, axis=1) - 1
        chosen = jnp.logical_and(
            hits[:, None, :] == 1,
            rank[:, None, :] == jnp.arange(per_slot, dtype=jnp.int32)[None, :, None],
        )
        local_row = jnp.sum(
            chosen.astype(jnp.int32) * jnp.arange(tok_dev, dtype=jnp.int32)[None, None, :], axis=2
        )
        src_rows = local_row + jnp.arange(slot_count, dtype=jnp.int32)[:, None] * tok_dev
        hidden = partner[0].shape[1]
        gate_up = jnp.concatenate([partner[0], partner[1]], axis=1)
        both_act = jnp.dot(all_packed, gate_up, preferred_element_type=jnp.float32)
        gate_act = both_act[:, :hidden]
        up_act = both_act[:, hidden:]
        activation = (jax.nn.silu(gate_act) * up_act).astype(jnp.bfloat16)
        pick_matrix = (
            src_rows.reshape(-1)[:, None]
            == jnp.arange(activation.shape[0], dtype=jnp.int32)[None, :]
        ).astype(jnp.bfloat16)
        picked = jnp.dot(pick_matrix, activation, preferred_element_type=jnp.float32).astype(
            jnp.bfloat16
        )
        produced = jnp.dot(picked, partner[2], preferred_element_type=jnp.float32).astype(
            jnp.bfloat16
        )
    else:
        outbound = jnp.take(normed, source_pair // top_count, axis=0).reshape(
            slot_count, per_slot, -1
        )
        arrived = lax.all_to_all(outbound, ("ctx", "eg"), split_axis=0, concat_axis=0, tiled=True)
        flat_rows = arrived.reshape(-1, arrived.shape[2])
        produced = expert_apply(flat_rows, partner[0], partner[1], partner[2])
    returned = lax.all_to_all(
        produced.reshape(slot_count, per_slot, -1),
        ("ctx", "eg"),
        split_axis=0,
        concat_axis=0,
        tiled=True,
    )
    returned_rows = returned.reshape(pair_count, -1)
    placed = position.reshape(tok_dev, top_count)[:, :, None] == jnp.arange(
        pair_count, dtype=jnp.int32
    )[None, None, :]
    mixing = jnp.sum(jnp.where(placed, gate_weights[:, :, None], 0.0), axis=1)
    high_part = mixing.astype(jnp.bfloat16)
    low_part = (mixing - high_part.astype(jnp.float32)).astype(jnp.bfloat16)
    both_parts = jnp.concatenate([high_part, low_part], axis=0)
    stacked_out = jnp.dot(both_parts, returned_rows, preferred_element_type=jnp.float32)
    combined = stacked_out[:tok_dev] + stacked_out[tok_dev:]
    moe_out = combined.astype(jnp.bfloat16)
    return (attn_out, moe_out)


def solution(mesh):
    return jax.shard_map(
        local,
        mesh=mesh,
        in_specs=(
            P(("groups", "ctx", "eg"), "rep"),
            P(("groups", "ctx"), "eg", "rep"),
            P(("groups", "ctx"), "eg", "rep"),
            P("groups", None),
            P("rep", "eg"),
            P(("groups", "ctx", "eg", "rep"), None),
            P(),
            P(("groups", "ctx", "eg", "rep"), None),
            P(("groups", "ctx", "eg", "rep"), None),
            P(),
            P(("ctx", "eg"), None, "rep"),
            P(("ctx", "eg"), None, "rep"),
            P(("ctx", "eg"), "rep", None),
        ),
        out_specs=(
            P(("groups", "ctx", "eg", "rep"), None),
            P(("groups", "ctx", "eg", "rep"), None),
        ),
        check_vma=False,
    )
```

```python
import math

import jax
import jax.numpy as jnp
from jax import lax
from jax.experimental import pallas as pl
from jax.sharding import PartitionSpec as P

HD = 128


def swapped(value, axis, bit):
    mask = 2**bit
    pairs = [(source, source ^ mask) for source in range(lax.axis_size(axis))]
    return lax.ppermute(value, axis, pairs)


def attention_kernel(query_ref, key_ref, value_ref, out_ref):
    inverse_root = 1.0 / math.sqrt(HD)
    key_block = key_ref[...]
    value_block = value_ref[...]
    for head in range(query_ref.shape[1] // HD):
        query_head = query_ref[:, head * HD : (head + 1) * HD]
        logits = (
            lax.dot_general(
                query_head,
                key_block,
                (((1,), (1,)), ((), ())),
                preferred_element_type=jnp.float32,
            )
            * inverse_root
        )
        largest = jnp.max(logits, axis=-1, keepdims=True)
        raised = jnp.exp(logits - largest)
        denominator = jnp.sum(raised, axis=-1, keepdims=True)
        weights_low = (raised / denominator).astype(jnp.bfloat16)
        blended = jnp.dot(weights_low, value_block, preferred_element_type=jnp.float32)
        out_ref[:, head * HD : (head + 1) * HD] = blended.astype(out_ref.dtype)


def attend_rows(queries_flat, context, kv_heads, interpret=False):
    row_count = queries_flat.shape[0]
    span = context.shape[0]
    group_width = queries_flat.shape[1] // kv_heads
    return pl.pallas_call(
        attention_kernel,
        grid=(kv_heads,),
        in_specs=[
            pl.BlockSpec((row_count, group_width), lambda k: (0, k)),
            pl.BlockSpec((span, HD), lambda k: (0, k)),
            pl.BlockSpec((span, HD), lambda k: (0, kv_heads + k)),
        ],
        out_specs=pl.BlockSpec((row_count, group_width), lambda k: (0, k)),
        out_shape=jax.ShapeDtypeStruct(queries_flat.shape, jnp.bfloat16),
        interpret=interpret,
    )(queries_flat, context, context)


def expert_apply(rows_in, gate_full, up_full, down_full):
    gate_act = jnp.dot(rows_in, gate_full, preferred_element_type=jnp.float32)
    up_act = jnp.dot(rows_in, up_full, preferred_element_type=jnp.float32)
    activation = (jax.nn.silu(gate_act) * up_act).astype(jnp.bfloat16)
    return jnp.dot(activation, down_full, preferred_element_type=jnp.float32).astype(jnp.bfloat16)


def local(
    queries,
    keys,
    values,
    selected,
    out_weight,
    residual,
    norm_gain,
    expert_ids,
    gate_weights,
    expert_home,
    w_gate,
    w_up,
    w_down,
):
    n_ctx = lax.axis_size("ctx")
    n_eg = lax.axis_size("eg")
    n_rep = lax.axis_size("rep")
    my_ctx = lax.axis_index("ctx")

    def fetch_panels():
        if n_rep == 1:
            return (w_gate[0], w_up[0], w_down[0])
        other_gate, other_up, other_down = swapped((w_gate, w_up, w_down), "rep", 0)
        first = lax.axis_index("rep") == 0
        gate_full = jnp.where(
            first,
            jnp.concatenate([w_gate[0], other_gate[0]], axis=1),
            jnp.concatenate([other_gate[0], w_gate[0]], axis=1),
        )
        up_full = jnp.where(
            first,
            jnp.concatenate([w_up[0], other_up[0]], axis=1),
            jnp.concatenate([other_up[0], w_up[0]], axis=1),
        )
        down_full = jnp.where(
            first,
            jnp.concatenate([w_down[0], other_down[0]], axis=0),
            jnp.concatenate([other_down[0], w_down[0]], axis=0),
        )
        return (gate_full, up_full, down_full)

    shard_blocks, slice_rows, kv_width = keys.shape
    pick_count = selected.shape[1]
    block_rows = slice_rows * n_eg
    my_eg = lax.axis_index("eg")
    both = jnp.concatenate([keys, values], axis=2)
    top_count = expert_ids.shape[1]
    use_gather = n_ctx * n_eg <= 4 * top_count
    if use_gather:
        flat_ids = expert_ids.reshape(-1).astype(jnp.bfloat16)
        id_count = flat_ids.shape[0]
        lane = shard_blocks * 2 * kv_width
        id_rows = -(-(-(-id_count // lane)) // 8) * 8
        id_slab = jnp.pad(flat_ids, (0, id_rows * lane - id_count)).reshape(
            shard_blocks, id_rows, 2 * kv_width
        )
        both = jnp.concatenate([both, id_slab], axis=1)
    gathered = lax.all_gather(both[None], ("ctx", "eg"), axis=0, tiled=True)
    if use_gather:
        all_ids = (
            gathered[:, :, slice_rows:, :]
            .reshape(n_ctx * n_eg, -1)[:, :id_count]
            .reshape(-1, top_count)
            .astype(jnp.int32)
        )
    held_rows = gathered.shape[2]
    by_slice = gathered.reshape(n_ctx * n_eg * shard_blocks, held_rows, 2 * kv_width)
    query_rows = queries.shape[0]
    my_block = (my_ctx * n_eg + my_eg) * query_rows // block_rows
    chosen_blocks = jnp.concatenate(
        [my_block[None].astype(jnp.int32), jnp.take(selected, my_block, axis=0)]
    )
    slice_index = (
        (chosen_blocks // shard_blocks)[:, None] * n_eg + jnp.arange(n_eg, dtype=jnp.int32)[None, :]
    ) * shard_blocks + (chosen_blocks % shard_blocks)[:, None]
    context = jnp.take(by_slice[:, :slice_rows], slice_index.reshape(-1), axis=0).reshape(
        -1, 2 * kv_width
    )
    span = (1 + pick_count) * block_rows
    kv_heads = kv_width // HD
    tok_dev = residual.shape[0]
    pieces = {0: out_weight}
    for bit in reversed(range(n_eg.bit_length() - 1)):
        stride = 2**bit
        held = sorted(pieces)
        if len(held) > 1:
            barrier_out = lax.optimization_barrier((tuple(pieces[m] for m in held), context))
            pieces = dict(zip(held, barrier_out[0]))
            context = barrier_out[1]
        fetched = swapped(tuple(pieces[m] for m in held), "eg", bit)
        for m, piece in zip(held, fetched):
            pieces[m + stride] = piece
    attended = attend_rows(queries, context, kv_heads)
    weight_cols = jnp.concatenate([pieces[m] for m in range(n_eg)], axis=1)
    out_by_piece = jnp.dot(attended, weight_cols, preferred_element_type=jnp.float32).reshape(
        query_rows, n_eg, -1
    )
    piece_of_col = jnp.arange(n_eg, dtype=jnp.int32) ^ my_eg
    partial_out = jnp.take(out_by_piece, piece_of_col, axis=1).reshape(query_rows, -1)
    attn_out = lax.psum_scatter(
        partial_out.astype(jnp.bfloat16), "rep", scatter_dimension=0, tiled=True
    )
    stream = residual.astype(jnp.float32) + attn_out.astype(jnp.float32)
    meansq = jnp.mean(stream * stream, axis=1, keepdims=True)
    normed = (stream * lax.rsqrt(meansq + 1e-06) * norm_gain).astype(jnp.bfloat16)
    top_count = expert_ids.shape[1]
    slot_count = n_ctx * n_eg
    pair_count = tok_dev * top_count
    per_slot = pair_count // slot_count
    home_slot = jnp.take(expert_home, expert_ids.reshape(-1), axis=0)
    indicator = (home_slot[:, None] == jnp.arange(slot_count, dtype=jnp.int32)[None, :]).astype(
        jnp.int32
    )
    rank_in_slot = jnp.sum((jnp.cumsum(indicator, axis=0) - 1) * indicator, axis=1)
    position = home_slot * per_slot + rank_in_slot
    source_pair = (
        jnp.zeros((pair_count,), jnp.int32)
        .at[position]
        .set(jnp.arange(pair_count, dtype=jnp.int32))
    )
    partner = fetch_panels()
    if use_gather:
        my_slot = my_ctx * n_eg + my_eg
        all_packed = lax.all_gather(normed, ("ctx", "eg"), axis=0, tiled=True)
        expert_count = expert_home.shape[0]
        my_expert = jnp.sum(
            jnp.where(expert_home == my_slot, jnp.arange(expert_count, dtype=jnp.int32), 0)
        )
        hits = jnp.any(all_ids == my_expert, axis=1)
        hits = hits.reshape(slot_count, tok_dev).astype(jnp.int32)
        rank = jnp.cumsum(hits, axis=1) - 1
        chosen = jnp.logical_and(
            hits[:, None, :] == 1,
            rank[:, None, :] == jnp.arange(per_slot, dtype=jnp.int32)[None, :, None],
        )
        local_row = jnp.sum(
            chosen.astype(jnp.int32) * jnp.arange(tok_dev, dtype=jnp.int32)[None, None, :], axis=2
        )
        src_rows = local_row + jnp.arange(slot_count, dtype=jnp.int32)[:, None] * tok_dev
        hidden = partner[0].shape[1]
        gate_up = jnp.concatenate([partner[0], partner[1]], axis=1)
        both_act = jnp.dot(all_packed, gate_up, preferred_element_type=jnp.float32)
        gate_act = both_act[:, :hidden]
        up_act = both_act[:, hidden:]
        activation = (jax.nn.silu(gate_act) * up_act).astype(jnp.bfloat16)
        pick_matrix = (
            src_rows.reshape(-1)[:, None]
            == jnp.arange(activation.shape[0], dtype=jnp.int32)[None, :]
        ).astype(jnp.bfloat16)
        picked = jnp.dot(pick_matrix, activation, preferred_element_type=jnp.float32).astype(
            jnp.bfloat16
        )
        produced = jnp.dot(picked, partner[2], preferred_element_type=jnp.float32).astype(
            jnp.bfloat16
        )
    else:
        outbound = jnp.take(normed, source_pair // top_count, axis=0).reshape(
            slot_count, per_slot, -1
        )
        arrived = lax.all_to_all(outbound, ("ctx", "eg"), split_axis=0, concat_axis=0, tiled=True)
        flat_rows = arrived.reshape(-1, arrived.shape[2])
        produced = expert_apply(flat_rows, partner[0], partner[1], partner[2])
    returned = lax.all_to_all(
        produced.reshape(slot_count, per_slot, -1),
        ("ctx", "eg"),
        split_axis=0,
        concat_axis=0,
        tiled=True,
    )
    returned_rows = returned.reshape(pair_count, -1)
    placed = position.reshape(tok_dev, top_count)[:, :, None] == jnp.arange(
        pair_count, dtype=jnp.int32
    )[None, None, :]
    mixing = jnp.sum(jnp.where(placed, gate_weights[:, :, None], 0.0), axis=1)
    high_part = mixing.astype(jnp.bfloat16)
    low_part = (mixing - high_part.astype(jnp.float32)).astype(jnp.bfloat16)
    both_parts = jnp.concatenate([high_part, low_part], axis=0)
    stacked_out = jnp.dot(both_parts, returned_rows, preferred_element_type=jnp.float32)
    combined = stacked_out[:tok_dev] + stacked_out[tok_dev:]
    moe_out = combined.astype(jnp.bfloat16)
    return (attn_out, moe_out)


def solution(mesh):
    return jax.shard_map(
        local,
        mesh=mesh,
        in_specs=(
            P(("groups", "ctx", "eg"), "rep"),
            P(("groups", "ctx"), "eg", "rep"),
            P(("groups", "ctx"), "eg", "rep"),
            P("groups", None),
            P("rep", "eg"),
            P(("groups", "ctx", "eg", "rep"), None),
            P(),
            P(("groups", "ctx", "eg", "rep"), None),
            P(("groups", "ctx", "eg", "rep"), None),
            P(),
            P(("ctx", "eg"), None, "rep"),
            P(("ctx", "eg"), None, "rep"),
            P(("ctx", "eg"), "rep", None),
        ),
        out_specs=(
            P(("groups", "ctx", "eg", "rep"), None),
            P(("groups", "ctx", "eg", "rep"), None),
        ),
        check_vma=False,
    )
```

```python
import math

import jax
import jax.numpy as jnp
from jax import lax
from jax.experimental import pallas as pl
from jax.sharding import PartitionSpec as P

HD = 128


def swapped(value, axis, bit):
    mask = 2**bit
    pairs = [(source, source ^ mask) for source in range(lax.axis_size(axis))]
    return lax.ppermute(value, axis, pairs)


def attention_kernel(query_ref, key_ref, value_ref, out_ref):
    inverse_root = 1.0 / math.sqrt(HD)
    key_block = key_ref[...]
    value_block = value_ref[...]
    for head in range(query_ref.shape[1] // HD):
        query_head = query_ref[:, head * HD : (head + 1) * HD]
        logits = (
            lax.dot_general(
                query_head,
                key_block,
                (((1,), (1,)), ((), ())),
                preferred_element_type=jnp.float32,
            )
            * inverse_root
        )
        largest = jnp.max(logits, axis=-1, keepdims=True)
        raised = jnp.exp(logits - largest)
        denominator = jnp.sum(raised, axis=-1, keepdims=True)
        weights_low = (raised / denominator).astype(jnp.bfloat16)
        blended = jnp.dot(weights_low, value_block, preferred_element_type=jnp.float32)
        out_ref[:, head * HD : (head + 1) * HD] = blended.astype(out_ref.dtype)


def attend_rows(queries_flat, context, kv_heads, interpret=False):
    row_count = queries_flat.shape[0]
    span = context.shape[0]
    group_width = queries_flat.shape[1] // kv_heads
    return pl.pallas_call(
        attention_kernel,
        grid=(kv_heads,),
        in_specs=[
            pl.BlockSpec((row_count, group_width), lambda k: (0, k)),
            pl.BlockSpec((span, HD), lambda k: (0, k)),
            pl.BlockSpec((span, HD), lambda k: (0, kv_heads + k)),
        ],
        out_specs=pl.BlockSpec((row_count, group_width), lambda k: (0, k)),
        out_shape=jax.ShapeDtypeStruct(queries_flat.shape, jnp.bfloat16),
        interpret=interpret,
    )(queries_flat, context, context)


def expert_apply(rows_in, gate_full, up_full, down_full):
    gate_act = jnp.dot(rows_in, gate_full, preferred_element_type=jnp.float32)
    up_act = jnp.dot(rows_in, up_full, preferred_element_type=jnp.float32)
    activation = (jax.nn.silu(gate_act) * up_act).astype(jnp.bfloat16)
    return jnp.dot(activation, down_full, preferred_element_type=jnp.float32).astype(jnp.bfloat16)


def local(
    queries,
    keys,
    values,
    selected,
    out_weight,
    residual,
    norm_gain,
    expert_ids,
    gate_weights,
    expert_home,
    w_gate,
    w_up,
    w_down,
):
    n_ctx = lax.axis_size("ctx")
    n_eg = lax.axis_size("eg")
    n_rep = lax.axis_size("rep")
    my_ctx = lax.axis_index("ctx")

    def fetch_panels():
        if n_rep == 1:
            return (w_gate[0], w_up[0], w_down[0])
        other_gate, other_up, other_down = swapped((w_gate, w_up, w_down), "rep", 0)
        first = lax.axis_index("rep") == 0
        gate_full = jnp.where(
            first,
            jnp.concatenate([w_gate[0], other_gate[0]], axis=1),
            jnp.concatenate([other_gate[0], w_gate[0]], axis=1),
        )
        up_full = jnp.where(
            first,
            jnp.concatenate([w_up[0], other_up[0]], axis=1),
            jnp.concatenate([other_up[0], w_up[0]], axis=1),
        )
        down_full = jnp.where(
            first,
            jnp.concatenate([w_down[0], other_down[0]], axis=0),
            jnp.concatenate([other_down[0], w_down[0]], axis=0),
        )
        return (gate_full, up_full, down_full)

    shard_blocks, slice_rows, kv_width = keys.shape
    pick_count = selected.shape[1]
    block_rows = slice_rows * n_eg
    my_eg = lax.axis_index("eg")
    both = jnp.concatenate([keys, values], axis=2)
    top_count = expert_ids.shape[1]
    use_gather = n_ctx * n_eg <= 4 * top_count
    if use_gather:
        flat_ids = expert_ids.reshape(-1).astype(jnp.bfloat16)
        id_count = flat_ids.shape[0]
        cells = shard_blocks * slice_rows
        id_cols = -(-(-(-id_count // cells)) // 128) * 128
        id_slab = jnp.pad(flat_ids, (0, id_cols * cells - id_count)).reshape(
            shard_blocks, slice_rows, id_cols
        )
        both = jnp.concatenate([both, id_slab], axis=2)
    gathered = lax.all_gather(both[None], ("ctx", "eg"), axis=0, tiled=True)
    if use_gather:
        all_ids = (
            gathered[:, :, :, 2 * kv_width :]
            .reshape(n_ctx * n_eg, -1)[:, :id_count]
            .reshape(-1, top_count)
            .astype(jnp.int32)
        )
    held_width = gathered.shape[3]
    by_slice = gathered.reshape(n_ctx * n_eg * shard_blocks, slice_rows, held_width)
    query_rows = queries.shape[0]
    my_block = (my_ctx * n_eg + my_eg) * query_rows // block_rows
    chosen_blocks = jnp.concatenate(
        [my_block[None].astype(jnp.int32), jnp.take(selected, my_block, axis=0)]
    )
    slice_index = (
        (chosen_blocks // shard_blocks)[:, None] * n_eg + jnp.arange(n_eg, dtype=jnp.int32)[None, :]
    ) * shard_blocks + (chosen_blocks % shard_blocks)[:, None]
    context = jnp.take(by_slice, slice_index.reshape(-1), axis=0).reshape(-1, held_width)
    span = (1 + pick_count) * block_rows
    kv_heads = kv_width // HD
    tok_dev = residual.shape[0]
    pieces = {0: out_weight}
    for bit in reversed(range(n_eg.bit_length() - 1)):
        stride = 2**bit
        held = sorted(pieces)
        if len(held) > 1:
            barrier_out = lax.optimization_barrier((tuple(pieces[m] for m in held), context))
            pieces = dict(zip(held, barrier_out[0]))
            context = barrier_out[1]
        fetched = swapped(tuple(pieces[m] for m in held), "eg", bit)
        for m, piece in zip(held, fetched):
            pieces[m + stride] = piece
    attended = attend_rows(queries, context, kv_heads)
    weight_cols = jnp.concatenate([pieces[m] for m in range(n_eg)], axis=1)
    out_by_piece = jnp.dot(attended, weight_cols, preferred_element_type=jnp.float32).reshape(
        query_rows, n_eg, -1
    )
    piece_of_col = jnp.arange(n_eg, dtype=jnp.int32) ^ my_eg
    partial_out = jnp.take(out_by_piece, piece_of_col, axis=1).reshape(query_rows, -1)
    attn_out = lax.psum_scatter(
        partial_out.astype(jnp.bfloat16), "rep", scatter_dimension=0, tiled=True
    )
    stream = residual.astype(jnp.float32) + attn_out.astype(jnp.float32)
    meansq = jnp.mean(stream * stream, axis=1, keepdims=True)
    normed = (stream * lax.rsqrt(meansq + 1e-06) * norm_gain).astype(jnp.bfloat16)
    top_count = expert_ids.shape[1]
    slot_count = n_ctx * n_eg
    pair_count = tok_dev * top_count
    per_slot = pair_count // slot_count
    home_slot = jnp.take(expert_home, expert_ids.reshape(-1), axis=0)
    indicator = (home_slot[:, None] == jnp.arange(slot_count, dtype=jnp.int32)[None, :]).astype(
        jnp.int32
    )
    rank_in_slot = jnp.sum((jnp.cumsum(indicator, axis=0) - 1) * indicator, axis=1)
    position = home_slot * per_slot + rank_in_slot
    source_pair = (
        jnp.zeros((pair_count,), jnp.int32)
        .at[position]
        .set(jnp.arange(pair_count, dtype=jnp.int32))
    )
    partner = fetch_panels()
    if use_gather:
        my_slot = my_ctx * n_eg + my_eg
        all_packed = lax.all_gather(normed, ("ctx", "eg"), axis=0, tiled=True)
        expert_count = expert_home.shape[0]
        my_expert = jnp.sum(
            jnp.where(expert_home == my_slot, jnp.arange(expert_count, dtype=jnp.int32), 0)
        )
        hits = jnp.any(all_ids == my_expert, axis=1)
        hits = hits.reshape(slot_count, tok_dev).astype(jnp.int32)
        rank = jnp.cumsum(hits, axis=1) - 1
        chosen = jnp.logical_and(
            hits[:, None, :] == 1,
            rank[:, None, :] == jnp.arange(per_slot, dtype=jnp.int32)[None, :, None],
        )
        local_row = jnp.sum(
            chosen.astype(jnp.int32) * jnp.arange(tok_dev, dtype=jnp.int32)[None, None, :], axis=2
        )
        src_rows = local_row + jnp.arange(slot_count, dtype=jnp.int32)[:, None] * tok_dev
        hidden = partner[0].shape[1]
        gate_up = jnp.concatenate([partner[0], partner[1]], axis=1)
        both_act = jnp.dot(all_packed, gate_up, preferred_element_type=jnp.float32)
        gate_act = both_act[:, :hidden]
        up_act = both_act[:, hidden:]
        activation = (jax.nn.silu(gate_act) * up_act).astype(jnp.bfloat16)
        pick_matrix = (
            src_rows.reshape(-1)[:, None]
            == jnp.arange(activation.shape[0], dtype=jnp.int32)[None, :]
        ).astype(jnp.bfloat16)
        picked = jnp.dot(pick_matrix, activation, preferred_element_type=jnp.float32).astype(
            jnp.bfloat16
        )
        produced = jnp.dot(picked, partner[2], preferred_element_type=jnp.float32).astype(
            jnp.bfloat16
        )
    else:
        outbound = jnp.take(normed, source_pair // top_count, axis=0).reshape(
            slot_count, per_slot, -1
        )
        arrived = lax.all_to_all(outbound, ("ctx", "eg"), split_axis=0, concat_axis=0, tiled=True)
        flat_rows = arrived.reshape(-1, arrived.shape[2])
        produced = expert_apply(flat_rows, partner[0], partner[1], partner[2])
    returned = lax.all_to_all(
        produced.reshape(slot_count, per_slot, -1),
        ("ctx", "eg"),
        split_axis=0,
        concat_axis=0,
        tiled=True,
    )
    returned_rows = returned.reshape(pair_count, -1)
    placed = position.reshape(tok_dev, top_count)[:, :, None] == jnp.arange(
        pair_count, dtype=jnp.int32
    )[None, None, :]
    mixing = jnp.sum(jnp.where(placed, gate_weights[:, :, None], 0.0), axis=1)
    high_part = mixing.astype(jnp.bfloat16)
    low_part = (mixing - high_part.astype(jnp.float32)).astype(jnp.bfloat16)
    both_parts = jnp.concatenate([high_part, low_part], axis=0)
    stacked_out = jnp.dot(both_parts, returned_rows, preferred_element_type=jnp.float32)
    combined = stacked_out[:tok_dev] + stacked_out[tok_dev:]
    moe_out = combined.astype(jnp.bfloat16)
    return (attn_out, moe_out)


def solution(mesh):
    return jax.shard_map(
        local,
        mesh=mesh,
        in_specs=(
            P(("groups", "ctx", "eg"), "rep"),
            P(("groups", "ctx"), "eg", "rep"),
            P(("groups", "ctx"), "eg", "rep"),
            P("groups", None),
            P("rep", "eg"),
            P(("groups", "ctx", "eg", "rep"), None),
            P(),
            P(("groups", "ctx", "eg", "rep"), None),
            P(("groups", "ctx", "eg", "rep"), None),
            P(),
            P(("ctx", "eg"), None, "rep"),
            P(("ctx", "eg"), None, "rep"),
            P(("ctx", "eg"), "rep", None),
        ),
        out_specs=(
            P(("groups", "ctx", "eg", "rep"), None),
            P(("groups", "ctx", "eg", "rep"), None),
        ),
        check_vma=False,
    )
```

```python
import math

import jax
import jax.numpy as jnp
from jax import lax
from jax.experimental import pallas as pl
from jax.sharding import PartitionSpec as P

HD = 128


def swapped(value, axis, bit):
    mask = 2**bit
    pairs = [(source, source ^ mask) for source in range(lax.axis_size(axis))]
    return lax.ppermute(value, axis, pairs)


def attention_kernel(query_ref, key_ref, value_ref, out_ref):
    inverse_root = 1.0 / math.sqrt(HD)
    key_block = key_ref[...]
    value_block = value_ref[...]
    for head in range(query_ref.shape[1] // HD):
        query_head = query_ref[:, head * HD : (head + 1) * HD]
        logits = (
            lax.dot_general(
                query_head,
                key_block,
                (((1,), (1,)), ((), ())),
                preferred_element_type=jnp.float32,
            )
            * inverse_root
        )
        largest = jnp.max(logits, axis=-1, keepdims=True)
        raised = jnp.exp(logits - largest)
        denominator = jnp.sum(raised, axis=-1, keepdims=True)
        weights_low = (raised / denominator).astype(jnp.bfloat16)
        blended = jnp.dot(weights_low, value_block, preferred_element_type=jnp.float32)
        out_ref[:, head * HD : (head + 1) * HD] = blended.astype(out_ref.dtype)


def attend_rows(queries_flat, context, kv_heads, interpret=False):
    row_count = queries_flat.shape[0]
    span = context.shape[0]
    group_width = queries_flat.shape[1] // kv_heads
    return pl.pallas_call(
        attention_kernel,
        grid=(kv_heads,),
        in_specs=[
            pl.BlockSpec((row_count, group_width), lambda k: (0, k)),
            pl.BlockSpec((span, HD), lambda k: (0, k)),
            pl.BlockSpec((span, HD), lambda k: (0, kv_heads + k)),
        ],
        out_specs=pl.BlockSpec((row_count, group_width), lambda k: (0, k)),
        out_shape=jax.ShapeDtypeStruct(queries_flat.shape, jnp.bfloat16),
        interpret=interpret,
    )(queries_flat, context, context)


def expert_apply(rows_in, gate_full, up_full, down_full):
    gate_act = jnp.dot(rows_in, gate_full, preferred_element_type=jnp.float32)
    up_act = jnp.dot(rows_in, up_full, preferred_element_type=jnp.float32)
    activation = (jax.nn.silu(gate_act) * up_act).astype(jnp.bfloat16)
    return jnp.dot(activation, down_full, preferred_element_type=jnp.float32).astype(jnp.bfloat16)


def local(
    queries,
    keys,
    values,
    selected,
    out_weight,
    residual,
    norm_gain,
    expert_ids,
    gate_weights,
    expert_home,
    w_gate,
    w_up,
    w_down,
):
    n_ctx = lax.axis_size("ctx")
    n_eg = lax.axis_size("eg")
    n_rep = lax.axis_size("rep")
    my_ctx = lax.axis_index("ctx")

    def fetch_panels():
        if n_rep == 1:
            return (w_gate[0], w_up[0], w_down[0])
        other_gate, other_up, other_down = swapped((w_gate, w_up, w_down), "rep", 0)
        first = lax.axis_index("rep") == 0
        gate_full = jnp.where(
            first,
            jnp.concatenate([w_gate[0], other_gate[0]], axis=1),
            jnp.concatenate([other_gate[0], w_gate[0]], axis=1),
        )
        up_full = jnp.where(
            first,
            jnp.concatenate([w_up[0], other_up[0]], axis=1),
            jnp.concatenate([other_up[0], w_up[0]], axis=1),
        )
        down_full = jnp.where(
            first,
            jnp.concatenate([w_down[0], other_down[0]], axis=0),
            jnp.concatenate([other_down[0], w_down[0]], axis=0),
        )
        return (gate_full, up_full, down_full)

    shard_blocks, slice_rows, kv_width = keys.shape
    pick_count = selected.shape[1]
    block_rows = slice_rows * n_eg
    my_eg = lax.axis_index("eg")
    both = jnp.concatenate([keys, values], axis=2)
    top_count = expert_ids.shape[1]
    use_gather = n_ctx * n_eg <= 4 * top_count
    if use_gather:
        flat_ids = expert_ids.reshape(-1).astype(jnp.bfloat16)
        id_count = flat_ids.shape[0]
        lane = shard_blocks * 2 * kv_width
        id_rows = -(-(-(-id_count // lane)) // 8) * 8
        id_slab = jnp.pad(flat_ids, (0, id_rows * lane - id_count)).reshape(
            shard_blocks, id_rows, 2 * kv_width
        )
        both = jnp.concatenate([both, id_slab], axis=1)
    gathered = lax.all_gather(both[None], ("ctx", "eg"), axis=0, tiled=True)
    if use_gather:
        all_ids = (
            gathered[:, :, slice_rows:, :]
            .reshape(n_ctx * n_eg, -1)[:, :id_count]
            .reshape(-1, top_count)
            .astype(jnp.int32)
        )
    held_rows = gathered.shape[2]
    by_slice = gathered.reshape(n_ctx * n_eg * shard_blocks, held_rows, 2 * kv_width)
    query_rows = queries.shape[0]
    my_block = (my_ctx * n_eg + my_eg) * query_rows // block_rows
    chosen_blocks = jnp.concatenate(
        [my_block[None].astype(jnp.int32), jnp.take(selected, my_block, axis=0)]
    )
    slice_index = (
        (chosen_blocks // shard_blocks)[:, None] * n_eg + jnp.arange(n_eg, dtype=jnp.int32)[None, :]
    ) * shard_blocks + (chosen_blocks % shard_blocks)[:, None]
    context = jnp.take(by_slice, slice_index.reshape(-1), axis=0)[:, :slice_rows].reshape(
        -1, 2 * kv_width
    )
    span = (1 + pick_count) * block_rows
    kv_heads = kv_width // HD
    tok_dev = residual.shape[0]
    pieces = {0: out_weight}
    for bit in reversed(range(n_eg.bit_length() - 1)):
        stride = 2**bit
        held = sorted(pieces)
        if len(held) > 1:
            barrier_out = lax.optimization_barrier((tuple(pieces[m] for m in held), context))
            pieces = dict(zip(held, barrier_out[0]))
            context = barrier_out[1]
        fetched = swapped(tuple(pieces[m] for m in held), "eg", bit)
        for m, piece in zip(held, fetched):
            pieces[m + stride] = piece
    attended = attend_rows(queries, context, kv_heads)
    weight_cols = jnp.concatenate([pieces[m] for m in range(n_eg)], axis=1)
    out_by_piece = jnp.dot(attended, weight_cols, preferred_element_type=jnp.float32).reshape(
        query_rows, n_eg, -1
    )
    piece_of_col = jnp.arange(n_eg, dtype=jnp.int32) ^ my_eg
    partial_out = jnp.take(out_by_piece, piece_of_col, axis=1).reshape(query_rows, -1)
    attn_out = lax.psum_scatter(
        partial_out.astype(jnp.bfloat16), "rep", scatter_dimension=0, tiled=True
    )
    stream = residual.astype(jnp.float32) + attn_out.astype(jnp.float32)
    meansq = jnp.mean(stream * stream, axis=1, keepdims=True)
    normed = (stream * lax.rsqrt(meansq + 1e-06) * norm_gain).astype(jnp.bfloat16)
    top_count = expert_ids.shape[1]
    slot_count = n_ctx * n_eg
    pair_count = tok_dev * top_count
    per_slot = pair_count // slot_count
    home_slot = jnp.take(expert_home, expert_ids.reshape(-1), axis=0)
    indicator = (home_slot[:, None] == jnp.arange(slot_count, dtype=jnp.int32)[None, :]).astype(
        jnp.int32
    )
    rank_in_slot = jnp.sum((jnp.cumsum(indicator, axis=0) - 1) * indicator, axis=1)
    position = home_slot * per_slot + rank_in_slot
    source_pair = (
        jnp.zeros((pair_count,), jnp.int32)
        .at[position]
        .set(jnp.arange(pair_count, dtype=jnp.int32))
    )
    partner = fetch_panels()
    if use_gather:
        my_slot = my_ctx * n_eg + my_eg
        all_packed = lax.all_gather(normed, ("ctx", "eg"), axis=0, tiled=True)
        expert_count = expert_home.shape[0]
        my_expert = jnp.sum(
            jnp.where(expert_home == my_slot, jnp.arange(expert_count, dtype=jnp.int32), 0)
        )
        hits = jnp.any(all_ids == my_expert, axis=1)
        hits = hits.reshape(slot_count, tok_dev).astype(jnp.int32)
        rank = jnp.cumsum(hits, axis=1) - 1
        chosen = jnp.logical_and(
            hits[:, None, :] == 1,
            rank[:, None, :] == jnp.arange(per_slot, dtype=jnp.int32)[None, :, None],
        )
        local_row = jnp.sum(
            chosen.astype(jnp.int32) * jnp.arange(tok_dev, dtype=jnp.int32)[None, None, :], axis=2
        )
        src_rows = local_row + jnp.arange(slot_count, dtype=jnp.int32)[:, None] * tok_dev
        hidden = partner[0].shape[1]
        gate_up = jnp.concatenate([partner[0], partner[1]], axis=1)
        both_act = jnp.dot(all_packed, gate_up, preferred_element_type=jnp.float32)
        gate_act = both_act[:, :hidden]
        up_act = both_act[:, hidden:]
        activation = (jax.nn.silu(gate_act) * up_act).astype(jnp.bfloat16)
        pick_matrix = (
            src_rows.reshape(-1)[:, None]
            == jnp.arange(activation.shape[0], dtype=jnp.int32)[None, :]
        ).astype(jnp.bfloat16)
        picked = jnp.dot(pick_matrix, activation, preferred_element_type=jnp.float32).astype(
            jnp.bfloat16
        )
        produced = jnp.dot(picked, partner[2], preferred_element_type=jnp.float32).astype(
            jnp.bfloat16
        )
    else:
        outbound = jnp.take(normed, source_pair // top_count, axis=0).reshape(
            slot_count, per_slot, -1
        )
        arrived = lax.all_to_all(outbound, ("ctx", "eg"), split_axis=0, concat_axis=0, tiled=True)
        flat_rows = arrived.reshape(-1, arrived.shape[2])
        produced = expert_apply(flat_rows, partner[0], partner[1], partner[2])
    returned = lax.all_to_all(
        produced.reshape(slot_count, per_slot, -1),
        ("ctx", "eg"),
        split_axis=0,
        concat_axis=0,
        tiled=True,
    )
    returned_rows = returned.reshape(pair_count, -1)
    placed = position.reshape(tok_dev, top_count)[:, :, None] == jnp.arange(
        pair_count, dtype=jnp.int32
    )[None, None, :]
    mixing = jnp.sum(jnp.where(placed, gate_weights[:, :, None], 0.0), axis=1)
    high_part = mixing.astype(jnp.bfloat16)
    low_part = (mixing - high_part.astype(jnp.float32)).astype(jnp.bfloat16)
    both_parts = jnp.concatenate([high_part, low_part], axis=0)
    stacked_out = jnp.dot(both_parts, returned_rows, preferred_element_type=jnp.float32)
    combined = stacked_out[:tok_dev] + stacked_out[tok_dev:]
    moe_out = combined.astype(jnp.bfloat16)
    return (attn_out, moe_out)


def solution(mesh):
    return jax.shard_map(
        local,
        mesh=mesh,
        in_specs=(
            P(("groups", "ctx", "eg"), "rep"),
            P(("groups", "ctx"), "eg", "rep"),
            P(("groups", "ctx"), "eg", "rep"),
            P("groups", None),
            P("rep", "eg"),
            P(("groups", "ctx", "eg", "rep"), None),
            P(),
            P(("groups", "ctx", "eg", "rep"), None),
            P(("groups", "ctx", "eg", "rep"), None),
            P(),
            P(("ctx", "eg"), None, "rep"),
            P(("ctx", "eg"), None, "rep"),
            P(("ctx", "eg"), "rep", None),
        ),
        out_specs=(
            P(("groups", "ctx", "eg", "rep"), None),
            P(("groups", "ctx", "eg", "rep"), None),
        ),
        check_vma=False,
    )
```

```python
import math

import jax
import jax.numpy as jnp
from jax import lax
from jax.experimental import pallas as pl
from jax.sharding import PartitionSpec as P

HD = 128


def swapped(value, axis, bit):
    mask = 2**bit
    pairs = [(source, source ^ mask) for source in range(lax.axis_size(axis))]
    return lax.ppermute(value, axis, pairs)


def attention_kernel(query_ref, key_ref, value_ref, out_ref):
    inverse_root = 1.0 / math.sqrt(HD)
    key_block = key_ref[...]
    value_block = value_ref[...]
    for head in range(query_ref.shape[1] // HD):
        query_head = query_ref[:, head * HD : (head + 1) * HD]
        logits = (
            lax.dot_general(
                query_head,
                key_block,
                (((1,), (1,)), ((), ())),
                preferred_element_type=jnp.float32,
            )
            * inverse_root
        )
        largest = jnp.max(logits, axis=-1, keepdims=True)
        raised = jnp.exp(logits - largest)
        denominator = jnp.sum(raised, axis=-1, keepdims=True)
        weights_low = (raised / denominator).astype(jnp.bfloat16)
        blended = jnp.dot(weights_low, value_block, preferred_element_type=jnp.float32)
        out_ref[:, head * HD : (head + 1) * HD] = blended.astype(out_ref.dtype)


def attend_rows(queries_flat, context, kv_heads, interpret=False):
    row_count = queries_flat.shape[0]
    span = context.shape[0]
    group_width = queries_flat.shape[1] // kv_heads
    return pl.pallas_call(
        attention_kernel,
        grid=(kv_heads,),
        in_specs=[
            pl.BlockSpec((row_count, group_width), lambda k: (0, k)),
            pl.BlockSpec((span, HD), lambda k: (0, k)),
            pl.BlockSpec((span, HD), lambda k: (0, kv_heads + k)),
        ],
        out_specs=pl.BlockSpec((row_count, group_width), lambda k: (0, k)),
        out_shape=jax.ShapeDtypeStruct(queries_flat.shape, jnp.bfloat16),
        interpret=interpret,
    )(queries_flat, context, context)


def expert_apply(rows_in, gate_full, up_full, down_full):
    gate_act = jnp.dot(rows_in, gate_full, preferred_element_type=jnp.float32)
    up_act = jnp.dot(rows_in, up_full, preferred_element_type=jnp.float32)
    activation = (jax.nn.silu(gate_act) * up_act).astype(jnp.bfloat16)
    return jnp.dot(activation, down_full, preferred_element_type=jnp.float32).astype(jnp.bfloat16)


def local(
    queries,
    keys,
    values,
    selected,
    out_weight,
    residual,
    norm_gain,
    expert_ids,
    gate_weights,
    expert_home,
    w_gate,
    w_up,
    w_down,
):
    n_ctx = lax.axis_size("ctx")
    n_eg = lax.axis_size("eg")
    n_rep = lax.axis_size("rep")
    my_ctx = lax.axis_index("ctx")

    def fetch_panels():
        if n_rep == 1:
            return (w_gate[0], w_up[0], w_down[0])
        other_gate, other_up, other_down = swapped((w_gate, w_up, w_down), "rep", 0)
        first = lax.axis_index("rep") == 0
        gate_full = jnp.where(
            first,
            jnp.concatenate([w_gate[0], other_gate[0]], axis=1),
            jnp.concatenate([other_gate[0], w_gate[0]], axis=1),
        )
        up_full = jnp.where(
            first,
            jnp.concatenate([w_up[0], other_up[0]], axis=1),
            jnp.concatenate([other_up[0], w_up[0]], axis=1),
        )
        down_full = jnp.where(
            first,
            jnp.concatenate([w_down[0], other_down[0]], axis=0),
            jnp.concatenate([other_down[0], w_down[0]], axis=0),
        )
        return (gate_full, up_full, down_full)

    shard_blocks, slice_rows, kv_width = keys.shape
    pick_count = selected.shape[1]
    block_rows = slice_rows * n_eg
    my_eg = lax.axis_index("eg")
    both = jnp.concatenate([keys, values], axis=2)
    top_count = expert_ids.shape[1]
    use_gather = n_ctx * n_eg <= 4 * top_count
    if use_gather:
        flat_ids = expert_ids.reshape(-1).astype(jnp.bfloat16)
        id_count = flat_ids.shape[0]
        lane = shard_blocks * 2 * kv_width
        id_rows = -(-(-(-id_count // lane)) // 8) * 8
        id_slab = jnp.pad(flat_ids, (0, id_rows * lane - id_count)).reshape(
            shard_blocks, id_rows, 2 * kv_width
        )
        both = jnp.concatenate([both, id_slab], axis=1)
    gathered = lax.all_gather(both[None], ("ctx", "eg"), axis=0, tiled=True)
    if use_gather:
        all_ids = (
            gathered[:, :, slice_rows:, :]
            .reshape(n_ctx * n_eg, -1)[:, :id_count]
            .reshape(-1, top_count)
            .astype(jnp.int32)
        )
    held_rows = gathered.shape[2]
    by_slice = gathered.reshape(n_ctx * n_eg * shard_blocks, held_rows, 2 * kv_width)
    query_rows = queries.shape[0]
    my_block = (my_ctx * n_eg + my_eg) * query_rows // block_rows
    chosen_blocks = jnp.concatenate(
        [my_block[None].astype(jnp.int32), jnp.take(selected, my_block, axis=0)]
    )
    slice_index = (
        (chosen_blocks // shard_blocks)[:, None] * n_eg + jnp.arange(n_eg, dtype=jnp.int32)[None, :]
    ) * shard_blocks + (chosen_blocks % shard_blocks)[:, None]
    context = jnp.take(by_slice, slice_index.reshape(-1), axis=0)[:, :slice_rows].reshape(
        -1, 2 * kv_width
    )
    span = (1 + pick_count) * block_rows
    kv_heads = kv_width // HD
    tok_dev = residual.shape[0]
    pieces = {0: out_weight}
    for bit in reversed(range(n_eg.bit_length() - 1)):
        stride = 2**bit
        held = sorted(pieces)
        if len(held) > 1:
            barrier_out = lax.optimization_barrier((tuple(pieces[m] for m in held), context))
            pieces = dict(zip(held, barrier_out[0]))
            context = barrier_out[1]
        fetched = swapped(tuple(pieces[m] for m in held), "eg", bit)
        for m, piece in zip(held, fetched):
            pieces[m + stride] = piece
    attended = attend_rows(queries, context, kv_heads)
    weight_cols = jnp.concatenate([pieces[m] for m in range(n_eg)], axis=1)
    out_by_piece = (
        jnp.dot(attended, weight_cols, preferred_element_type=jnp.float32)
        .astype(jnp.bfloat16)
        .reshape(query_rows, n_eg, -1)
    )
    piece_of_col = jnp.arange(n_eg, dtype=jnp.int32) ^ my_eg
    partial_out = jnp.take(out_by_piece, piece_of_col, axis=1).reshape(query_rows, -1)
    attn_out = lax.psum_scatter(partial_out, "rep", scatter_dimension=0, tiled=True)
    stream = residual.astype(jnp.float32) + attn_out.astype(jnp.float32)
    meansq = jnp.mean(stream * stream, axis=1, keepdims=True)
    normed = (stream * lax.rsqrt(meansq + 1e-06) * norm_gain).astype(jnp.bfloat16)
    top_count = expert_ids.shape[1]
    slot_count = n_ctx * n_eg
    pair_count = tok_dev * top_count
    per_slot = pair_count // slot_count
    home_slot = jnp.take(expert_home, expert_ids.reshape(-1), axis=0)
    indicator = (home_slot[:, None] == jnp.arange(slot_count, dtype=jnp.int32)[None, :]).astype(
        jnp.int32
    )
    rank_in_slot = jnp.sum((jnp.cumsum(indicator, axis=0) - 1) * indicator, axis=1)
    position = home_slot * per_slot + rank_in_slot
    source_pair = (
        jnp.zeros((pair_count,), jnp.int32)
        .at[position]
        .set(jnp.arange(pair_count, dtype=jnp.int32))
    )
    partner = fetch_panels()
    if use_gather:
        my_slot = my_ctx * n_eg + my_eg
        all_packed = lax.all_gather(normed, ("ctx", "eg"), axis=0, tiled=True)
        expert_count = expert_home.shape[0]
        my_expert = jnp.sum(
            jnp.where(expert_home == my_slot, jnp.arange(expert_count, dtype=jnp.int32), 0)
        )
        hits = jnp.any(all_ids == my_expert, axis=1)
        hits = hits.reshape(slot_count, tok_dev).astype(jnp.int32)
        rank = jnp.cumsum(hits, axis=1) - 1
        chosen = jnp.logical_and(
            hits[:, None, :] == 1,
            rank[:, None, :] == jnp.arange(per_slot, dtype=jnp.int32)[None, :, None],
        )
        local_row = jnp.sum(
            chosen.astype(jnp.int32) * jnp.arange(tok_dev, dtype=jnp.int32)[None, None, :], axis=2
        )
        src_rows = local_row + jnp.arange(slot_count, dtype=jnp.int32)[:, None] * tok_dev
        hidden = partner[0].shape[1]
        gate_up = jnp.concatenate([partner[0], partner[1]], axis=1)
        both_act = jnp.dot(all_packed, gate_up, preferred_element_type=jnp.float32)
        gate_act = both_act[:, :hidden]
        up_act = both_act[:, hidden:]
        activation = (jax.nn.silu(gate_act) * up_act).astype(jnp.bfloat16)
        pick_matrix = (
            src_rows.reshape(-1)[:, None]
            == jnp.arange(activation.shape[0], dtype=jnp.int32)[None, :]
        ).astype(jnp.bfloat16)
        picked = jnp.dot(pick_matrix, activation, preferred_element_type=jnp.float32).astype(
            jnp.bfloat16
        )
        produced = jnp.dot(picked, partner[2], preferred_element_type=jnp.float32).astype(
            jnp.bfloat16
        )
    else:
        outbound = jnp.take(normed, source_pair // top_count, axis=0).reshape(
            slot_count, per_slot, -1
        )
        arrived = lax.all_to_all(outbound, ("ctx", "eg"), split_axis=0, concat_axis=0, tiled=True)
        flat_rows = arrived.reshape(-1, arrived.shape[2])
        produced = expert_apply(flat_rows, partner[0], partner[1], partner[2])
    returned = lax.all_to_all(
        produced.reshape(slot_count, per_slot, -1),
        ("ctx", "eg"),
        split_axis=0,
        concat_axis=0,
        tiled=True,
    )
    returned_rows = returned.reshape(pair_count, -1)
    placed = position.reshape(tok_dev, top_count)[:, :, None] == jnp.arange(
        pair_count, dtype=jnp.int32
    )[None, None, :]
    mixing = jnp.sum(jnp.where(placed, gate_weights[:, :, None], 0.0), axis=1)
    high_part = mixing.astype(jnp.bfloat16)
    low_part = (mixing - high_part.astype(jnp.float32)).astype(jnp.bfloat16)
    both_parts = jnp.concatenate([high_part, low_part], axis=0)
    stacked_out = jnp.dot(both_parts, returned_rows, preferred_element_type=jnp.float32)
    combined = stacked_out[:tok_dev] + stacked_out[tok_dev:]
    moe_out = combined.astype(jnp.bfloat16)
    return (attn_out, moe_out)


def solution(mesh):
    return jax.shard_map(
        local,
        mesh=mesh,
        in_specs=(
            P(("groups", "ctx", "eg"), "rep"),
            P(("groups", "ctx"), "eg", "rep"),
            P(("groups", "ctx"), "eg", "rep"),
            P("groups", None),
            P("rep", "eg"),
            P(("groups", "ctx", "eg", "rep"), None),
            P(),
            P(("groups", "ctx", "eg", "rep"), None),
            P(("groups", "ctx", "eg", "rep"), None),
            P(),
            P(("ctx", "eg"), None, "rep"),
            P(("ctx", "eg"), None, "rep"),
            P(("ctx", "eg"), "rep", None),
        ),
        out_specs=(
            P(("groups", "ctx", "eg", "rep"), None),
            P(("groups", "ctx", "eg", "rep"), None),
        ),
        check_vma=False,
    )
```
